32 devices in a mesh: groups: 2 (over y), leaf: 4 (over z), state: 2 (over x), sub: 2 (over core).
Axes of the slice: x: 2, y: 2, z: 4, core: 2. Of those that a mesh axis runs over, the one named last changes fastest.
Arguments:
- sphere_coef: bfloat16 [12, 25, 2, 2, 4, 2048], P(None, None, None, None, None, ('groups', 'leaf', 'state', 'sub')), parts along dimension 5, may hold values from -6 to 6
- live_blocks: int32 [32], P(('groups', 'leaf', 'state', 'sub')), parts along dimension 0, may hold values from 1 to 4, as said below
- cluster: int32 [2048], P(('groups', 'leaf', 'state', 'sub')), parts along dimension 0, may hold values from 0 to 15
- leaf_parent: int32 [512], P(('groups', 'leaf', 'state', 'sub')), parts along dimension 0, may hold values from 0 to 1
- leaf_octant: int32 [512], P(('groups', 'leaf', 'state', 'sub')), parts along dimension 0, may hold values from 0 to 7
- box_octant: int32 [64], P(('groups', 'leaf', 'state', 'sub')), parts along dimension 0, may hold values from 0 to 7
- rotation: float32 [8, 2, 12, 25, 25], replicated, may hold values from -0.875 to 0.875
- axial_one: float32 [2, 25, 2, 12, 2, 12], replicated, may hold values from -0.3125 to 0.3125
- axial_two: float32 [2, 25, 2, 12, 2, 12], replicated, may hold values from -0.3125 to 0.3125
- owner_rotation: float32 [8, 2, 12, 25, 25], P(('groups', 'leaf')), parts along dimension 0, may hold values from -0.875 to 0.875
- owner_axial: float32 [8, 2, 25, 2, 128, 2, 12], P(('groups', 'leaf'), None, None, None, ('state', 'sub')), parts along dimension 0, may hold values from -0.875 to 0.875
- owner_angle: float32 [8], P('groups'), parts along dimension 0, may hold values from -3.140625 to 3.140625
- turn_table: bfloat16 [8, 128, 25, 256], P(('groups', 'leaf'), ('state', 'sub')), parts along dimension 0, may hold values from -0.625 to 0.625
- angular_table: bfloat16 [256, 128, 32], P('leaf', ('state', 'sub')), may hold values from -0.375 to 0.375
Outputs:
- far_field: float32 [32, 4, 2, 2, 2048], P(('groups', 'leaf', 'state', 'sub')), parts along dimension 0
The draws below stay inside these ranges and needn't reach their ends.
There are 2 independent parts, one for each index of `groups`. The reference program is written for one: setup_inputs(seed, part) draws one part's arguments, and reference() takes and returns one part's arrays. A program takes and returns all parts, laid end to end along the dimension named above; an argument that names none is the same for every part. Nothing has to cross between parts.
Inputs may be any that keep to these rules, and one draw needn't show every extreme that they name: `live_blocks`: live blocks of 16 sphere slots on each device; some device has all 4 live in every draw.
All inputs are finite; a program needn't handle non-finite values.
Results may differ from the reference program's by a relative error of at most 0.018.
Values may be sent and summed in bfloat16 or wider, within the bound.
No kernel may reach another device: no remote copies, remote signals or barrier semaphores. Data moves between devices by JAX's collectives and lax.ppermute only.
A program may use at most 64 MiB of HBM per device.

```python
import math
import jax
import jax.numpy as jnp
from jax import lax

L = 12
MW = 25
STATES = 4
SPH_DEV = 64
SBLK = 4
LEAF_DEV = 16
BOX_DEV = 2
PHI = 2048
HOLDERS = 16
SPHERES = 1024
LEAVES = 256
BOXES = 32
NR = 128
MP = 256
THETA = 16
N_LEAF = 4


def draw_live_blocks(key, part):
    first_key, second_key = jax.random.split(key)
    counts = jax.random.randint(first_key, (HOLDERS,), 1, SBLK + 1)
    position = jax.random.randint(second_key, (), 0, HOLDERS)
    return jnp.where(jnp.arange(HOLDERS) == position, SBLK, counts).astype(jnp.int32)


def touch_ends(result, own_key, low, high):
    shape = result.shape
    place = [jax.random.randint(jax.random.fold_in(own_key, axis), (), 0, shape[axis]) for axis in range(len(shape))]
    result = result.at[tuple(place)].set(low)
    longest = shape.index(max(shape))
    place[longest] = (place[longest] + 1) % shape[longest]
    return result.at[tuple(place)].set(high)


def steps_of(own_key, dims, cuts, low, top_value):
    def one(axis_at, parts):
        heights = jax.random.uniform(jax.random.fold_in(jax.random.fold_in(own_key, 6), axis_at), (parts,), jnp.float32, low / len(cuts), top_value / len(cuts))
        return jnp.repeat(jnp.exp(heights), dims[axis_at] // parts).reshape((-1,) + (1,) * (len(dims) - axis_at - 1))

    gain = one(*cuts[0])
    for cut in cuts[1:]:
        gain = gain * one(*cut)
    return gain


def noise(key, dims, deviation, reach, pieces=(), kind=jnp.bfloat16):
    values = deviation * jax.random.normal(key, dims, jnp.float32)
    if pieces:
        values = values * steps_of(key, dims, pieces, -0.22, 0.18)
    return jnp.clip(values, -reach, reach).astype(kind)


def setup_inputs(seed: int = 0, part: int = 0) -> dict:
    seeds = jax.random.split(jax.random.key(seed), 15)
    part_keys = jax.random.split(jax.random.fold_in(seeds[14], part), 15)
    return {
        "sphere_coef": noise(part_keys[0], (L, MW, 2, 2, STATES, SPHERES), 1.0, 6.0, ((5, 16),)),
        "live_blocks": draw_live_blocks(jax.random.fold_in(jax.random.fold_in(seeds[14], part), 71), part),
        "cluster": touch_ends(jax.random.randint(part_keys[2], (SPHERES,), 0, LEAF_DEV), jax.random.fold_in(part_keys[2], 1), 0, LEAF_DEV - 1).astype(jnp.int32),
        "leaf_parent": touch_ends(jax.random.randint(part_keys[3], (LEAVES,), 0, BOX_DEV), jax.random.fold_in(part_keys[3], 1), 0, BOX_DEV - 1).astype(jnp.int32),
        "leaf_octant": touch_ends(jax.random.randint(part_keys[4], (LEAVES,), 0, 8), jax.random.fold_in(part_keys[4], 1), 0, 7).astype(jnp.int32),
        "box_octant": touch_ends(jax.random.randint(part_keys[5], (BOXES,), 0, 8), jax.random.fold_in(part_keys[5], 1), 0, 7).astype(jnp.int32),
        "rotation": noise(seeds[6], (8, 2, L, MW, MW), (2 * MW) ** -0.5, 0.875, (), jnp.float32),
        "axial_one": noise(seeds[7], (2, MW, 2, L, 2, L), (48 * LEAF_DEV // BOX_DEV) ** -0.5, 0.3125, (), jnp.float32),
        "axial_two": noise(seeds[8], (2, MW, 2, L, 2, L), (48 * BOXES // N_LEAF) ** -0.5, 0.3125, (), jnp.float32),
        "owner_rotation": noise(part_keys[9], (N_LEAF, 2, L, MW, MW), (2 * MW) ** -0.5, 0.875, ((0, 4),), jnp.float32),
        "owner_axial": noise(part_keys[10], (N_LEAF, 2, MW, 2, NR, 2, L), 48 ** -0.5, 0.875, ((0, 4), (4, 4)), jnp.float32),
        "owner_angle": jnp.clip(jax.random.uniform(part_keys[11], (N_LEAF,), jnp.float32, -3.140625, 3.140625), -3.140625, 3.140625),
        "turn_table": noise(part_keys[12], (N_LEAF, NR, MW, MP), (MW * N_LEAF) ** -0.5, 0.625, ((0, 4), (1, 4))),
        "angular_table": noise(seeds[13], (MP, NR, 2 * THETA), (2 * NR) ** -0.5, 0.375, ((0, 4), (1, 4))),
    }


def complex_join(first, second, half):
    real = first[..., :half] - second[..., half:]
    imag = first[..., half:] + second[..., :half]
    return jnp.concatenate([real, imag], axis=-1)

def turn_select(vectors, rotation, octants, backward):
    degrees, orders, width = vectors.shape
    if backward:
        mats = jnp.transpose(rotation, (1, 2, 0, 4, 3))
        sign = -1.0
    else:
        mats = jnp.transpose(rotation, (1, 2, 0, 3, 4))
        sign = 1.0
    mats = mats.reshape(2, degrees, 8 * orders, orders)
    first = jnp.einsum('lQp,lpC->lQC', mats[0], vectors, precision=lax.Precision.HIGHEST)
    second = sign * jnp.einsum('lQp,lpC->lQC', mats[1], vectors, precision=lax.Precision.HIGHEST)
    joined = complex_join(first, second, width // 2).reshape(degrees, 8, orders, width)
    count = octants.shape[0]
    chosen = (octants[None, :] == jnp.arange(8, dtype=jnp.int32)[:, None]).astype(jnp.float32)
    column_mask = jnp.tile(chosen, (1, width // count))
    return lax.optimization_barrier(jnp.sum(joined * column_mask[None, :, None, :], axis=1))

def axial_apply(vectors, axial):
    degrees, orders, width = vectors.shape
    rest = width // 4
    moved = vectors.reshape(degrees, orders, 2, 2, rest)
    moved = jnp.transpose(moved, (1, 3, 0, 2, 4)).reshape(orders, 2 * degrees, 2 * rest)
    mats = axial.reshape(2, orders, 2 * degrees, 2 * degrees)
    first = jnp.einsum('qab,qbC->qaC', mats[0], moved, precision=lax.Precision.HIGHEST)
    second = jnp.einsum('qab,qbC->qaC', mats[1], moved, precision=lax.Precision.HIGHEST)
    joined = complex_join(first, second, rest).reshape(orders, 2, degrees, 2, rest)
    return jnp.transpose(joined, (2, 0, 3, 1, 4)).reshape(degrees, orders, width)

def move_expansion(vectors, octants, rotation, axial):
    turned = turn_select(vectors, rotation, octants, False)
    return turn_select(axial_apply(turned, axial), rotation, octants, True)

def local_boxes(sphere_block, live_count, cluster, leaf_parent, leaf_octant, box_octant, rotation, axial_one, axial_two):
    degrees, orders = (sphere_block.shape[0], sphere_block.shape[1])
    channel = sphere_block.shape[2] * sphere_block.shape[3] * sphere_block.shape[4]
    slots = sphere_block.shape[-1]
    per_block = slots // SBLK
    alive = jnp.arange(slots, dtype=jnp.int32) // per_block < live_count
    leaf_total = leaf_parent.shape[0]
    member = ((cluster[:, None] == jnp.arange(leaf_total, dtype=jnp.int32)[None, :]) & alive[:, None]).astype(jnp.float32)
    ident = jnp.eye(channel, dtype=jnp.float32)
    spread = (ident[:, None, :, None] * member[None, :, None, :]).reshape(channel * slots, channel * leaf_total)
    leaves = jnp.dot(sphere_block.reshape(degrees * orders, channel * slots).astype(jnp.float32), spread, precision=lax.Precision.HIGHEST).reshape(degrees, orders, channel * leaf_total)
    moved = move_expansion(leaves, leaf_octant, rotation, axial_one)
    box_total = box_octant.shape[0]
    parents = (leaf_parent[:, None] == jnp.arange(box_total, dtype=jnp.int32)[None, :]).astype(jnp.float32)
    wide_parents = (ident[:, None, :, None] * parents[None, :, None, :]).reshape(channel * leaf_total, channel * box_total)
    boxes = jnp.einsum('lpC,CD->lpD', moved, wide_parents, precision=lax.Precision.HIGHEST)
    outer = move_expansion(boxes, box_octant, rotation, axial_two)
    return outer.reshape(degrees, orders, channel, box_total).sum(-1)

def owner_frame(owner_sum, owner_turn, owner_shift):
    degrees, orders, width = owner_sum.shape
    states = width // 4
    first = jnp.einsum('lqp,lpC->lqC', owner_turn[0], owner_sum, precision=lax.Precision.HIGHEST)
    second = jnp.einsum('lqp,lpC->lqC', owner_turn[1], owner_sum, precision=lax.Precision.HIGHEST)
    turned = complex_join(first, second, width // 2)
    moved = turned.reshape(degrees, orders, 2, 2, states)
    moved = jnp.transpose(moved, (1, 3, 0, 2, 4)).reshape(orders, 2 * degrees, 2 * states)
    root_degrees = owner_shift.shape[3]
    mats = owner_shift.reshape(2, orders, 2 * root_degrees, 2 * degrees)
    first = jnp.einsum('qab,qbC->qaC', mats[0], moved, precision=lax.Precision.HIGHEST)
    second = jnp.einsum('qab,qbC->qaC', mats[1], moved, precision=lax.Precision.HIGHEST)
    joined = complex_join(first, second, states).reshape(orders, 2, root_degrees, 2, states)
    framed = jnp.transpose(joined, (2, 1, 3, 4, 0)).reshape(root_degrees, 4 * states, orders)
    return framed.astype(jnp.bfloat16)

def rotate_back(framed, functions, azimuth, first_order, half_orders):
    root_degrees, width = (framed.shape[0], framed.shape[1])
    states = width // 4
    orders_here = functions.shape[2]
    values = jnp.einsum('nCm,nmj->nCj', framed.astype(jnp.float32), functions.astype(jnp.float32), precision=lax.Precision.HIGHEST)
    values = values.reshape(root_degrees, 2, 2, states, orders_here)
    order_values = (first_order + jnp.arange(orders_here, dtype=jnp.int32) - half_orders).astype(jnp.float32)
    cosine = jnp.cos(order_values * azimuth)
    sine = jnp.sin(order_values * azimuth)
    real_part = cosine * values[:, :, 0] + sine * values[:, :, 1]
    imag_part = cosine * values[:, :, 1] - sine * values[:, :, 0]
    joined = jnp.stack([real_part, imag_part], axis=2)
    return jnp.transpose(joined, (4, 1, 2, 3, 0)).reshape(orders_here, 4 * states * root_degrees)

def legendre_field(root_coef, table):
    orders_here, root_degrees = (table.shape[0], table.shape[1])
    lat_total = table.shape[2] // 2
    rows = root_coef.shape[1] // root_degrees
    states = rows // 4
    half = rows // 2
    blocks = jnp.einsum('jrn,jnK->jrK', root_coef.reshape(orders_here, rows, root_degrees).astype(jnp.float32), table.astype(jnp.float32), precision=lax.Precision.HIGHEST)
    theta_part = blocks[:, :half, :lat_total] + blocks[:, half:, lat_total:]
    cross = blocks[:, :half, lat_total:] + blocks[:, half:, :lat_total]
    phi_part = jnp.concatenate([-cross[:, states:], cross[:, :states]], axis=1)
    return jnp.concatenate([theta_part, phi_part], axis=1)

def phase_table(orders, longitudes):
    order_ids = jnp.arange(orders, dtype=jnp.int32) - orders // 2
    column = jnp.arange(2 * longitudes, dtype=jnp.int32)
    along = column % longitudes
    quarter = (column // longitudes).astype(jnp.float32)
    remainder = jnp.mod(order_ids[:, None] * along[None, :], longitudes)
    phase = remainder.astype(jnp.float32) * (2.0 * math.pi / longitudes) - quarter[None, :] * (0.5 * math.pi)
    return jnp.cos(phase).astype(jnp.bfloat16)

def synthesize(spectrum, longitudes, states):
    orders = spectrum.shape[1]
    table = phase_table(orders, longitudes)
    product = jnp.dot(spectrum.astype(jnp.float32), table.astype(jnp.float32), precision=lax.Precision.HIGHEST)
    product = product.reshape(2, 2, states, -1, 2 * longitudes)
    real_part = product[:, 0, :, :, :longitudes] - product[:, 1, :, :, longitudes:]
    imag_part = product[:, 0, :, :, longitudes:] + product[:, 1, :, :, :longitudes]
    joined = jnp.stack([real_part, imag_part], axis=3)
    return jnp.transpose(joined, (2, 1, 0, 3, 4)) * (1.0 / math.sqrt(orders))

def reference(sphere_coef, live_blocks, cluster, leaf_parent, leaf_octant, box_octant, rotation, axial_one, axial_two, owner_rotation, owner_axial, owner_angle, turn_table, angular_table):
    holders = live_blocks.shape[0]
    grouped = sphere_coef.reshape(sphere_coef.shape[:-1] + (holders, SPH_DEV))
    grouped = jnp.moveaxis(grouped, 5, 0)
    records = (grouped, live_blocks, cluster.reshape(holders, SPH_DEV), leaf_parent.reshape(holders, LEAF_DEV), leaf_octant.reshape(holders, LEAF_DEV), box_octant.reshape(holders, BOX_DEV))

    def one_holder(record):
        return local_boxes(record[0], record[1], record[2], record[3], record[4], record[5], rotation, axial_one, axial_two)
    partials = lax.map(one_holder, records)
    owner_sum = partials.reshape((N_LEAF, holders // N_LEAF) + partials.shape[1:]).sum(axis=1)
    frames = lax.map(lambda record: owner_frame(record[0], record[1], record[2]), (owner_sum, owner_rotation, owner_axial))

    def add_owner(running, record):
        return (running + rotate_back(record[0], record[1], record[2], 0, MP // 2), None)
    initial = jnp.zeros((MP, 16 * NR), jnp.float32)
    root, _ = lax.scan(add_owner, initial, (frames, turn_table, owner_angle))
    root_coef = root.astype(jnp.bfloat16)
    block_rows = MP // N_LEAF

    def synth_block(block_id):
        first_row = block_id * block_rows
        root_piece = lax.dynamic_slice_in_dim(root_coef, first_row, block_rows, 0)
        table_piece = lax.dynamic_slice_in_dim(angular_table, first_row, block_rows, 0)
        return legendre_field(root_piece, table_piece)
    fields = lax.map(synth_block, jnp.arange(N_LEAF, dtype=jnp.int32))
    field_full = fields.reshape(MP, 16, THETA)
    spectrum = jnp.transpose(field_full, (1, 2, 0)).reshape(16 * THETA, MP).astype(jnp.bfloat16)
    return synthesize(spectrum, PHI, STATES)
```

```python
import math

import jax
import jax.numpy as jnp
from jax import lax
from jax.sharding import PartitionSpec as P

SBLK = 4
PHI = 2048
HI = lax.Precision.HIGHEST


def forward_blocks(rot):
    wr, wi = rot[..., 0, :, :, :], rot[..., 1, :, :, :]
    top = jnp.stack([wr, -wi], axis=-2)
    bottom = jnp.stack([wi, wr], axis=-2)
    return jnp.stack([top, bottom], axis=-4)


def backward_blocks(rot):
    wr = jnp.swapaxes(rot[..., 0, :, :, :], -1, -2)
    wi = jnp.swapaxes(rot[..., 1, :, :, :], -1, -2)
    top = jnp.stack([wr, wi], axis=-2)
    bottom = jnp.stack([-wi, wr], axis=-2)
    return jnp.stack([top, bottom], axis=-4)


def axial_blocks(axial):
    ar, ai = axial[0], axial[1]
    top = jnp.stack([ar, -ai], axis=-3)
    bottom = jnp.stack([ai, ar], axis=-3)
    return jnp.stack([top, bottom], axis=1)


def level(grouped, rot, axial):
    wf = forward_blocks(rot)
    wb = backward_blocks(rot)
    ab = axial_blocks(axial)
    turned = jnp.einsum("onaqrp,onrptj->qatnoj", wf, grouped, precision=HI)
    shifted = jnp.einsum("qauwrtn,qrtnoj->wauoqj", ab, turned, precision=HI)
    return _back(wb, shifted)


def _back(wb, shifted):
    return jnp.einsum("owbpaq,wauoqj->wbpuj", wb, shifted, precision=HI)


def local_boxes(sphere_block, live_count, cluster, leaf_parent, leaf_octant, box_octant, rotation, axial_one, axial_two):
    degrees, orders, parts, types, states, slots = sphere_block.shape
    per_block = slots // SBLK
    box_total = box_octant.shape[0]
    leaf_total = leaf_parent.shape[0]
    alive = jnp.arange(slots, dtype=jnp.int32) // per_block < live_count
    member = (cluster[:, None] == jnp.arange(leaf_total, dtype=jnp.int32)[None, :]) & alive[:, None]
    key = leaf_octant * box_total + leaf_parent
    group = key[:, None] == jnp.arange(8 * box_total, dtype=jnp.int32)[None, :]
    sphere_group = jnp.dot(member.astype(jnp.float32), group.astype(jnp.float32)).astype(jnp.bfloat16)
    sphere_group = sphere_group.reshape(slots, 8, box_total)
    grouped = jnp.einsum("nprtsS,Sob->onrptsb", sphere_block, sphere_group, preferred_element_type=jnp.float32)
    grouped = grouped.reshape(8, degrees, parts, orders, types, states * box_total)
    boxes = level(grouped, rotation, axial_one).reshape(degrees, parts, orders, types, states, box_total)
    pick = (box_octant[None, :] == jnp.arange(8, dtype=jnp.int32)[:, None]).astype(jnp.float32)
    outer_grouped = jnp.einsum("nrptsb,ob->onrpts", boxes, pick, precision=HI)
    return level(outer_grouped, rotation, axial_two)


def owner_frame(owner_sum, owner_turn, owner_shift):
    wf = forward_blocks(owner_turn)
    ab = axial_blocks(owner_shift)
    turned = jnp.einsum("naqrp,nrpts->qatns", wf, owner_sum, precision=HI)
    shifted = jnp.einsum("qauwrtn,qrtns->wuasq", ab, turned, precision=HI)
    return shifted.astype(jnp.bfloat16)


def rotate_back(framed, functions, azimuth, half_orders):
    orders_here = functions.shape[2]
    values = jnp.einsum("wursq,wqj->jursw", framed, functions, preferred_element_type=jnp.float32)
    order_values = (jnp.arange(orders_here, dtype=jnp.int32) - half_orders).astype(jnp.float32)
    cosine = jnp.cos(order_values * azimuth)[:, None, None, None]
    sine = jnp.sin(order_values * azimuth)[:, None, None, None]
    real_part = cosine * values[:, :, 0] + sine * values[:, :, 1]
    imag_part = cosine * values[:, :, 1] - sine * values[:, :, 0]
    joined = jnp.stack([real_part, imag_part], axis=2)
    return joined.reshape(orders_here, -1)


def legendre_field(root_coef, table):
    orders_here, root_degrees = (table.shape[0], table.shape[1])
    lat_total = table.shape[2] // 2
    tab = table.reshape(orders_here, root_degrees, 2, lat_total)
    blocks = jnp.einsum("jursw,jwkh->jukrsh", root_coef, tab, preferred_element_type=jnp.float32)
    theta_part = blocks[:, 0, 0] + blocks[:, 1, 1]
    cross = blocks[:, 0, 1] + blocks[:, 1, 0]
    phi_part = jnp.stack([-cross[:, 1], cross[:, 0]], axis=1)
    return jnp.stack([theta_part, phi_part], axis=1)


def synthesize(spectrum, longitudes):
    orders = spectrum.shape[-1]
    fine = 128
    coarse = longitudes // fine
    order_ids = jnp.arange(orders, dtype=jnp.int32) - orders // 2
    coarse_angle = jnp.mod(order_ids[:, None] * (fine * jnp.arange(coarse, dtype=jnp.int32))[None, :], longitudes)
    coarse_angle = coarse_angle.astype(jnp.float32) * (2.0 * math.pi / longitudes)
    fine_angle = jnp.mod(order_ids[:, None] * jnp.arange(fine, dtype=jnp.int32)[None, :], longitudes)
    fine_angle = fine_angle.astype(jnp.float32) * (2.0 * math.pi / longitudes)
    pc, ps = jnp.cos(coarse_angle), jnp.sin(coarse_angle)
    qc, qs = jnp.cos(fine_angle), jnp.sin(fine_angle)
    spec = spectrum.astype(jnp.float32)
    sr, si = spec[:, 0], spec[:, 1]
    vr = sr[..., None, :] * pc.T - si[..., None, :] * ps.T
    vi = sr[..., None, :] * ps.T + si[..., None, :] * pc.T
    lhs = jnp.stack([vr, vi], axis=-2)
    rhs = jnp.stack([jnp.stack([qc, qs], axis=1), jnp.stack([-qs, qc], axis=1)], axis=0)
    out = jnp.einsum("csxkam,amfb->xscfkb", lhs, rhs, precision=HI)
    out = out.reshape(out.shape[:4] + (longitudes,))
    return out * (1.0 / math.sqrt(orders))


def on_device(
    sphere_coef,
    live_blocks,
    cluster,
    leaf_parent,
    leaf_octant,
    box_octant,
    rotation,
    axial_one,
    axial_two,
    owner_rotation,
    owner_axial,
    owner_angle,
    turn_table,
    angular_table,
):
    partial_owner = local_boxes(
        sphere_coef,
        live_blocks[0],
        cluster,
        leaf_parent,
        leaf_octant,
        box_octant,
        rotation,
        axial_one,
        axial_two,
    )
    owner_sum = lax.psum(partial_owner, ("state", "sub"))
    framed = owner_frame(owner_sum, owner_rotation[0], owner_axial[0])
    leaf_size = lax.axis_size("leaf")
    orders = turn_table.shape[3]
    half_orders = orders // 2
    own_orders = orders // leaf_size
    own_azimuth = owner_angle[lax.axis_index("leaf")]
    contribution = rotate_back(framed, turn_table[0], own_azimuth, half_orders)
    root = lax.psum_scatter(contribution, "leaf", scatter_dimension=0, tiled=True)
    root_coef = root.astype(jnp.bfloat16).reshape(own_orders, 2, 2, -1, angular_table.shape[1])
    field = legendre_field(root_coef, angular_table)
    group_size = lax.axis_size("state") * lax.axis_size("sub")
    lat_total = field.shape[-1]
    lat_rows = lat_total // (leaf_size * group_size)
    shaped = field.reshape(own_orders, 2, 2, -1, leaf_size, group_size, lat_rows)
    shaped = jnp.transpose(shaped, (5, 4, 1, 2, 3, 6, 0))
    lead = shaped.shape[2:6]
    shaped = shaped.reshape(group_size, leaf_size, -1)
    summed = lax.psum_scatter(shaped.astype(jnp.bfloat16), ("state", "sub"), scatter_dimension=0, tiled=True)
    moved = lax.all_to_all(summed, "leaf", split_axis=1, concat_axis=0, tiled=True)
    spectrum = moved.reshape((leaf_size,) + lead + (own_orders,))
    spectrum = jnp.moveaxis(spectrum, 0, -2).reshape(lead + (orders,))
    return synthesize(spectrum, PHI)


def solution(mesh):
    return jax.shard_map(
        on_device,
        mesh=mesh,
        in_specs=(
            P(None, None, None, None, None, ("groups", "leaf", "state", "sub")),
            P(("groups", "leaf", "state", "sub")),
            P(("groups", "leaf", "state", "sub")),
            P(("groups", "leaf", "state", "sub")),
            P(("groups", "leaf", "state", "sub")),
            P(("groups", "leaf", "state", "sub")),
            P(),
            P(),
            P(),
            P(("groups", "leaf"), None, None, None, None),
            P(("groups", "leaf"), None, None, None, ("state", "sub"), None, None),
            P("groups"),
            P(("groups", "leaf"), ("state", "sub"), None, None),
            P("leaf", ("state", "sub"), None),
        ),
        out_specs=P(("groups", "leaf", "state", "sub"), None, None, None, None),
        check_vma=False,
    )
```

```python
import math

import jax
import jax.numpy as jnp
from jax import lax
from jax.sharding import PartitionSpec as P

STATES = 4
SBLK = 4
PHI = 2048
HI = lax.Precision.HIGHEST


def complex_join(first, second, half):
    real = first[..., :half] - second[..., half:]
    imag = first[..., half:] + second[..., :half]
    return jnp.concatenate([real, imag], axis=-1)


def turn_select(vectors, rotation, octants, backward):
    degrees, orders, width = vectors.shape
    if backward:
        mats = jnp.transpose(rotation, (1, 2, 0, 4, 3))
        sign = -1.0
    else:
        mats = jnp.transpose(rotation, (1, 2, 0, 3, 4))
        sign = 1.0
    mats = mats.reshape(2, degrees, 8 * orders, orders)
    first = jnp.einsum("lQp,lpC->lQC", mats[0], vectors, precision=lax.Precision.HIGHEST)
    second = sign * jnp.einsum("lQp,lpC->lQC", mats[1], vectors, precision=lax.Precision.HIGHEST)
    joined = complex_join(first, second, width // 2).reshape(degrees, 8, orders, width)
    count = octants.shape[0]
    chosen = (octants[None, :] == jnp.arange(8, dtype=jnp.int32)[:, None]).astype(jnp.float32)
    column_mask = jnp.tile(chosen, (1, width // count))
    return jnp.sum(joined * column_mask[None, :, None, :], axis=1)


def axial_apply(vectors, axial):
    degrees, orders, width = vectors.shape
    rest = width // 4
    moved = vectors.reshape(degrees, orders, 2, 2, rest)
    moved = jnp.transpose(moved, (1, 3, 0, 2, 4)).reshape(orders, 2 * degrees, 2 * rest)
    mats = axial.reshape(2, orders, 2 * degrees, 2 * degrees)
    first = jnp.einsum("qab,qbC->qaC", mats[0], moved, precision=lax.Precision.HIGHEST)
    second = jnp.einsum("qab,qbC->qaC", mats[1], moved, precision=lax.Precision.HIGHEST)
    joined = complex_join(first, second, rest).reshape(orders, 2, degrees, 2, rest)
    return jnp.transpose(joined, (2, 0, 3, 1, 4)).reshape(degrees, orders, width)


def move_expansion(vectors, octants, rotation, axial):
    turned = turn_select(vectors, rotation, octants, False)
    return turn_select(axial_apply(turned, axial), rotation, octants, True)


def local_boxes(
    sphere_block,
    live_count,
    cluster,
    leaf_parent,
    leaf_octant,
    box_octant,
    rotation,
    axial_one,
    axial_two,
):
    degrees, orders = (sphere_block.shape[0], sphere_block.shape[1])
    channel = sphere_block.shape[2] * sphere_block.shape[3] * sphere_block.shape[4]
    slots = sphere_block.shape[-1]
    per_block = slots // SBLK
    alive = jnp.arange(slots, dtype=jnp.int32) // per_block < live_count
    leaf_total = leaf_parent.shape[0]
    member = (
        (cluster[:, None] == jnp.arange(leaf_total, dtype=jnp.int32)[None, :]) & alive[:, None]
    ).astype(jnp.bfloat16)
    ident = jnp.eye(channel, dtype=jnp.bfloat16)
    spread = (ident[:, None, :, None] * member[None, :, None, :]).reshape(
        channel * slots, channel * leaf_total
    )
    leaves = jnp.dot(
        sphere_block.reshape(degrees * orders, channel * slots),
        spread,
        preferred_element_type=jnp.float32,
    ).reshape(degrees, orders, channel * leaf_total)
    moved = move_expansion(leaves, leaf_octant, rotation, axial_one)
    box_total = box_octant.shape[0]
    parents = (leaf_parent[:, None] == jnp.arange(box_total, dtype=jnp.int32)[None, :]).astype(
        jnp.float32
    )
    wide_ident = jnp.eye(channel, dtype=jnp.float32)
    wide_parents = (wide_ident[:, None, :, None] * parents[None, :, None, :]).reshape(
        channel * leaf_total, channel * box_total
    )
    boxes = jnp.einsum("lpC,CD->lpD", moved, wide_parents, precision=lax.Precision.HIGHEST)
    outer = move_expansion(boxes, box_octant, rotation, axial_two)
    return outer.reshape(degrees, orders, channel, box_total).sum(-1)


def owner_frame(owner_sum, owner_turn, owner_shift):
    degrees, orders, width = owner_sum.shape
    states = width // 4
    first = jnp.einsum("lqp,lpC->lqC", owner_turn[0], owner_sum, precision=lax.Precision.HIGHEST)
    second = jnp.einsum("lqp,lpC->lqC", owner_turn[1], owner_sum, precision=lax.Precision.HIGHEST)
    turned = complex_join(first, second, width // 2)
    moved = turned.reshape(degrees, orders, 2, 2, states)
    moved = jnp.transpose(moved, (1, 3, 0, 2, 4)).reshape(orders, 2 * degrees, 2 * states)
    root_degrees = owner_shift.shape[3]
    mats = owner_shift.reshape(2, orders, 2 * root_degrees, 2 * degrees)
    first = jnp.einsum("qab,qbC->qaC", mats[0], moved, precision=lax.Precision.HIGHEST)
    second = jnp.einsum("qab,qbC->qaC", mats[1], moved, precision=lax.Precision.HIGHEST)
    joined = complex_join(first, second, states).reshape(orders, 2, root_degrees, 2, states)
    framed = jnp.transpose(joined, (2, 1, 3, 4, 0)).reshape(root_degrees, 4 * states, orders)
    return framed.astype(jnp.bfloat16)


def rotate_back(framed, functions, azimuth, half_orders):
    root_degrees, width = (framed.shape[0], framed.shape[1])
    states = width // 4
    orders_here = functions.shape[2]
    values = jnp.einsum("nCm,nmj->nCj", framed, functions, preferred_element_type=jnp.float32)
    values = values.reshape(root_degrees, 2, 2, states, orders_here)
    order_values = (jnp.arange(orders_here, dtype=jnp.int32) - half_orders).astype(jnp.float32)
    cosine = jnp.cos(order_values * azimuth)
    sine = jnp.sin(order_values * azimuth)
    real_part = cosine * values[:, :, 0] + sine * values[:, :, 1]
    imag_part = cosine * values[:, :, 1] - sine * values[:, :, 0]
    joined = jnp.stack([real_part, imag_part], axis=2)
    return jnp.transpose(joined, (4, 1, 2, 3, 0)).reshape(orders_here, 4 * states * root_degrees)


def legendre_field(root_coef, table):
    orders_here, root_degrees = (table.shape[0], table.shape[1])
    lat_total = table.shape[2] // 2
    rows = root_coef.shape[1] // root_degrees
    states = rows // 4
    half = rows // 2
    blocks = jnp.einsum(
        "jrn,jnK->jrK",
        root_coef.reshape(orders_here, rows, root_degrees),
        table,
        preferred_element_type=jnp.float32,
    )
    theta_part = blocks[:, :half, :lat_total] + blocks[:, half:, lat_total:]
    cross = blocks[:, :half, lat_total:] + blocks[:, half:, :lat_total]
    phi_part = jnp.concatenate([-cross[:, states:], cross[:, :states]], axis=1)
    return jnp.concatenate([theta_part, phi_part], axis=1)


def synthesize(spectrum, longitudes):
    orders = spectrum.shape[-1]
    fine = 128
    coarse = longitudes // fine
    order_ids = jnp.arange(orders, dtype=jnp.int32) - orders // 2
    coarse_angle = jnp.mod(order_ids[:, None] * (fine * jnp.arange(coarse, dtype=jnp.int32))[None, :], longitudes)
    coarse_angle = coarse_angle.astype(jnp.float32) * (2.0 * math.pi / longitudes)
    fine_angle = jnp.mod(order_ids[:, None] * jnp.arange(fine, dtype=jnp.int32)[None, :], longitudes)
    fine_angle = fine_angle.astype(jnp.float32) * (2.0 * math.pi / longitudes)
    pc, ps = jnp.cos(coarse_angle), jnp.sin(coarse_angle)
    qc, qs = jnp.cos(fine_angle), jnp.sin(fine_angle)
    spec = spectrum.astype(jnp.float32)
    sr, si = spec[:, 0], spec[:, 1]
    vr = sr[..., None, :] * pc.T - si[..., None, :] * ps.T
    vi = sr[..., None, :] * ps.T + si[..., None, :] * pc.T
    lhs = jnp.stack([vr, vi], axis=-2)
    rhs = jnp.stack([jnp.stack([qc, qs], axis=1), jnp.stack([-qs, qc], axis=1)], axis=0)
    out = jnp.einsum("csxkam,amfb->xscfkb", lhs, rhs, precision=HI)
    out = out.reshape(out.shape[:4] + (longitudes,))
    return out * (1.0 / math.sqrt(orders))


def on_device(
    sphere_coef,
    live_blocks,
    cluster,
    leaf_parent,
    leaf_octant,
    box_octant,
    rotation,
    axial_one,
    axial_two,
    owner_rotation,
    owner_axial,
    owner_angle,
    turn_table,
    angular_table,
):
    partial_owner = local_boxes(
        sphere_coef,
        live_blocks[0],
        cluster,
        leaf_parent,
        leaf_octant,
        box_octant,
        rotation,
        axial_one,
        axial_two,
    )
    owner_sum = lax.psum(partial_owner, ("state", "sub"))
    framed = owner_frame(owner_sum, owner_rotation[0], owner_axial[0])
    leaf_size = lax.axis_size("leaf")
    orders = turn_table.shape[3]
    half_orders = orders // 2
    own_orders = orders // leaf_size
    own_azimuth = owner_angle[lax.axis_index("leaf")]
    piece = turn_table[0]
    root = lax.psum_scatter(
        rotate_back(framed, piece, own_azimuth, half_orders),
        "leaf",
        scatter_dimension=0,
        tiled=True,
    )
    root_coef = root.astype(jnp.bfloat16)
    field = legendre_field(root_coef, angular_table)
    channel = field.shape[1]
    group_size = lax.axis_size("state") * lax.axis_size("sub")
    lat_rows = field.shape[2] // (leaf_size * group_size)
    shaped = field.reshape(own_orders, channel, leaf_size, group_size, lat_rows)
    shaped = jnp.transpose(shaped, (3, 2, 1, 4, 0)).reshape(
        group_size, leaf_size, channel * lat_rows * own_orders
    )
    summed = lax.psum_scatter(
        shaped.astype(jnp.bfloat16), ("state", "sub"), scatter_dimension=0, tiled=True
    )
    moved = lax.all_to_all(summed, "leaf", split_axis=1, concat_axis=2, tiled=True)
    spectrum = moved.reshape(leaf_size, channel, lat_rows, own_orders)
    spectrum = jnp.transpose(spectrum, (1, 2, 0, 3)).reshape(2, 2, -1, lat_rows, orders)
    return synthesize(spectrum, PHI)


def solution(mesh):
    return jax.shard_map(
        on_device,
        mesh=mesh,
        in_specs=(
            P(None, None, None, None, None, ("groups", "leaf", "state", "sub")),
            P(("groups", "leaf", "state", "sub")),
            P(("groups", "leaf", "state", "sub")),
            P(("groups", "leaf", "state", "sub")),
            P(("groups", "leaf", "state", "sub")),
            P(("groups", "leaf", "state", "sub")),
            P(),
            P(),
            P(),
            P(("groups", "leaf"), None, None, None, None),
            P(("groups", "leaf"), None, None, None, ("state", "sub"), None, None),
            P("groups"),
            P(("groups", "leaf"), ("state", "sub"), None, None),
            P("leaf", ("state", "sub"), None),
        ),
        out_specs=P(("groups", "leaf", "state", "sub"), None, None, None, None),
        check_vma=False,
    )
```

```python
import math

import jax
import jax.numpy as jnp
from jax import lax
from jax.sharding import PartitionSpec as P

STATES = 4
SBLK = 4
PHI = 2048
HI = lax.Precision.HIGHEST
TABLE_BYTES = 8 << 20


def complex_join(first, second, half):
    real = first[..., :half] - second[..., half:]
    imag = first[..., half:] + second[..., :half]
    return jnp.concatenate([real, imag], axis=-1)


def turn_select(vectors, rotation, octants, backward):
    degrees, orders, width = vectors.shape
    if backward:
        mats = jnp.transpose(rotation, (1, 2, 0, 4, 3))
        sign = -1.0
    else:
        mats = jnp.transpose(rotation, (1, 2, 0, 3, 4))
        sign = 1.0
    mats = mats.reshape(2, degrees, 8 * orders, orders)
    first = jnp.einsum("lQp,lpC->lQC", mats[0], vectors, precision=lax.Precision.HIGHEST)
    second = sign * jnp.einsum("lQp,lpC->lQC", mats[1], vectors, precision=lax.Precision.HIGHEST)
    joined = complex_join(first, second, width // 2).reshape(degrees, 8, orders, width)
    count = octants.shape[0]
    chosen = (octants[None, :] == jnp.arange(8, dtype=jnp.int32)[:, None]).astype(jnp.float32)
    column_mask = jnp.tile(chosen, (1, width // count))
    return jnp.sum(joined * column_mask[None, :, None, :], axis=1)


def axial_apply(vectors, axial):
    degrees, orders, width = vectors.shape
    rest = width // 4
    moved = vectors.reshape(degrees, orders, 2, 2, rest)
    moved = jnp.transpose(moved, (1, 3, 0, 2, 4)).reshape(orders, 2 * degrees, 2 * rest)
    mats = axial.reshape(2, orders, 2 * degrees, 2 * degrees)
    first = jnp.einsum("qab,qbC->qaC", mats[0], moved, precision=lax.Precision.HIGHEST)
    second = jnp.einsum("qab,qbC->qaC", mats[1], moved, precision=lax.Precision.HIGHEST)
    joined = complex_join(first, second, rest).reshape(orders, 2, degrees, 2, rest)
    return jnp.transpose(joined, (2, 0, 3, 1, 4)).reshape(degrees, orders, width)


def move_expansion(vectors, octants, rotation, axial):
    turned = turn_select(vectors, rotation, octants, False)
    return turn_select(axial_apply(turned, axial), rotation, octants, True)


def local_boxes(
    sphere_block,
    live_count,
    cluster,
    leaf_parent,
    leaf_octant,
    box_octant,
    rotation,
    axial_one,
    axial_two,
):
    degrees, orders = (sphere_block.shape[0], sphere_block.shape[1])
    channel = sphere_block.shape[2] * sphere_block.shape[3] * sphere_block.shape[4]
    slots = sphere_block.shape[-1]
    per_block = slots // SBLK
    alive = jnp.arange(slots, dtype=jnp.int32) // per_block < live_count
    leaf_total = leaf_parent.shape[0]
    member = (
        (cluster[:, None] == jnp.arange(leaf_total, dtype=jnp.int32)[None, :]) & alive[:, None]
    ).astype(jnp.bfloat16)
    ident = jnp.eye(channel, dtype=jnp.bfloat16)
    spread = (ident[:, None, :, None] * member[None, :, None, :]).reshape(
        channel * slots, channel * leaf_total
    )
    leaves = jnp.dot(
        sphere_block.reshape(degrees * orders, channel * slots),
        spread,
        preferred_element_type=jnp.float32,
    ).reshape(degrees, orders, channel * leaf_total)
    moved = move_expansion(leaves, leaf_octant, rotation, axial_one)
    box_total = box_octant.shape[0]
    parents = (leaf_parent[:, None] == jnp.arange(box_total, dtype=jnp.int32)[None, :]).astype(
        jnp.float32
    )
    wide_ident = jnp.eye(channel, dtype=jnp.float32)
    wide_parents = (wide_ident[:, None, :, None] * parents[None, :, None, :]).reshape(
        channel * leaf_total, channel * box_total
    )
    boxes = jnp.einsum("lpC,CD->lpD", moved, wide_parents, precision=lax.Precision.HIGHEST)
    outer = move_expansion(boxes, box_octant, rotation, axial_two)
    return outer.reshape(degrees, orders, channel, box_total).sum(-1)


def owner_frame(owner_sum, owner_turn, owner_shift):
    degrees, orders, width = owner_sum.shape
    states = width // 4
    first = jnp.einsum("lqp,lpC->lqC", owner_turn[0], owner_sum, precision=lax.Precision.HIGHEST)
    second = jnp.einsum("lqp,lpC->lqC", owner_turn[1], owner_sum, precision=lax.Precision.HIGHEST)
    turned = complex_join(first, second, width // 2)
    moved = turned.reshape(degrees, orders, 2, 2, states)
    moved = jnp.transpose(moved, (1, 3, 0, 2, 4)).reshape(orders, 2 * degrees, 2 * states)
    root_degrees = owner_shift.shape[3]
    mats = owner_shift.reshape(2, orders, 2 * root_degrees, 2 * degrees)
    first = jnp.einsum("qab,qbC->qaC", mats[0], moved, precision=lax.Precision.HIGHEST)
    second = jnp.einsum("qab,qbC->qaC", mats[1], moved, precision=lax.Precision.HIGHEST)
    joined = complex_join(first, second, states).reshape(orders, 2, root_degrees, 2, states)
    framed = jnp.transpose(joined, (2, 1, 3, 4, 0)).reshape(root_degrees, 4 * states, orders)
    return framed.astype(jnp.bfloat16)


def rotate_back(framed, functions, azimuth, half_orders):
    root_degrees, width = (framed.shape[0], framed.shape[1])
    states = width // 4
    orders_here = functions.shape[2]
    values = jnp.einsum("nCm,nmj->nCj", framed, functions, preferred_element_type=jnp.float32)
    values = values.reshape(root_degrees, 2, 2, states, orders_here)
    order_values = (jnp.arange(orders_here, dtype=jnp.int32) - half_orders).astype(jnp.float32)
    cosine = jnp.cos(order_values * azimuth)
    sine = jnp.sin(order_values * azimuth)
    real_part = cosine * values[:, :, 0] + sine * values[:, :, 1]
    imag_part = cosine * values[:, :, 1] - sine * values[:, :, 0]
    joined = jnp.stack([real_part, imag_part], axis=2)
    return jnp.transpose(joined, (4, 1, 2, 3, 0)).reshape(orders_here, 4 * states * root_degrees)


def legendre_field(root_coef, table):
    orders_here, root_degrees = (table.shape[0], table.shape[1])
    lat_total = table.shape[2] // 2
    rows = root_coef.shape[1] // root_degrees
    states = rows // 4
    half = rows // 2
    blocks = jnp.einsum(
        "jrn,jnK->jrK",
        root_coef.reshape(orders_here, rows, root_degrees),
        table,
        preferred_element_type=jnp.float32,
        precision=HI,
    )
    theta_part = blocks[:, :half, :lat_total] + blocks[:, half:, lat_total:]
    cross = blocks[:, :half, lat_total:] + blocks[:, half:, :lat_total]
    phi_part = jnp.concatenate([-cross[:, states:], cross[:, :states]], axis=1)
    return jnp.concatenate([theta_part, phi_part], axis=1)


def synthesize(spectrum, longitudes):
    orders = spectrum.shape[-1]
    fine = 128
    coarse = longitudes // fine
    order_ids = jnp.arange(orders, dtype=jnp.int32) - orders // 2
    coarse_angle = jnp.mod(order_ids[:, None] * (fine * jnp.arange(coarse, dtype=jnp.int32))[None, :], longitudes)
    coarse_angle = coarse_angle.astype(jnp.float32) * (2.0 * math.pi / longitudes)
    fine_angle = jnp.mod(order_ids[:, None] * jnp.arange(fine, dtype=jnp.int32)[None, :], longitudes)
    fine_angle = fine_angle.astype(jnp.float32) * (2.0 * math.pi / longitudes)
    pc, ps = jnp.cos(coarse_angle), jnp.sin(coarse_angle)
    qc, qs = jnp.cos(fine_angle), jnp.sin(fine_angle)
    spec = spectrum.astype(jnp.float32)
    sr, si = spec[:, 0], spec[:, 1]
    vr = sr[..., None, :] * pc.T - si[..., None, :] * ps.T
    vi = sr[..., None, :] * ps.T + si[..., None, :] * pc.T
    lhs = jnp.stack([vr, vi], axis=-2)
    rhs = jnp.stack([jnp.stack([qc, qs], axis=1), jnp.stack([-qs, qc], axis=1)], axis=0)
    out = jnp.einsum("csxkam,amfb->xscfkb", lhs, rhs, precision=HI)
    out = out.reshape(out.shape[:4] + (longitudes,))
    return out * (1.0 / math.sqrt(orders))


def on_device(
    sphere_coef,
    live_blocks,
    cluster,
    leaf_parent,
    leaf_octant,
    box_octant,
    rotation,
    axial_one,
    axial_two,
    owner_rotation,
    owner_axial,
    owner_angle,
    turn_table,
    angular_table,
):
    partial_owner = local_boxes(
        sphere_coef,
        live_blocks[0],
        cluster,
        leaf_parent,
        leaf_octant,
        box_octant,
        rotation,
        axial_one,
        axial_two,
    )
    leaf_size = lax.axis_size("leaf")
    group_size = lax.axis_size("state") * lax.axis_size("sub")
    devices = leaf_size * group_size
    orders = turn_table.shape[3]
    half_orders = orders // 2
    gather_table = angular_table.size * leaf_size * 4 <= TABLE_BYTES
    if gather_table:
        full_table = lax.all_gather(angular_table, "leaf", axis=0, tiled=True)
    owner_sum = lax.psum(partial_owner, ("state", "sub"))
    framed = owner_frame(owner_sum, owner_rotation[0], owner_axial[0])
    own_azimuth = owner_angle[lax.axis_index("leaf")]
    contribution = rotate_back(framed, turn_table[0], own_azimuth, half_orders)
    if gather_table:
        field = legendre_field(contribution, full_table.astype(jnp.float32))
        lat_total = field.shape[2]
        lat_rows = lat_total // devices
        shaped = field.reshape(orders, 2, 2, -1, devices, lat_rows)
        shaped = jnp.transpose(shaped, (4, 1, 2, 3, 5, 0))
        lead = shaped.shape[1:5]
        shaped = shaped.reshape(devices, -1)
        summed = lax.psum_scatter(shaped, ("leaf", "state", "sub"), scatter_dimension=0, tiled=True)
        spectrum = summed.astype(jnp.bfloat16).reshape(lead + (orders,))
        return synthesize(spectrum, PHI)
    own_orders = orders // leaf_size
    root = lax.psum_scatter(contribution, "leaf", scatter_dimension=0, tiled=True)
    root_coef = root.astype(jnp.bfloat16)
    field = legendre_field(root_coef, angular_table)
    channel = field.shape[1]
    lat_rows = field.shape[2] // devices
    shaped = field.reshape(own_orders, channel, leaf_size, group_size, lat_rows)
    shaped = jnp.transpose(shaped, (3, 2, 1, 4, 0)).reshape(group_size, leaf_size, channel * lat_rows * own_orders)
    summed = lax.psum_scatter(shaped.astype(jnp.bfloat16), ("state", "sub"), scatter_dimension=0, tiled=True)
    moved = lax.all_to_all(summed, "leaf", split_axis=1, concat_axis=2, tiled=True)
    spectrum = moved.reshape(leaf_size, channel, lat_rows, own_orders)
    spectrum = jnp.transpose(spectrum, (1, 2, 0, 3)).reshape(2, 2, -1, lat_rows, orders)
    return synthesize(spectrum, PHI)


def solution(mesh):
    return jax.shard_map(
        on_device,
        mesh=mesh,
        in_specs=(
            P(None, None, None, None, None, ("groups", "leaf", "state", "sub")),
            P(("groups", "leaf", "state", "sub")),
            P(("groups", "leaf", "state", "sub")),
            P(("groups", "leaf", "state", "sub")),
            P(("groups", "leaf", "state", "sub")),
            P(("groups", "leaf", "state", "sub")),
            P(),
            P(),
            P(),
            P(("groups", "leaf"), None, None, None, None),
            P(("groups", "leaf"), None, None, None, ("state", "sub"), None, None),
            P("groups"),
            P(("groups", "leaf"), ("state", "sub"), None, None),
            P("leaf", ("state", "sub"), None),
        ),
        out_specs=P(("groups", "leaf", "state", "sub"), None, None, None, None),
        check_vma=False,
    )
```

```python
import math

import jax
import jax.numpy as jnp
from jax import lax
from jax.sharding import PartitionSpec as P

STATES = 4
SBLK = 4
PHI = 2048
HI = lax.Precision.HIGHEST


def complex_join(first, second, half):
    real = first[..., :half] - second[..., half:]
    imag = first[..., half:] + second[..., :half]
    return jnp.concatenate([real, imag], axis=-1)


def turn_select(vectors, rotation, octants, backward):
    degrees, orders, width = vectors.shape
    if backward:
        mats = jnp.transpose(rotation, (1, 2, 0, 4, 3))
        sign = -1.0
    else:
        mats = jnp.transpose(rotation, (1, 2, 0, 3, 4))
        sign = 1.0
    mats = mats.reshape(2, degrees, 8 * orders, orders)
    first = jnp.einsum("lQp,lpC->lQC", mats[0], vectors, precision=lax.Precision.HIGHEST)
    second = sign * jnp.einsum("lQp,lpC->lQC", mats[1], vectors, precision=lax.Precision.HIGHEST)
    joined = complex_join(first, second, width // 2).reshape(degrees, 8, orders, width)
    count = octants.shape[0]
    chosen = (octants[None, :] == jnp.arange(8, dtype=jnp.int32)[:, None]).astype(jnp.float32)
    column_mask = jnp.tile(chosen, (1, width // count))
    return jnp.sum(joined * column_mask[None, :, None, :], axis=1)


def axial_apply(vectors, axial):
    degrees, orders, width = vectors.shape
    rest = width // 4
    moved = vectors.reshape(degrees, orders, 2, 2, rest)
    moved = jnp.transpose(moved, (1, 3, 0, 2, 4)).reshape(orders, 2 * degrees, 2 * rest)
    mats = axial.reshape(2, orders, 2 * degrees, 2 * degrees)
    first = jnp.einsum("qab,qbC->qaC", mats[0], moved, precision=lax.Precision.HIGHEST)
    second = jnp.einsum("qab,qbC->qaC", mats[1], moved, precision=lax.Precision.HIGHEST)
    joined = complex_join(first, second, rest).reshape(orders, 2, degrees, 2, rest)
    return jnp.transpose(joined, (2, 0, 3, 1, 4)).reshape(degrees, orders, width)


def move_expansion(vectors, octants, rotation, axial):
    turned = turn_select(vectors, rotation, octants, False)
    return turn_select(axial_apply(turned, axial), rotation, octants, True)


def local_boxes(
    sphere_block,
    live_count,
    cluster,
    leaf_parent,
    leaf_octant,
    box_octant,
    rotation,
    axial_one,
    axial_two,
):
    degrees, orders = (sphere_block.shape[0], sphere_block.shape[1])
    channel = sphere_block.shape[2] * sphere_block.shape[3] * sphere_block.shape[4]
    slots = sphere_block.shape[-1]
    per_block = slots // SBLK
    alive = jnp.arange(slots, dtype=jnp.int32) // per_block < live_count
    leaf_total = leaf_parent.shape[0]
    member = (
        (cluster[:, None] == jnp.arange(leaf_total, dtype=jnp.int32)[None, :]) & alive[:, None]
    ).astype(jnp.bfloat16)
    ident = jnp.eye(channel, dtype=jnp.bfloat16)
    spread = (ident[:, None, :, None] * member[None, :, None, :]).reshape(
        channel * slots, channel * leaf_total
    )
    leaves = jnp.dot(
        sphere_block.reshape(degrees * orders, channel * slots),
        spread,
        preferred_element_type=jnp.float32,
    ).reshape(degrees, orders, channel * leaf_total)
    moved = move_expansion(leaves, leaf_octant, rotation, axial_one)
    box_total = box_octant.shape[0]
    parents = (leaf_parent[:, None] == jnp.arange(box_total, dtype=jnp.int32)[None, :]).astype(
        jnp.float32
    )
    wide_ident = jnp.eye(channel, dtype=jnp.float32)
    wide_parents = (wide_ident[:, None, :, None] * parents[None, :, None, :]).reshape(
        channel * leaf_total, channel * box_total
    )
    boxes = jnp.einsum("lpC,CD->lpD", moved, wide_parents, precision=lax.Precision.HIGHEST)
    outer = move_expansion(boxes, box_octant, rotation, axial_two)
    return outer.reshape(degrees, orders, channel, box_total).sum(-1)


def owner_frame(owner_sum, owner_turn, owner_shift):
    degrees, orders, width = owner_sum.shape
    states = width // 4
    first = jnp.einsum("lqp,lpC->lqC", owner_turn[0], owner_sum, precision=lax.Precision.HIGHEST)
    second = jnp.einsum("lqp,lpC->lqC", owner_turn[1], owner_sum, precision=lax.Precision.HIGHEST)
    turned = complex_join(first, second, width // 2)
    moved = turned.reshape(degrees, orders, 2, 2, states)
    moved = jnp.transpose(moved, (1, 3, 0, 2, 4)).reshape(orders, 2 * degrees, 2 * states)
    root_degrees = owner_shift.shape[3]
    mats = owner_shift.reshape(2, orders, 2 * root_degrees, 2 * degrees)
    first = jnp.einsum("qab,qbC->qaC", mats[0], moved, precision=lax.Precision.HIGHEST)
    second = jnp.einsum("qab,qbC->qaC", mats[1], moved, precision=lax.Precision.HIGHEST)
    joined = complex_join(first, second, states).reshape(orders, 2, root_degrees, 2, states)
    framed = jnp.transpose(joined, (2, 1, 3, 4, 0)).reshape(root_degrees, 4 * states, orders)
    return framed.astype(jnp.bfloat16)


def rotate_back(framed, functions, azimuth, half_orders):
    root_degrees, width = (framed.shape[0], framed.shape[1])
    states = width // 4
    orders_here = functions.shape[2]
    values = jnp.einsum("nCm,nmj->nCj", framed, functions, preferred_element_type=jnp.float32)
    values = values.reshape(root_degrees, 2, 2, states, orders_here)
    order_values = (jnp.arange(orders_here, dtype=jnp.int32) - half_orders).astype(jnp.float32)
    cosine = jnp.cos(order_values * azimuth)
    sine = jnp.sin(order_values * azimuth)
    real_part = cosine * values[:, :, 0] + sine * values[:, :, 1]
    imag_part = cosine * values[:, :, 1] - sine * values[:, :, 0]
    joined = jnp.stack([real_part, imag_part], axis=2)
    return jnp.transpose(joined, (4, 1, 2, 3, 0)).reshape(orders_here, 4 * states * root_degrees)


def legendre_field(root_coef, table):
    orders_here, root_degrees = (table.shape[0], table.shape[1])
    lat_total = table.shape[2] // 2
    rows = root_coef.shape[1] // root_degrees
    states = rows // 4
    half = rows // 2
    blocks = jnp.einsum(
        "jrn,jnK->jrK",
        root_coef.reshape(orders_here, rows, root_degrees),
        table,
        preferred_element_type=jnp.float32,
    )
    theta_part = blocks[:, :half, :lat_total] + blocks[:, half:, lat_total:]
    cross = blocks[:, :half, lat_total:] + blocks[:, half:, :lat_total]
    phi_part = jnp.concatenate([-cross[:, states:], cross[:, :states]], axis=1)
    return jnp.concatenate([theta_part, phi_part], axis=1)


def synthesize(spectrum, longitudes):
    orders = spectrum.shape[-1]
    fine = 128
    coarse = longitudes // fine
    order_ids = jnp.arange(orders, dtype=jnp.int32) - orders // 2
    coarse_angle = jnp.mod(order_ids[:, None] * (fine * jnp.arange(coarse, dtype=jnp.int32))[None, :], longitudes)
    coarse_angle = coarse_angle.astype(jnp.float32) * (2.0 * math.pi / longitudes)
    fine_angle = jnp.mod(order_ids[:, None] * jnp.arange(fine, dtype=jnp.int32)[None, :], longitudes)
    fine_angle = fine_angle.astype(jnp.float32) * (2.0 * math.pi / longitudes)
    pc, ps = jnp.cos(coarse_angle), jnp.sin(coarse_angle)
    qc, qs = jnp.cos(fine_angle), jnp.sin(fine_angle)
    spec = spectrum.astype(jnp.float32)
    sr, si = spec[:, 0], spec[:, 1]
    vr = sr[..., None, :] * pc.T - si[..., None, :] * ps.T
    vi = sr[..., None, :] * ps.T + si[..., None, :] * pc.T
    lhs = jnp.stack([vr, vi], axis=-2)
    rhs = jnp.stack([jnp.stack([qc, qs], axis=1), jnp.stack([-qs, qc], axis=1)], axis=0)
    out = jnp.einsum("csxkam,amfb->xscfkb", lhs, rhs, precision=HI)
    out = out.reshape(out.shape[:4] + (longitudes,))
    return out * (1.0 / math.sqrt(orders))


def pair_sum(x, axis):
    if lax.axis_size(axis) != 2:
        return lax.psum(x, axis)
    return x + lax.ppermute(x, axis, [(0, 1), (1, 0)])


def pair_scatter(x, axis):
    me = lax.axis_index(axis)
    keep = jnp.where(me == 0, x[0], x[1])
    give = jnp.where(me == 0, x[1], x[0])
    got = lax.ppermute(give.astype(jnp.bfloat16), axis, [(0, 1), (1, 0)])
    return keep + got.astype(keep.dtype)


def shift_all_to_all(x, axis):
    n = lax.axis_size(axis)
    me = lax.axis_index(axis)
    rows = jnp.arange(n)
    result = jnp.zeros_like(x)
    for step in range(n):
        target = (me + step) % n
        piece = jnp.take(x, target, axis=0)
        if step:
            piece = lax.ppermute(piece, axis, [(i, (i + step) % n) for i in range(n)])
        source = (me - step) % n
        result = jnp.where((rows == source).reshape((n,) + (1,) * (x.ndim - 1)), piece[None], result)
    return result


def on_device(
    sphere_coef,
    live_blocks,
    cluster,
    leaf_parent,
    leaf_octant,
    box_octant,
    rotation,
    axial_one,
    axial_two,
    owner_rotation,
    owner_axial,
    owner_angle,
    turn_table,
    angular_table,
):
    partial_owner = local_boxes(
        sphere_coef,
        live_blocks[0],
        cluster,
        leaf_parent,
        leaf_octant,
        box_octant,
        rotation,
        axial_one,
        axial_two,
    )
    owner_sum = pair_sum(pair_sum(partial_owner, "sub"), "state")
    framed = owner_frame(owner_sum, owner_rotation[0], owner_axial[0])
    leaf_size = lax.axis_size("leaf")
    orders = turn_table.shape[3]
    half_orders = orders // 2
    own_orders = orders // leaf_size
    own_azimuth = owner_angle[lax.axis_index("leaf")]
    piece = turn_table[0]
    root = lax.psum_scatter(
        rotate_back(framed, piece, own_azimuth, half_orders),
        "leaf",
        scatter_dimension=0,
        tiled=True,
    )
    root_coef = root.astype(jnp.bfloat16)
    field = legendre_field(root_coef, angular_table)
    channel = field.shape[1]
    group_size = lax.axis_size("state") * lax.axis_size("sub")
    lat_rows = field.shape[2] // (leaf_size * group_size)
    shaped = field.reshape(own_orders, channel, leaf_size, group_size, lat_rows)
    shaped = jnp.transpose(shaped, (3, 2, 1, 4, 0)).reshape(
        group_size, leaf_size, channel * lat_rows * own_orders
    )
    if lax.axis_size("state") == 2 and lax.axis_size("sub") == 2 and leaf_size <= 4:
        halves = shaped.reshape((2, 2) + shaped.shape[1:])
        summed = pair_scatter(pair_scatter(jnp.swapaxes(halves, 0, 1), "sub"), "state")
        moved = shift_all_to_all(summed.astype(jnp.bfloat16), "leaf")
    else:
        summed = lax.psum_scatter(shaped.astype(jnp.bfloat16), ("state", "sub"), scatter_dimension=0, tiled=True)
        moved = lax.all_to_all(summed, "leaf", split_axis=1, concat_axis=2, tiled=True)
    spectrum = moved.reshape(leaf_size, channel, lat_rows, own_orders)
    spectrum = jnp.transpose(spectrum, (1, 2, 0, 3)).reshape(2, 2, -1, lat_rows, orders)
    return synthesize(spectrum, PHI)


def solution(mesh):
    return jax.shard_map(
        on_device,
        mesh=mesh,
        in_specs=(
            P(None, None, None, None, None, ("groups", "leaf", "state", "sub")),
            P(("groups", "leaf", "state", "sub")),
            P(("groups", "leaf", "state", "sub")),
            P(("groups", "leaf", "state", "sub")),
            P(("groups", "leaf", "state", "sub")),
            P(("groups", "leaf", "state", "sub")),
            P(),
            P(),
            P(),
            P(("groups", "leaf"), None, None, None, None),
            P(("groups", "leaf"), None, None, None, ("state", "sub"), None, None),
            P("groups"),
            P(("groups", "leaf"), ("state", "sub"), None, None),
            P("leaf", ("state", "sub"), None),
        ),
        out_specs=P(("groups", "leaf", "state", "sub"), None, None, None, None),
        check_vma=False,
    )
```

```python
import math

import jax
import jax.numpy as jnp
from jax import lax
from jax.sharding import PartitionSpec as P

STATES = 4
SBLK = 4
PHI = 2048
HI = lax.Precision.HIGHEST


def complex_join(first, second, half):
    real = first[..., :half] - second[..., half:]
    imag = first[..., half:] + second[..., :half]
    return jnp.concatenate([real, imag], axis=-1)


def turn_select(vectors, rotation, octants, backward):
    degrees, orders, width = vectors.shape
    if backward:
        mats = jnp.transpose(rotation, (1, 2, 0, 4, 3))
        sign = -1.0
    else:
        mats = jnp.transpose(rotation, (1, 2, 0, 3, 4))
        sign = 1.0
    mats = mats.reshape(2, degrees, 8 * orders, orders)
    first = jnp.einsum("lQp,lpC->lQC", mats[0], vectors, precision=lax.Precision.HIGHEST)
    second = sign * jnp.einsum("lQp,lpC->lQC", mats[1], vectors, precision=lax.Precision.HIGHEST)
    joined = complex_join(first, second, width // 2).reshape(degrees, 8, orders, width)
    count = octants.shape[0]
    chosen = (octants[None, :] == jnp.arange(8, dtype=jnp.int32)[:, None]).astype(jnp.float32)
    column_mask = jnp.tile(chosen, (1, width // count))
    return jnp.sum(joined * column_mask[None, :, None, :], axis=1)


def axial_apply(vectors, axial):
    degrees, orders, width = vectors.shape
    rest = width // 4
    moved = vectors.reshape(degrees, orders, 2, 2, rest)
    moved = jnp.transpose(moved, (1, 3, 0, 2, 4)).reshape(orders, 2 * degrees, 2 * rest)
    mats = axial.reshape(2, orders, 2 * degrees, 2 * degrees)
    first = jnp.einsum("qab,qbC->qaC", mats[0], moved, precision=lax.Precision.HIGHEST)
    second = jnp.einsum("qab,qbC->qaC", mats[1], moved, precision=lax.Precision.HIGHEST)
    joined = complex_join(first, second, rest).reshape(orders, 2, degrees, 2, rest)
    return jnp.transpose(joined, (2, 0, 3, 1, 4)).reshape(degrees, orders, width)


def move_expansion(vectors, octants, rotation, axial):
    turned = turn_select(vectors, rotation, octants, False)
    return turn_select(axial_apply(turned, axial), rotation, octants, True)


def local_boxes(
    sphere_block,
    live_count,
    cluster,
    leaf_parent,
    leaf_octant,
    box_octant,
    rotation,
    axial_one,
    axial_two,
):
    degrees, orders = (sphere_block.shape[0], sphere_block.shape[1])
    channel = sphere_block.shape[2] * sphere_block.shape[3] * sphere_block.shape[4]
    slots = sphere_block.shape[-1]
    per_block = slots // SBLK
    alive = jnp.arange(slots, dtype=jnp.int32) // per_block < live_count
    leaf_total = leaf_parent.shape[0]
    member = (
        (cluster[:, None] == jnp.arange(leaf_total, dtype=jnp.int32)[None, :]) & alive[:, None]
    ).astype(jnp.bfloat16)
    ident = jnp.eye(channel, dtype=jnp.bfloat16)
    spread = (ident[:, None, :, None] * member[None, :, None, :]).reshape(
        channel * slots, channel * leaf_total
    )
    leaves = jnp.dot(
        sphere_block.reshape(degrees * orders, channel * slots),
        spread,
        preferred_element_type=jnp.float32,
    ).reshape(degrees, orders, channel * leaf_total)
    moved = move_expansion(leaves, leaf_octant, rotation, axial_one)
    box_total = box_octant.shape[0]
    parents = (leaf_parent[:, None] == jnp.arange(box_total, dtype=jnp.int32)[None, :]).astype(
        jnp.float32
    )
    wide_ident = jnp.eye(channel, dtype=jnp.float32)
    wide_parents = (wide_ident[:, None, :, None] * parents[None, :, None, :]).reshape(
        channel * leaf_total, channel * box_total
    )
    boxes = jnp.einsum("lpC,CD->lpD", moved, wide_parents, precision=lax.Precision.HIGHEST)
    outer = move_expansion(boxes, box_octant, rotation, axial_two)
    return outer.reshape(degrees, orders, channel, box_total).sum(-1)


def owner_frame(owner_sum, owner_turn, owner_shift):
    degrees, orders, width = owner_sum.shape
    states = width // 4
    first = jnp.einsum("lqp,lpC->lqC", owner_turn[0], owner_sum, precision=lax.Precision.HIGHEST)
    second = jnp.einsum("lqp,lpC->lqC", owner_turn[1], owner_sum, precision=lax.Precision.HIGHEST)
    turned = complex_join(first, second, width // 2)
    moved = turned.reshape(degrees, orders, 2, 2, states)
    moved = jnp.transpose(moved, (1, 3, 0, 2, 4)).reshape(orders, 2 * degrees, 2 * states)
    root_degrees = owner_shift.shape[3]
    mats = owner_shift.reshape(2, orders, 2 * root_degrees, 2 * degrees)
    first = jnp.einsum("qab,qbC->qaC", mats[0], moved, precision=lax.Precision.HIGHEST)
    second = jnp.einsum("qab,qbC->qaC", mats[1], moved, precision=lax.Precision.HIGHEST)
    joined = complex_join(first, second, states).reshape(orders, 2, root_degrees, 2, states)
    framed = jnp.transpose(joined, (2, 1, 3, 4, 0)).reshape(root_degrees, 4 * states, orders)
    return framed.astype(jnp.bfloat16)


def rotate_back(framed, functions, azimuth, half_orders):
    root_degrees, width = (framed.shape[0], framed.shape[1])
    states = width // 4
    orders_here = functions.shape[2]
    values = jnp.einsum("nCm,nmj->nCj", framed, functions, preferred_element_type=jnp.float32)
    values = values.reshape(root_degrees, 2, 2, states, orders_here)
    order_values = (jnp.arange(orders_here, dtype=jnp.int32) - half_orders).astype(jnp.float32)
    cosine = jnp.cos(order_values * azimuth)
    sine = jnp.sin(order_values * azimuth)
    real_part = cosine * values[:, :, 0] + sine * values[:, :, 1]
    imag_part = cosine * values[:, :, 1] - sine * values[:, :, 0]
    joined = jnp.stack([real_part, imag_part], axis=2)
    return jnp.transpose(joined, (4, 1, 2, 3, 0)).reshape(orders_here, 4 * states * root_degrees)


def legendre_field(root_coef, table):
    orders_here, root_degrees = (table.shape[0], table.shape[1])
    lat_total = table.shape[2] // 2
    rows = root_coef.shape[1] // root_degrees
    states = rows // 4
    half = rows // 2
    blocks = jnp.einsum(
        "jrn,jnK->jrK",
        root_coef.reshape(orders_here, rows, root_degrees),
        table,
        preferred_element_type=jnp.float32,
    )
    theta_part = blocks[:, :half, :lat_total] + blocks[:, half:, lat_total:]
    cross = blocks[:, :half, lat_total:] + blocks[:, half:, :lat_total]
    phi_part = jnp.concatenate([-cross[:, states:], cross[:, :states]], axis=1)
    return jnp.concatenate([theta_part, phi_part], axis=1)


def synthesize(spectrum, longitudes):
    orders = spectrum.shape[-1]
    fine = 128
    coarse = longitudes // fine
    order_ids = jnp.arange(orders, dtype=jnp.int32) - orders // 2
    coarse_angle = jnp.mod(order_ids[:, None] * (fine * jnp.arange(coarse, dtype=jnp.int32))[None, :], longitudes)
    coarse_angle = coarse_angle.astype(jnp.float32) * (2.0 * math.pi / longitudes)
    fine_angle = jnp.mod(order_ids[:, None] * jnp.arange(fine, dtype=jnp.int32)[None, :], longitudes)
    fine_angle = fine_angle.astype(jnp.float32) * (2.0 * math.pi / longitudes)
    pc, ps = jnp.cos(coarse_angle), jnp.sin(coarse_angle)
    qc, qs = jnp.cos(fine_angle), jnp.sin(fine_angle)
    spec = spectrum.astype(jnp.float32)
    sr, si = spec[:, 0], spec[:, 1]
    vr = sr[..., None, :] * pc.T - si[..., None, :] * ps.T
    vi = sr[..., None, :] * ps.T + si[..., None, :] * pc.T
    lhs = jnp.stack([vr, vi], axis=-2)
    rhs = jnp.stack([jnp.stack([qc, qs], axis=1), jnp.stack([-qs, qc], axis=1)], axis=0)
    out = jnp.einsum("csxkam,amfb->xscfkb", lhs, rhs, precision=HI)
    out = out.reshape(out.shape[:4] + (longitudes,))
    return out * (1.0 / math.sqrt(orders))


def pair_sum(x, axis):
    if lax.axis_size(axis) != 2:
        return lax.psum(x, axis)
    return x + lax.ppermute(x, axis, [(0, 1), (1, 0)])


def pair_scatter(x, axis):
    me = lax.axis_index(axis)
    keep = jnp.where(me == 0, x[0], x[1])
    give = jnp.where(me == 0, x[1], x[0])
    got = lax.ppermute(give.astype(jnp.bfloat16), axis, [(0, 1), (1, 0)])
    return keep + got.astype(keep.dtype)


def shift_all_to_all(x, axis):
    n = lax.axis_size(axis)
    me = lax.axis_index(axis)
    rows = jnp.arange(n)
    result = jnp.zeros_like(x)
    for step in range(n):
        target = (me + step) % n
        piece = jnp.take(x, target, axis=0)
        if step:
            piece = lax.ppermute(piece, axis, [(i, (i + step) % n) for i in range(n)])
        source = (me - step) % n
        result = jnp.where((rows == source).reshape((n,) + (1,) * (x.ndim - 1)), piece[None], result)
    return result


def shift_reduce_scatter(x, axis):
    n = lax.axis_size(axis)
    me = lax.axis_index(axis)
    total = jnp.take(x, me, axis=0)
    for step in range(1, n):
        piece = jnp.take(x, (me + step) % n, axis=0).astype(jnp.bfloat16)
        piece = lax.ppermute(piece, axis, [(i, (i + step) % n) for i in range(n)])
        total = total + piece.astype(total.dtype)
    return total


def on_device(
    sphere_coef,
    live_blocks,
    cluster,
    leaf_parent,
    leaf_octant,
    box_octant,
    rotation,
    axial_one,
    axial_two,
    owner_rotation,
    owner_axial,
    owner_angle,
    turn_table,
    angular_table,
):
    partial_owner = local_boxes(
        sphere_coef,
        live_blocks[0],
        cluster,
        leaf_parent,
        leaf_octant,
        box_octant,
        rotation,
        axial_one,
        axial_two,
    )
    owner_sum = pair_sum(pair_sum(partial_owner, "sub"), "state")
    framed = owner_frame(owner_sum, owner_rotation[0], owner_axial[0])
    leaf_size = lax.axis_size("leaf")
    orders = turn_table.shape[3]
    half_orders = orders // 2
    own_orders = orders // leaf_size
    own_azimuth = owner_angle[lax.axis_index("leaf")]
    piece = turn_table[0]
    contribution = rotate_back(framed, piece, own_azimuth, half_orders)
    if leaf_size <= 4:
        root = shift_reduce_scatter(contribution.reshape((leaf_size, own_orders) + contribution.shape[1:]), "leaf")
    else:
        root = lax.psum_scatter(contribution, "leaf", scatter_dimension=0, tiled=True)
    root_coef = root.astype(jnp.bfloat16)
    field = legendre_field(root_coef, angular_table)
    channel = field.shape[1]
    group_size = lax.axis_size("state") * lax.axis_size("sub")
    lat_rows = field.shape[2] // (leaf_size * group_size)
    shaped = field.reshape(own_orders, channel, leaf_size, group_size, lat_rows)
    shaped = jnp.transpose(shaped, (3, 2, 1, 4, 0)).reshape(
        group_size, leaf_size, channel * lat_rows * own_orders
    )
    if lax.axis_size("state") == 2 and lax.axis_size("sub") == 2 and leaf_size <= 4:
        halves = shaped.reshape((2, 2) + shaped.shape[1:])
        summed = pair_scatter(pair_scatter(jnp.swapaxes(halves, 0, 1), "sub"), "state")
        moved = shift_all_to_all(summed.astype(jnp.bfloat16), "leaf")
    else:
        summed = lax.psum_scatter(shaped.astype(jnp.bfloat16), ("state", "sub"), scatter_dimension=0, tiled=True)
        moved = lax.all_to_all(summed, "leaf", split_axis=1, concat_axis=2, tiled=True)
    spectrum = moved.reshape(leaf_size, channel, lat_rows, own_orders)
    spectrum = jnp.transpose(spectrum, (1, 2, 0, 3)).reshape(2, 2, -1, lat_rows, orders)
    return synthesize(spectrum, PHI)


def solution(mesh):
    return jax.shard_map(
        on_device,
        mesh=mesh,
        in_specs=(
            P(None, None, None, None, None, ("groups", "leaf", "state", "sub")),
            P(("groups", "leaf", "state", "sub")),
            P(("groups", "leaf", "state", "sub")),
            P(("groups", "leaf", "state", "sub")),
            P(("groups", "leaf", "state", "sub")),
            P(("groups", "leaf", "state", "sub")),
            P(),
            P(),
            P(),
            P(("groups", "leaf"), None, None, None, None),
            P(("groups", "leaf"), None, None, None, ("state", "sub"), None, None),
            P("groups"),
            P(("groups", "leaf"), ("state", "sub"), None, None),
            P("leaf", ("state", "sub"), None),
        ),
        out_specs=P(("groups", "leaf", "state", "sub"), None, None, None, None),
        check_vma=False,
    )
```

```python
import math

import jax
import jax.numpy as jnp
from jax import lax
from jax.sharding import PartitionSpec as P

STATES = 4
SBLK = 4
PHI = 2048
HI = lax.Precision.HIGHEST
TABLE_BYTES = 8 << 20


def complex_join(first, second, half):
    real = first[..., :half] - second[..., half:]
    imag = first[..., half:] + second[..., :half]
    return jnp.concatenate([real, imag], axis=-1)


def turn_select(vectors, rotation, octants, backward):
    degrees, orders, width = vectors.shape
    if backward:
        mats = jnp.transpose(rotation, (1, 2, 0, 4, 3))
        sign = -1.0
    else:
        mats = jnp.transpose(rotation, (1, 2, 0, 3, 4))
        sign = 1.0
    mats = mats.reshape(2, degrees, 8 * orders, orders)
    first = jnp.einsum("lQp,lpC->lQC", mats[0], vectors, precision=lax.Precision.HIGHEST)
    second = sign * jnp.einsum("lQp,lpC->lQC", mats[1], vectors, precision=lax.Precision.HIGHEST)
    joined = complex_join(first, second, width // 2).reshape(degrees, 8, orders, width)
    count = octants.shape[0]
    chosen = (octants[None, :] == jnp.arange(8, dtype=jnp.int32)[:, None]).astype(jnp.float32)
    column_mask = jnp.tile(chosen, (1, width // count))
    return jnp.sum(joined * column_mask[None, :, None, :], axis=1)


def axial_apply(vectors, axial):
    degrees, orders, width = vectors.shape
    rest = width // 4
    moved = vectors.reshape(degrees, orders, 2, 2, rest)
    moved = jnp.transpose(moved, (1, 3, 0, 2, 4)).reshape(orders, 2 * degrees, 2 * rest)
    mats = axial.reshape(2, orders, 2 * degrees, 2 * degrees)
    first = jnp.einsum("qab,qbC->qaC", mats[0], moved, precision=lax.Precision.HIGHEST)
    second = jnp.einsum("qab,qbC->qaC", mats[1], moved, precision=lax.Precision.HIGHEST)
    joined = complex_join(first, second, rest).reshape(orders, 2, degrees, 2, rest)
    return jnp.transpose(joined, (2, 0, 3, 1, 4)).reshape(degrees, orders, width)


def move_expansion(vectors, octants, rotation, axial):
    turned = turn_select(vectors, rotation, octants, False)
    return turn_select(axial_apply(turned, axial), rotation, octants, True)


def local_boxes(
    sphere_block,
    live_count,
    cluster,
    leaf_parent,
    leaf_octant,
    box_octant,
    rotation,
    axial_one,
    axial_two,
):
    degrees, orders = (sphere_block.shape[0], sphere_block.shape[1])
    channel = sphere_block.shape[2] * sphere_block.shape[3] * sphere_block.shape[4]
    slots = sphere_block.shape[-1]
    per_block = slots // SBLK
    alive = jnp.arange(slots, dtype=jnp.int32) // per_block < live_count
    leaf_total = leaf_parent.shape[0]
    member = (
        (cluster[:, None] == jnp.arange(leaf_total, dtype=jnp.int32)[None, :]) & alive[:, None]
    ).astype(jnp.bfloat16)
    ident = jnp.eye(channel, dtype=jnp.bfloat16)
    spread = (ident[:, None, :, None] * member[None, :, None, :]).reshape(
        channel * slots, channel * leaf_total
    )
    leaves = jnp.dot(
        sphere_block.reshape(degrees * orders, channel * slots),
        spread,
        preferred_element_type=jnp.float32,
    ).reshape(degrees, orders, channel * leaf_total)
    moved = move_expansion(leaves, leaf_octant, rotation, axial_one)
    box_total = box_octant.shape[0]
    parents = (leaf_parent[:, None] == jnp.arange(box_total, dtype=jnp.int32)[None, :]).astype(
        jnp.float32
    )
    wide_ident = jnp.eye(channel, dtype=jnp.float32)
    wide_parents = (wide_ident[:, None, :, None] * parents[None, :, None, :]).reshape(
        channel * leaf_total, channel * box_total
    )
    boxes = jnp.einsum("lpC,CD->lpD", moved, wide_parents, precision=lax.Precision.HIGHEST)
    outer = move_expansion(boxes, box_octant, rotation, axial_two)
    return outer.reshape(degrees, orders, channel, box_total).sum(-1)


def owner_frame(owner_sum, owner_turn, owner_shift):
    degrees, orders, width = owner_sum.shape
    states = width // 4
    first = jnp.einsum("lqp,lpC->lqC", owner_turn[0], owner_sum, precision=lax.Precision.HIGHEST)
    second = jnp.einsum("lqp,lpC->lqC", owner_turn[1], owner_sum, precision=lax.Precision.HIGHEST)
    turned = complex_join(first, second, width // 2)
    moved = turned.reshape(degrees, orders, 2, 2, states)
    moved = jnp.transpose(moved, (1, 3, 0, 2, 4)).reshape(orders, 2 * degrees, 2 * states)
    root_degrees = owner_shift.shape[3]
    mats = owner_shift.reshape(2, orders, 2 * root_degrees, 2 * degrees)
    first = jnp.einsum("qab,qbC->qaC", mats[0], moved, precision=lax.Precision.HIGHEST)
    second = jnp.einsum("qab,qbC->qaC", mats[1], moved, precision=lax.Precision.HIGHEST)
    joined = complex_join(first, second, states).reshape(orders, 2, root_degrees, 2, states)
    framed = jnp.transpose(joined, (2, 1, 3, 4, 0)).reshape(root_degrees, 4 * states, orders)
    return framed.astype(jnp.bfloat16)


def rotate_back(framed, functions, azimuth, half_orders):
    root_degrees, width = (framed.shape[0], framed.shape[1])
    states = width // 4
    orders_here = functions.shape[2]
    values = jnp.einsum("nCm,nmj->nCj", framed, functions, preferred_element_type=jnp.float32)
    values = values.reshape(root_degrees, 2, 2, states, orders_here)
    order_values = (jnp.arange(orders_here, dtype=jnp.int32) - half_orders).astype(jnp.float32)
    cosine = jnp.cos(order_values * azimuth)
    sine = jnp.sin(order_values * azimuth)
    real_part = cosine * values[:, :, 0] + sine * values[:, :, 1]
    imag_part = cosine * values[:, :, 1] - sine * values[:, :, 0]
    joined = jnp.stack([real_part, imag_part], axis=2)
    return jnp.transpose(joined, (4, 1, 2, 3, 0)).reshape(orders_here, 4 * states * root_degrees)


def legendre_field(root_coef, table):
    orders_here, root_degrees = (table.shape[0], table.shape[1])
    lat_total = table.shape[2] // 2
    rows = root_coef.shape[1] // root_degrees
    states = rows // 4
    half = rows // 2
    blocks = jnp.einsum(
        "jrn,jnK->jrK",
        root_coef.reshape(orders_here, rows, root_degrees),
        table,
        preferred_element_type=jnp.float32,
    )
    theta_part = blocks[:, :half, :lat_total] + blocks[:, half:, lat_total:]
    cross = blocks[:, :half, lat_total:] + blocks[:, half:, :lat_total]
    phi_part = jnp.concatenate([-cross[:, states:], cross[:, :states]], axis=1)
    return jnp.concatenate([theta_part, phi_part], axis=1)


def synthesize(spectrum, longitudes):
    orders = spectrum.shape[-1]
    fine = 128
    coarse = longitudes // fine
    order_ids = jnp.arange(orders, dtype=jnp.int32) - orders // 2
    coarse_angle = jnp.mod(order_ids[:, None] * (fine * jnp.arange(coarse, dtype=jnp.int32))[None, :], longitudes)
    coarse_angle = coarse_angle.astype(jnp.float32) * (2.0 * math.pi / longitudes)
    fine_angle = jnp.mod(order_ids[:, None] * jnp.arange(fine, dtype=jnp.int32)[None, :], longitudes)
    fine_angle = fine_angle.astype(jnp.float32) * (2.0 * math.pi / longitudes)
    pc, ps = jnp.cos(coarse_angle), jnp.sin(coarse_angle)
    qc, qs = jnp.cos(fine_angle), jnp.sin(fine_angle)
    spec = spectrum.astype(jnp.float32)
    sr, si = spec[:, 0], spec[:, 1]
    vr = sr[..., None, :] * pc.T - si[..., None, :] * ps.T
    vi = sr[..., None, :] * ps.T + si[..., None, :] * pc.T
    lhs = jnp.stack([vr, vi], axis=-2)
    rhs = jnp.stack([jnp.stack([qc, qs], axis=1), jnp.stack([-qs, qc], axis=1)], axis=0)
    out = jnp.einsum("csxkam,amfb->xscfkb", lhs, rhs, precision=HI)
    out = out.reshape(out.shape[:4] + (longitudes,))
    return out * (1.0 / math.sqrt(orders))


def pair_sum(x, axis):
    if lax.axis_size(axis) != 2:
        return lax.psum(x, axis)
    return x + lax.ppermute(x, axis, [(0, 1), (1, 0)])


def pair_scatter(x, axis):
    me = lax.axis_index(axis)
    keep = jnp.where(me == 0, x[0], x[1])
    give = jnp.where(me == 0, x[1], x[0])
    got = lax.ppermute(give.astype(jnp.bfloat16), axis, [(0, 1), (1, 0)])
    return keep + got.astype(keep.dtype)


def shift_all_to_all(x, axis):
    n = lax.axis_size(axis)
    me = lax.axis_index(axis)
    rows = jnp.arange(n)
    result = jnp.zeros_like(x)
    for step in range(n):
        target = (me + step) % n
        piece = jnp.take(x, target, axis=0)
        if step:
            piece = lax.ppermute(piece, axis, [(i, (i + step) % n) for i in range(n)])
        source = (me - step) % n
        result = jnp.where((rows == source).reshape((n,) + (1,) * (x.ndim - 1)), piece[None], result)
    return result


def shift_reduce_scatter(x, axis):
    n = lax.axis_size(axis)
    me = lax.axis_index(axis)
    total = jnp.take(x, me, axis=0)
    for step in range(1, n):
        piece = jnp.take(x, (me + step) % n, axis=0).astype(jnp.bfloat16)
        piece = lax.ppermute(piece, axis, [(i, (i + step) % n) for i in range(n)])
        total = total + piece.astype(total.dtype)
    return total


def shift_all_gather(x, axis):
    n = lax.axis_size(axis)
    me = lax.axis_index(axis)
    rows = jnp.arange(n).reshape((n,) + (1,) * x.ndim)
    result = jnp.zeros((n,) + x.shape, x.dtype)
    for step in range(n):
        piece = x if step == 0 else lax.ppermute(x, axis, [(i, (i + step) % n) for i in range(n)])
        result = jnp.where(rows == (me - step) % n, piece[None], result)
    return result


def on_device(
    sphere_coef,
    live_blocks,
    cluster,
    leaf_parent,
    leaf_octant,
    box_octant,
    rotation,
    axial_one,
    axial_two,
    owner_rotation,
    owner_axial,
    owner_angle,
    turn_table,
    angular_table,
):
    partial_owner = local_boxes(
        sphere_coef,
        live_blocks[0],
        cluster,
        leaf_parent,
        leaf_octant,
        box_octant,
        rotation,
        axial_one,
        axial_two,
    )
    leaf_size = lax.axis_size("leaf")
    pairs = lax.axis_size("state") == 2 and lax.axis_size("sub") == 2 and leaf_size <= 4
    spread = pairs and angular_table.size * leaf_size * 4 <= TABLE_BYTES
    if spread:
        full_table = shift_all_gather(angular_table, "leaf")
        full_table = full_table.reshape((-1,) + angular_table.shape[1:]).astype(jnp.float32)
    owner_sum = pair_sum(pair_sum(partial_owner, "sub"), "state")
    framed = owner_frame(owner_sum, owner_rotation[0], owner_axial[0])
    if spread:
        orders = turn_table.shape[3]
        contribution = rotate_back(framed, turn_table[0], owner_angle[lax.axis_index("leaf")], orders // 2)
        field = legendre_field(contribution, full_table)
        channel = field.shape[1]
        lat_rows = field.shape[2] // (leaf_size * 4)
        shaped = field.reshape(orders, channel, leaf_size, 4, lat_rows)
        shaped = jnp.transpose(shaped, (2, 3, 1, 4, 0)).reshape(leaf_size, 2, 2, channel * lat_rows * orders)
        summed = shift_reduce_scatter(shaped, "leaf")
        summed = pair_scatter(pair_scatter(jnp.swapaxes(summed, 0, 1), "sub"), "state")
        spectrum = summed.astype(jnp.bfloat16).reshape(2, 2, -1, lat_rows, orders)
        return synthesize(spectrum, PHI)
    leaf_size = lax.axis_size("leaf")
    orders = turn_table.shape[3]
    half_orders = orders // 2
    own_orders = orders // leaf_size
    own_azimuth = owner_angle[lax.axis_index("leaf")]
    piece = turn_table[0]
    contribution = rotate_back(framed, piece, own_azimuth, half_orders)
    if leaf_size <= 4:
        root = shift_reduce_scatter(contribution.reshape((leaf_size, own_orders) + contribution.shape[1:]), "leaf")
    else:
        root = lax.psum_scatter(contribution, "leaf", scatter_dimension=0, tiled=True)
    root_coef = root.astype(jnp.bfloat16)
    field = legendre_field(root_coef, angular_table)
    channel = field.shape[1]
    group_size = lax.axis_size("state") * lax.axis_size("sub")
    lat_rows = field.shape[2] // (leaf_size * group_size)
    shaped = field.reshape(own_orders, channel, leaf_size, group_size, lat_rows)
    shaped = jnp.transpose(shaped, (3, 2, 1, 4, 0)).reshape(
        group_size, leaf_size, channel * lat_rows * own_orders
    )
    if lax.axis_size("state") == 2 and lax.axis_size("sub") == 2 and leaf_size <= 4:
        halves = shaped.reshape((2, 2) + shaped.shape[1:])
        summed = pair_scatter(pair_scatter(jnp.swapaxes(halves, 0, 1), "sub"), "state")
        moved = shift_all_to_all(summed.astype(jnp.bfloat16), "leaf")
    else:
        summed = lax.psum_scatter(shaped.astype(jnp.bfloat16), ("state", "sub"), scatter_dimension=0, tiled=True)
        moved = lax.all_to_all(summed, "leaf", split_axis=1, concat_axis=2, tiled=True)
    spectrum = moved.reshape(leaf_size, channel, lat_rows, own_orders)
    spectrum = jnp.transpose(spectrum, (1, 2, 0, 3)).reshape(2, 2, -1, lat_rows, orders)
    return synthesize(spectrum, PHI)


def solution(mesh):
    return jax.shard_map(
        on_device,
        mesh=mesh,
        in_specs=(
            P(None, None, None, None, None, ("groups", "leaf", "state", "sub")),
            P(("groups", "leaf", "state", "sub")),
            P(("groups", "leaf", "state", "sub")),
            P(("groups", "leaf", "state", "sub")),
            P(("groups", "leaf", "state", "sub")),
            P(("groups", "leaf", "state", "sub")),
            P(),
            P(),
            P(),
            P(("groups", "leaf"), None, None, None, None),
            P(("groups", "leaf"), None, None, None, ("state", "sub"), None, None),
            P("groups"),
            P(("groups", "leaf"), ("state", "sub"), None, None),
            P("leaf", ("state", "sub"), None),
        ),
        out_specs=P(("groups", "leaf", "state", "sub"), None, None, None, None),
        check_vma=False,
    )
```

```python
import math

import jax
import jax.numpy as jnp
from jax import lax
from jax.sharding import PartitionSpec as P

STATES = 4
SBLK = 4
PHI = 2048
HI = lax.Precision.HIGH


def complex_join(first, second, half):
    real = first[..., :half] - second[..., half:]
    imag = first[..., half:] + second[..., :half]
    return jnp.concatenate([real, imag], axis=-1)


def turn_select(vectors, rotation, octants, backward):
    degrees, orders, width = vectors.shape
    if backward:
        mats = jnp.transpose(rotation, (1, 2, 0, 4, 3))
        sign = -1.0
    else:
        mats = jnp.transpose(rotation, (1, 2, 0, 3, 4))
        sign = 1.0
    mats = mats.reshape(2, degrees, 8 * orders, orders)
    first = jnp.einsum("lQp,lpC->lQC", mats[0], vectors, precision=HI)
    second = sign * jnp.einsum("lQp,lpC->lQC", mats[1], vectors, precision=HI)
    joined = complex_join(first, second, width // 2).reshape(degrees, 8, orders, width)
    count = octants.shape[0]
    chosen = (octants[None, :] == jnp.arange(8, dtype=jnp.int32)[:, None]).astype(jnp.float32)
    column_mask = jnp.tile(chosen, (1, width // count))
    return jnp.sum(joined * column_mask[None, :, None, :], axis=1)


def axial_apply(vectors, axial):
    degrees, orders, width = vectors.shape
    rest = width // 4
    moved = vectors.reshape(degrees, orders, 2, 2, rest)
    moved = jnp.transpose(moved, (1, 3, 0, 2, 4)).reshape(orders, 2 * degrees, 2 * rest)
    mats = axial.reshape(2, orders, 2 * degrees, 2 * degrees)
    first = jnp.einsum("qab,qbC->qaC", mats[0], moved, precision=HI)
    second = jnp.einsum("qab,qbC->qaC", mats[1], moved, precision=HI)
    joined = complex_join(first, second, rest).reshape(orders, 2, degrees, 2, rest)
    return jnp.transpose(joined, (2, 0, 3, 1, 4)).reshape(degrees, orders, width)


def move_expansion(vectors, octants, rotation, axial):
    turned = turn_select(vectors, rotation, octants, False)
    return turn_select(axial_apply(turned, axial), rotation, octants, True)


def local_boxes(
    sphere_block,
    live_count,
    cluster,
    leaf_parent,
    leaf_octant,
    box_octant,
    rotation,
    axial_one,
    axial_two,
):
    degrees, orders = (sphere_block.shape[0], sphere_block.shape[1])
    channel = sphere_block.shape[2] * sphere_block.shape[3] * sphere_block.shape[4]
    slots = sphere_block.shape[-1]
    per_block = slots // SBLK
    alive = jnp.arange(slots, dtype=jnp.int32) // per_block < live_count
    leaf_total = leaf_parent.shape[0]
    member = (
        (cluster[:, None] == jnp.arange(leaf_total, dtype=jnp.int32)[None, :]) & alive[:, None]
    ).astype(jnp.bfloat16)
    ident = jnp.eye(channel, dtype=jnp.bfloat16)
    spread = (ident[:, None, :, None] * member[None, :, None, :]).reshape(
        channel * slots, channel * leaf_total
    )
    leaves = jnp.dot(
        sphere_block.reshape(degrees * orders, channel * slots),
        spread,
        preferred_element_type=jnp.float32,
    ).reshape(degrees, orders, channel * leaf_total)
    moved = move_expansion(leaves, leaf_octant, rotation, axial_one)
    box_total = box_octant.shape[0]
    parents = (leaf_parent[:, None] == jnp.arange(box_total, dtype=jnp.int32)[None, :]).astype(
        jnp.float32
    )
    wide_ident = jnp.eye(channel, dtype=jnp.float32)
    wide_parents = (wide_ident[:, None, :, None] * parents[None, :, None, :]).reshape(
        channel * leaf_total, channel * box_total
    )
    boxes = jnp.einsum("lpC,CD->lpD", moved, wide_parents, precision=HI)
    outer = move_expansion(boxes, box_octant, rotation, axial_two)
    return outer.reshape(degrees, orders, channel, box_total).sum(-1)


def owner_frame(owner_sum, owner_turn, owner_shift):
    degrees, orders, width = owner_sum.shape
    states = width // 4
    first = jnp.einsum("lqp,lpC->lqC", owner_turn[0], owner_sum, precision=HI)
    second = jnp.einsum("lqp,lpC->lqC", owner_turn[1], owner_sum, precision=HI)
    turned = complex_join(first, second, width // 2)
    moved = turned.reshape(degrees, orders, 2, 2, states)
    moved = jnp.transpose(moved, (1, 3, 0, 2, 4)).reshape(orders, 2 * degrees, 2 * states)
    root_degrees = owner_shift.shape[3]
    mats = owner_shift.reshape(2, orders, 2 * root_degrees, 2 * degrees)
    first = jnp.einsum("qab,qbC->qaC", mats[0], moved, precision=HI)
    second = jnp.einsum("qab,qbC->qaC", mats[1], moved, precision=HI)
    joined = complex_join(first, second, states).reshape(orders, 2, root_degrees, 2, states)
    framed = jnp.transpose(joined, (2, 1, 3, 4, 0)).reshape(root_degrees, 4 * states, orders)
    return framed.astype(jnp.bfloat16)


def rotate_back(framed, functions, azimuth, half_orders):
    root_degrees, width = (framed.shape[0], framed.shape[1])
    states = width // 4
    orders_here = functions.shape[2]
    values = jnp.einsum("nCm,nmj->nCj", framed, functions, preferred_element_type=jnp.float32)
    values = values.reshape(root_degrees, 2, 2, states, orders_here)
    order_values = (jnp.arange(orders_here, dtype=jnp.int32) - half_orders).astype(jnp.float32)
    cosine = jnp.cos(order_values * azimuth)
    sine = jnp.sin(order_values * azimuth)
    real_part = cosine * values[:, :, 0] + sine * values[:, :, 1]
    imag_part = cosine * values[:, :, 1] - sine * values[:, :, 0]
    joined = jnp.stack([real_part, imag_part], axis=2)
    return jnp.transpose(joined, (4, 1, 2, 3, 0)).reshape(orders_here, 4 * states * root_degrees)


def legendre_field(root_coef, table):
    orders_here, root_degrees = (table.shape[0], table.shape[1])
    lat_total = table.shape[2] // 2
    rows = root_coef.shape[1] // root_degrees
    states = rows // 4
    half = rows // 2
    blocks = jnp.einsum(
        "jrn,jnK->jrK",
        root_coef.reshape(orders_here, rows, root_degrees),
        table,
        preferred_element_type=jnp.float32,
    )
    theta_part = blocks[:, :half, :lat_total] + blocks[:, half:, lat_total:]
    cross = blocks[:, :half, lat_total:] + blocks[:, half:, :lat_total]
    phi_part = jnp.concatenate([-cross[:, states:], cross[:, :states]], axis=1)
    return jnp.concatenate([theta_part, phi_part], axis=1)


def synthesize(spectrum, longitudes):
    orders = spectrum.shape[-1]
    fine = 128
    coarse = longitudes // fine
    order_ids = jnp.arange(orders, dtype=jnp.int32) - orders // 2
    coarse_angle = jnp.mod(order_ids[:, None] * (fine * jnp.arange(coarse, dtype=jnp.int32))[None, :], longitudes)
    coarse_angle = coarse_angle.astype(jnp.float32) * (2.0 * math.pi / longitudes)
    fine_angle = jnp.mod(order_ids[:, None] * jnp.arange(fine, dtype=jnp.int32)[None, :], longitudes)
    fine_angle = fine_angle.astype(jnp.float32) * (2.0 * math.pi / longitudes)
    pc, ps = jnp.cos(coarse_angle), jnp.sin(coarse_angle)
    qc, qs = jnp.cos(fine_angle), jnp.sin(fine_angle)
    spec = spectrum.astype(jnp.float32)
    sr, si = spec[:, 0], spec[:, 1]
    vr = sr[..., None, :] * pc.T - si[..., None, :] * ps.T
    vi = sr[..., None, :] * ps.T + si[..., None, :] * pc.T
    lhs = jnp.stack([vr, vi], axis=-2)
    rhs = jnp.stack([jnp.stack([qc, qs], axis=1), jnp.stack([-qs, qc], axis=1)], axis=0)
    out = jnp.einsum("csxkam,amfb->xscfkb", lhs, rhs, precision=HI)
    out = out.reshape(out.shape[:4] + (longitudes,))
    return out * (1.0 / math.sqrt(orders))


def pair_sum(x, axis):
    if lax.axis_size(axis) != 2:
        return lax.psum(x, axis)
    return x + lax.ppermute(x, axis, [(0, 1), (1, 0)])


def pair_scatter(x, axis):
    me = lax.axis_index(axis)
    keep = jnp.where(me == 0, x[0], x[1])
    give = jnp.where(me == 0, x[1], x[0])
    got = lax.ppermute(give.astype(jnp.bfloat16), axis, [(0, 1), (1, 0)])
    return keep + got.astype(keep.dtype)


def shift_all_to_all(x, axis):
    n = lax.axis_size(axis)
    me = lax.axis_index(axis)
    rows = jnp.arange(n)
    result = jnp.zeros_like(x)
    for step in range(n):
        target = (me + step) % n
        piece = jnp.take(x, target, axis=0)
        if step:
            piece = lax.ppermute(piece, axis, [(i, (i + step) % n) for i in range(n)])
        source = (me - step) % n
        result = jnp.where((rows == source).reshape((n,) + (1,) * (x.ndim - 1)), piece[None], result)
    return result


def shift_reduce_scatter(x, axis):
    n = lax.axis_size(axis)
    me = lax.axis_index(axis)
    total = jnp.take(x, me, axis=0)
    for step in range(1, n):
        piece = jnp.take(x, (me + step) % n, axis=0).astype(jnp.bfloat16)
        piece = lax.ppermute(piece, axis, [(i, (i + step) % n) for i in range(n)])
        total = total + piece.astype(total.dtype)
    return total


def on_device(
    sphere_coef,
    live_blocks,
    cluster,
    leaf_parent,
    leaf_octant,
    box_octant,
    rotation,
    axial_one,
    axial_two,
    owner_rotation,
    owner_axial,
    owner_angle,
    turn_table,
    angular_table,
):
    partial_owner = local_boxes(
        sphere_coef,
        live_blocks[0],
        cluster,
        leaf_parent,
        leaf_octant,
        box_octant,
        rotation,
        axial_one,
        axial_two,
    )
    owner_sum = pair_sum(pair_sum(partial_owner, "sub"), "state")
    framed = owner_frame(owner_sum, owner_rotation[0], owner_axial[0])
    leaf_size = lax.axis_size("leaf")
    orders = turn_table.shape[3]
    half_orders = orders // 2
    own_orders = orders // leaf_size
    own_azimuth = owner_angle[lax.axis_index("leaf")]
    piece = turn_table[0]
    contribution = rotate_back(framed, piece, own_azimuth, half_orders)
    if leaf_size <= 4:
        root = shift_reduce_scatter(contribution.reshape((leaf_size, own_orders) + contribution.shape[1:]), "leaf")
    else:
        root = lax.psum_scatter(contribution, "leaf", scatter_dimension=0, tiled=True)
    root_coef = root.astype(jnp.bfloat16)
    field = legendre_field(root_coef, angular_table)
    channel = field.shape[1]
    group_size = lax.axis_size("state") * lax.axis_size("sub")
    lat_rows = field.shape[2] // (leaf_size * group_size)
    shaped = field.reshape(own_orders, channel, leaf_size, group_size, lat_rows)
    shaped = jnp.transpose(shaped, (3, 2, 1, 4, 0)).reshape(
        group_size, leaf_size, channel * lat_rows * own_orders
    )
    if lax.axis_size("state") == 2 and lax.axis_size("sub") == 2 and leaf_size <= 4:
        halves = shaped.reshape((2, 2) + shaped.shape[1:])
        summed = pair_scatter(pair_scatter(jnp.swapaxes(halves, 0, 1), "sub"), "state")
        moved = shift_all_to_all(summed.astype(jnp.bfloat16), "leaf")
    else:
        summed = lax.psum_scatter(shaped.astype(jnp.bfloat16), ("state", "sub"), scatter_dimension=0, tiled=True)
        moved = lax.all_to_all(summed, "leaf", split_axis=1, concat_axis=2, tiled=True)
    spectrum = moved.reshape(leaf_size, channel, lat_rows, own_orders)
    spectrum = jnp.transpose(spectrum, (1, 2, 0, 3)).reshape(2, 2, -1, lat_rows, orders)
    return synthesize(spectrum, PHI)


def solution(mesh):
    return jax.shard_map(
        on_device,
        mesh=mesh,
        in_specs=(
            P(None, None, None, None, None, ("groups", "leaf", "state", "sub")),
            P(("groups", "leaf", "state", "sub")),
            P(("groups", "leaf", "state", "sub")),
            P(("groups", "leaf", "state", "sub")),
            P(("groups", "leaf", "state", "sub")),
            P(("groups", "leaf", "state", "sub")),
            P(),
            P(),
            P(),
            P(("groups", "leaf"), None, None, None, None),
            P(("groups", "leaf"), None, None, None, ("state", "sub"), None, None),
            P("groups"),
            P(("groups", "leaf"), ("state", "sub"), None, None),
            P("leaf", ("state", "sub"), None),
        ),
        out_specs=P(("groups", "leaf", "state", "sub"), None, None, None, None),
        check_vma=False,
    )
```

```python
import math

import jax
import jax.numpy as jnp
from jax import lax
from jax.sharding import PartitionSpec as P

STATES = 4
SBLK = 4
PHI = 2048
HI = lax.Precision.HIGH


def complex_join(first, second, half):
    real = first[..., :half] - second[..., half:]
    imag = first[..., half:] + second[..., :half]
    return jnp.concatenate([real, imag], axis=-1)


def turn_select(vectors, rotation, octants, backward):
    degrees, orders, width = vectors.shape
    if backward:
        mats = jnp.transpose(rotation, (1, 2, 0, 4, 3))
        sign = -1.0
    else:
        mats = jnp.transpose(rotation, (1, 2, 0, 3, 4))
        sign = 1.0
    mats = mats.reshape(2, degrees, 8 * orders, orders)
    first = jnp.einsum("lQp,lpC->lQC", mats[0], vectors, precision=HI)
    second = sign * jnp.einsum("lQp,lpC->lQC", mats[1], vectors, precision=HI)
    joined = complex_join(first, second, width // 2).reshape(degrees, 8, orders, width)
    count = octants.shape[0]
    chosen = (octants[None, :] == jnp.arange(8, dtype=jnp.int32)[:, None]).astype(jnp.float32)
    column_mask = jnp.tile(chosen, (1, width // count))
    return jnp.sum(joined * column_mask[None, :, None, :], axis=1)


def axial_apply(vectors, axial):
    degrees, orders, width = vectors.shape
    rest = width // 4
    moved = vectors.reshape(degrees, orders, 2, 2, rest)
    moved = jnp.transpose(moved, (1, 3, 0, 2, 4)).reshape(orders, 2 * degrees, 2 * rest)
    mats = axial.reshape(2, orders, 2 * degrees, 2 * degrees)
    first = jnp.einsum("qab,qbC->qaC", mats[0], moved, precision=HI)
    second = jnp.einsum("qab,qbC->qaC", mats[1], moved, precision=HI)
    joined = complex_join(first, second, rest).reshape(orders, 2, degrees, 2, rest)
    return jnp.transpose(joined, (2, 0, 3, 1, 4)).reshape(degrees, orders, width)


def move_expansion(vectors, octants, rotation, axial):
    turned = turn_select(vectors, rotation, octants, False)
    return turn_select(axial_apply(turned, axial), rotation, octants, True)


def local_boxes(
    sphere_block,
    live_count,
    cluster,
    leaf_parent,
    leaf_octant,
    box_octant,
    rotation,
    axial_one,
    axial_two,
):
    degrees, orders = (sphere_block.shape[0], sphere_block.shape[1])
    channel = sphere_block.shape[2] * sphere_block.shape[3] * sphere_block.shape[4]
    slots = sphere_block.shape[-1]
    per_block = slots // SBLK
    alive = jnp.arange(slots, dtype=jnp.int32) // per_block < live_count
    leaf_total = leaf_parent.shape[0]
    member = (
        (cluster[:, None] == jnp.arange(leaf_total, dtype=jnp.int32)[None, :]) & alive[:, None]
    ).astype(jnp.bfloat16)
    ident = jnp.eye(channel, dtype=jnp.bfloat16)
    spread = (ident[:, None, :, None] * member[None, :, None, :]).reshape(
        channel * slots, channel * leaf_total
    )
    leaves = jnp.dot(
        sphere_block.reshape(degrees * orders, channel * slots),
        spread,
        preferred_element_type=jnp.float32,
    ).reshape(degrees, orders, channel * leaf_total)
    moved = move_expansion(leaves, leaf_octant, rotation, axial_one)
    box_total = box_octant.shape[0]
    parents = (leaf_parent[:, None] == jnp.arange(box_total, dtype=jnp.int32)[None, :]).astype(
        jnp.float32
    )
    wide_ident = jnp.eye(channel, dtype=jnp.float32)
    wide_parents = (wide_ident[:, None, :, None] * parents[None, :, None, :]).reshape(
        channel * leaf_total, channel * box_total
    )
    boxes = jnp.einsum("lpC,CD->lpD", moved, wide_parents, precision=HI)
    outer = move_expansion(boxes, box_octant, rotation, axial_two)
    return outer.reshape(degrees, orders, channel, box_total).sum(-1)


def owner_frame(owner_sum, owner_turn, owner_shift):
    degrees, orders, width = owner_sum.shape
    states = width // 4
    first = jnp.einsum("lqp,lpC->lqC", owner_turn[0], owner_sum, precision=HI)
    second = jnp.einsum("lqp,lpC->lqC", owner_turn[1], owner_sum, precision=HI)
    turned = complex_join(first, second, width // 2)
    moved = turned.reshape(degrees, orders, 2, 2, states)
    moved = jnp.transpose(moved, (1, 3, 0, 2, 4)).reshape(orders, 2 * degrees, 2 * states)
    root_degrees = owner_shift.shape[3]
    mats = owner_shift.reshape(2, orders, 2 * root_degrees, 2 * degrees)
    first = jnp.einsum("qab,qbC->qaC", mats[0], moved, precision=HI)
    second = jnp.einsum("qab,qbC->qaC", mats[1], moved, precision=HI)
    joined = complex_join(first, second, states).reshape(orders, 2, root_degrees, 2, states)
    framed = jnp.transpose(joined, (2, 1, 3, 4, 0)).reshape(root_degrees, 4 * states, orders)
    return framed.astype(jnp.bfloat16)


def rotate_back(framed, functions, azimuth, half_orders):
    root_degrees, width = (framed.shape[0], framed.shape[1])
    states = width // 4
    orders_here = functions.shape[2]
    values = jnp.einsum("nCm,nmj->nCj", framed, functions, preferred_element_type=jnp.float32)
    values = values.reshape(root_degrees, 2, 2, states, orders_here)
    order_values = (jnp.arange(orders_here, dtype=jnp.int32) - half_orders).astype(jnp.float32)
    cosine = jnp.cos(order_values * azimuth)
    sine = jnp.sin(order_values * azimuth)
    real_part = cosine * values[:, :, 0] + sine * values[:, :, 1]
    imag_part = cosine * values[:, :, 1] - sine * values[:, :, 0]
    joined = jnp.stack([real_part, imag_part], axis=2)
    return jnp.transpose(joined, (4, 1, 2, 3, 0)).reshape(orders_here, 4 * states * root_degrees)


def legendre_field(root_coef, table):
    orders_here, root_degrees = (table.shape[0], table.shape[1])
    lat_total = table.shape[2] // 2
    rows = root_coef.shape[1] // root_degrees
    states = rows // 4
    half = rows // 2
    blocks = jnp.einsum(
        "jrn,jnK->jrK",
        root_coef.reshape(orders_here, rows, root_degrees),
        table,
        preferred_element_type=jnp.float32,
    )
    theta_part = blocks[:, :half, :lat_total] + blocks[:, half:, lat_total:]
    cross = blocks[:, :half, lat_total:] + blocks[:, half:, :lat_total]
    phi_part = jnp.concatenate([-cross[:, states:], cross[:, :states]], axis=1)
    return jnp.concatenate([theta_part, phi_part], axis=1)


def synthesize(spectrum, longitudes):
    orders = spectrum.shape[-1]
    fine = 128
    coarse = longitudes // fine
    order_ids = jnp.arange(orders, dtype=jnp.int32) - orders // 2
    coarse_angle = jnp.mod(order_ids[:, None] * (fine * jnp.arange(coarse, dtype=jnp.int32))[None, :], longitudes)
    coarse_angle = coarse_angle.astype(jnp.float32) * (2.0 * math.pi / longitudes)
    fine_angle = jnp.mod(order_ids[:, None] * jnp.arange(fine, dtype=jnp.int32)[None, :], longitudes)
    fine_angle = fine_angle.astype(jnp.float32) * (2.0 * math.pi / longitudes)
    pc, ps = jnp.cos(coarse_angle), jnp.sin(coarse_angle)
    qc, qs = jnp.cos(fine_angle), jnp.sin(fine_angle)
    spec = spectrum.astype(jnp.float32)
    sr, si = spec[:, 0], spec[:, 1]
    vr = sr[..., None, :] * pc.T - si[..., None, :] * ps.T
    vi = sr[..., None, :] * ps.T + si[..., None, :] * pc.T
    lhs = jnp.stack([vr, vi], axis=-2)
    rhs = jnp.stack([jnp.stack([qc, qs], axis=1), jnp.stack([-qs, qc], axis=1)], axis=0)
    out = jnp.einsum("csxkam,amfb->xscfkb", lhs, rhs, precision=HI)
    out = out.reshape(out.shape[:4] + (longitudes,))
    return out * (1.0 / math.sqrt(orders))


def pair_sum(x, axis):
    if lax.axis_size(axis) != 2:
        return lax.psum(x, axis)
    return x + lax.ppermute(x, axis, [(0, 1), (1, 0)])


def pair_scatter(x, axis):
    me = lax.axis_index(axis)
    keep = jnp.where(me == 0, x[0], x[1])
    give = jnp.where(me == 0, x[1], x[0])
    got = lax.ppermute(give.astype(jnp.bfloat16), axis, [(0, 1), (1, 0)])
    return keep + got.astype(keep.dtype)


def shift_all_to_all(x, axis):
    n = lax.axis_size(axis)
    me = lax.axis_index(axis)
    rows = jnp.arange(n)
    result = jnp.zeros_like(x)
    for step in range(n):
        target = (me + step) % n
        piece = jnp.take(x, target, axis=0)
        if step:
            piece = lax.ppermute(piece, axis, [(i, (i + step) % n) for i in range(n)])
        source = (me - step) % n
        result = jnp.where((rows == source).reshape((n,) + (1,) * (x.ndim - 1)), piece[None], result)
    return result


def shift_reduce_scatter(x, axis):
    n = lax.axis_size(axis)
    me = lax.axis_index(axis)
    total = jnp.take(x, me, axis=0)
    for step in range(1, n):
        piece = jnp.take(x, (me + step) % n, axis=0).astype(jnp.bfloat16)
        piece = lax.ppermute(piece, axis, [(i, (i + step) % n) for i in range(n)])
        total = total + piece.astype(total.dtype)
    return total


def group_sum(x, axes):
    n = 1
    for axis in axes:
        n *= lax.axis_size(axis)
    total = x
    for step in range(1, n):
        total = total + lax.ppermute(x, axes, [(i, (i + step) % n) for i in range(n)])
    return total


def direct_exchange(x, axes, blocks):
    n = x.shape[0]
    me = lax.axis_index(axes)
    rows = jnp.arange(blocks).reshape((blocks,) + (1,) * (x.ndim - 1))
    result = jnp.zeros((blocks,) + x.shape[1:], jnp.float32)
    for step in range(n):
        piece = jnp.take(x, (me + step) % n, axis=0)
        if step:
            piece = lax.ppermute(piece.astype(jnp.bfloat16), axes, [(i, (i + step) % n) for i in range(n)])
        source = (me - step) % n
        result = result + jnp.where(rows == source // (n // blocks), piece.astype(jnp.float32)[None], 0.0)
    return result


def on_device(
    sphere_coef,
    live_blocks,
    cluster,
    leaf_parent,
    leaf_octant,
    box_octant,
    rotation,
    axial_one,
    axial_two,
    owner_rotation,
    owner_axial,
    owner_angle,
    turn_table,
    angular_table,
):
    partial_owner = local_boxes(
        sphere_coef,
        live_blocks[0],
        cluster,
        leaf_parent,
        leaf_octant,
        box_octant,
        rotation,
        axial_one,
        axial_two,
    )
    if lax.axis_size("state") * lax.axis_size("sub") <= 4:
        owner_sum = group_sum(partial_owner, ("state", "sub"))
    else:
        owner_sum = pair_sum(pair_sum(partial_owner, "sub"), "state")
    framed = owner_frame(owner_sum, owner_rotation[0], owner_axial[0])
    leaf_size = lax.axis_size("leaf")
    orders = turn_table.shape[3]
    half_orders = orders // 2
    own_orders = orders // leaf_size
    own_azimuth = owner_angle[lax.axis_index("leaf")]
    piece = turn_table[0]
    contribution = rotate_back(framed, piece, own_azimuth, half_orders)
    if leaf_size <= 4:
        root = shift_reduce_scatter(contribution.reshape((leaf_size, own_orders) + contribution.shape[1:]), "leaf")
    else:
        root = lax.psum_scatter(contribution, "leaf", scatter_dimension=0, tiled=True)
    root_coef = root.astype(jnp.bfloat16)
    field = legendre_field(root_coef, angular_table)
    channel = field.shape[1]
    group_size = lax.axis_size("state") * lax.axis_size("sub")
    lat_rows = field.shape[2] // (leaf_size * group_size)
    shaped = field.reshape(own_orders, channel, leaf_size, group_size, lat_rows)
    shaped = jnp.transpose(shaped, (3, 2, 1, 4, 0)).reshape(
        group_size, leaf_size, channel * lat_rows * own_orders
    )
    if lax.axis_size("state") == 2 and lax.axis_size("sub") == 2 and leaf_size <= 4:
        pieces = jnp.swapaxes(shaped, 0, 1).reshape(leaf_size * group_size, -1)
        moved = direct_exchange(pieces, ("leaf", "state", "sub"), leaf_size)
    else:
        summed = lax.psum_scatter(shaped.astype(jnp.bfloat16), ("state", "sub"), scatter_dimension=0, tiled=True)
        moved = lax.all_to_all(summed, "leaf", split_axis=1, concat_axis=2, tiled=True)
    spectrum = moved.reshape(leaf_size, channel, lat_rows, own_orders)
    spectrum = jnp.transpose(spectrum, (1, 2, 0, 3)).reshape(2, 2, -1, lat_rows, orders)
    return synthesize(spectrum, PHI)


def solution(mesh):
    return jax.shard_map(
        on_device,
        mesh=mesh,
        in_specs=(
            P(None, None, None, None, None, ("groups", "leaf", "state", "sub")),
            P(("groups", "leaf", "state", "sub")),
            P(("groups", "leaf", "state", "sub")),
            P(("groups", "leaf", "state", "sub")),
            P(("groups", "leaf", "state", "sub")),
            P(("groups", "leaf", "state", "sub")),
            P(),
            P(),
            P(),
            P(("groups", "leaf"), None, None, None, None),
            P(("groups", "leaf"), None, None, None, ("state", "sub"), None, None),
            P("groups"),
            P(("groups", "leaf"), ("state", "sub"), None, None),
            P("leaf", ("state", "sub"), None),
        ),
        out_specs=P(("groups", "leaf", "state", "sub"), None, None, None, None),
        check_vma=False,
    )
```

```python
import math

import jax
import jax.numpy as jnp
from jax import lax
from jax.sharding import PartitionSpec as P

STATES = 4
SBLK = 4
PHI = 2048
HI = lax.Precision.HIGH
LEAF_PREC = lax.Precision.DEFAULT


def complex_join(first, second, half):
    real = first[..., :half] - second[..., half:]
    imag = first[..., half:] + second[..., :half]
    return jnp.concatenate([real, imag], axis=-1)


def turn_select(vectors, rotation, octants, backward, prec):
    degrees, orders, width = vectors.shape
    if backward:
        mats = jnp.transpose(rotation, (1, 2, 0, 4, 3))
        sign = -1.0
    else:
        mats = jnp.transpose(rotation, (1, 2, 0, 3, 4))
        sign = 1.0
    mats = mats.reshape(2, degrees, 8 * orders, orders)
    first = jnp.einsum("lQp,lpC->lQC", mats[0], vectors, precision=prec)
    second = sign * jnp.einsum("lQp,lpC->lQC", mats[1], vectors, precision=prec)
    joined = complex_join(first, second, width // 2).reshape(degrees, 8, orders, width)
    count = octants.shape[0]
    chosen = (octants[None, :] == jnp.arange(8, dtype=jnp.int32)[:, None]).astype(jnp.float32)
    column_mask = jnp.tile(chosen, (1, width // count))
    return jnp.sum(joined * column_mask[None, :, None, :], axis=1)


def axial_apply(vectors, axial, prec):
    degrees, orders, width = vectors.shape
    rest = width // 4
    moved = vectors.reshape(degrees, orders, 2, 2, rest)
    moved = jnp.transpose(moved, (1, 3, 0, 2, 4)).reshape(orders, 2 * degrees, 2 * rest)
    mats = axial.reshape(2, orders, 2 * degrees, 2 * degrees)
    first = jnp.einsum("qab,qbC->qaC", mats[0], moved, precision=prec)
    second = jnp.einsum("qab,qbC->qaC", mats[1], moved, precision=prec)
    joined = complex_join(first, second, rest).reshape(orders, 2, degrees, 2, rest)
    return jnp.transpose(joined, (2, 0, 3, 1, 4)).reshape(degrees, orders, width)


def move_expansion(vectors, octants, rotation, axial, prec):
    turned = turn_select(vectors, rotation, octants, False, prec)
    return turn_select(axial_apply(turned, axial, prec), rotation, octants, True, prec)


def local_boxes(
    sphere_block,
    live_count,
    cluster,
    leaf_parent,
    leaf_octant,
    box_octant,
    rotation,
    axial_one,
    axial_two,
):
    degrees, orders = (sphere_block.shape[0], sphere_block.shape[1])
    channel = sphere_block.shape[2] * sphere_block.shape[3] * sphere_block.shape[4]
    slots = sphere_block.shape[-1]
    per_block = slots // SBLK
    alive = jnp.arange(slots, dtype=jnp.int32) // per_block < live_count
    leaf_total = leaf_parent.shape[0]
    member = (
        (cluster[:, None] == jnp.arange(leaf_total, dtype=jnp.int32)[None, :]) & alive[:, None]
    ).astype(jnp.bfloat16)
    ident = jnp.eye(channel, dtype=jnp.bfloat16)
    spread = (ident[:, None, :, None] * member[None, :, None, :]).reshape(
        channel * slots, channel * leaf_total
    )
    leaves = jnp.dot(
        sphere_block.reshape(degrees * orders, channel * slots),
        spread,
        preferred_element_type=jnp.float32,
    ).reshape(degrees, orders, channel * leaf_total)
    moved = move_expansion(leaves, leaf_octant, rotation, axial_one, LEAF_PREC)
    box_total = box_octant.shape[0]
    parents = (leaf_parent[:, None] == jnp.arange(box_total, dtype=jnp.int32)[None, :]).astype(
        jnp.float32
    )
    wide_ident = jnp.eye(channel, dtype=jnp.float32)
    wide_parents = (wide_ident[:, None, :, None] * parents[None, :, None, :]).reshape(
        channel * leaf_total, channel * box_total
    )
    boxes = jnp.einsum("lpC,CD->lpD", moved, wide_parents, precision=HI)
    outer = move_expansion(boxes, box_octant, rotation, axial_two, HI)
    return outer.reshape(degrees, orders, channel, box_total).sum(-1)


def owner_frame(owner_sum, owner_turn, owner_shift):
    degrees, orders, width = owner_sum.shape
    states = width // 4
    first = jnp.einsum("lqp,lpC->lqC", owner_turn[0], owner_sum, precision=HI)
    second = jnp.einsum("lqp,lpC->lqC", owner_turn[1], owner_sum, precision=HI)
    turned = complex_join(first, second, width // 2)
    moved = turned.reshape(degrees, orders, 2, 2, states)
    moved = jnp.transpose(moved, (1, 3, 0, 2, 4)).reshape(orders, 2 * degrees, 2 * states)
    root_degrees = owner_shift.shape[3]
    mats = owner_shift.reshape(2, orders, 2 * root_degrees, 2 * degrees)
    first = jnp.einsum("qab,qbC->qaC", mats[0], moved, precision=HI)
    second = jnp.einsum("qab,qbC->qaC", mats[1], moved, precision=HI)
    joined = complex_join(first, second, states).reshape(orders, 2, root_degrees, 2, states)
    framed = jnp.transpose(joined, (2, 1, 3, 4, 0)).reshape(root_degrees, 4 * states, orders)
    return framed.astype(jnp.bfloat16)


def rotate_back(framed, functions, azimuth, half_orders):
    root_degrees, width = (framed.shape[0], framed.shape[1])
    states = width // 4
    orders_here = functions.shape[2]
    values = jnp.einsum("nCm,nmj->nCj", framed, functions, preferred_element_type=jnp.float32)
    values = values.reshape(root_degrees, 2, 2, states, orders_here)
    order_values = (jnp.arange(orders_here, dtype=jnp.int32) - half_orders).astype(jnp.float32)
    cosine = jnp.cos(order_values * azimuth)
    sine = jnp.sin(order_values * azimuth)
    real_part = cosine * values[:, :, 0] + sine * values[:, :, 1]
    imag_part = cosine * values[:, :, 1] - sine * values[:, :, 0]
    joined = jnp.stack([real_part, imag_part], axis=2)
    return jnp.transpose(joined, (4, 1, 2, 3, 0)).reshape(orders_here, 4 * states * root_degrees)


def legendre_field(root_coef, table):
    orders_here, root_degrees = (table.shape[0], table.shape[1])
    lat_total = table.shape[2] // 2
    rows = root_coef.shape[1] // root_degrees
    states = rows // 4
    half = rows // 2
    blocks = jnp.einsum(
        "jrn,jnK->jrK",
        root_coef.reshape(orders_here, rows, root_degrees),
        table,
        preferred_element_type=jnp.float32,
    )
    theta_part = blocks[:, :half, :lat_total] + blocks[:, half:, lat_total:]
    cross = blocks[:, :half, lat_total:] + blocks[:, half:, :lat_total]
    phi_part = jnp.concatenate([-cross[:, states:], cross[:, :states]], axis=1)
    return jnp.concatenate([theta_part, phi_part], axis=1)


def synthesize(spectrum, longitudes):
    orders = spectrum.shape[-1]
    fine = 128
    coarse = longitudes // fine
    order_ids = jnp.arange(orders, dtype=jnp.int32) - orders // 2
    coarse_angle = jnp.mod(order_ids[:, None] * (fine * jnp.arange(coarse, dtype=jnp.int32))[None, :], longitudes)
    coarse_angle = coarse_angle.astype(jnp.float32) * (2.0 * math.pi / longitudes)
    fine_angle = jnp.mod(order_ids[:, None] * jnp.arange(fine, dtype=jnp.int32)[None, :], longitudes)
    fine_angle = fine_angle.astype(jnp.float32) * (2.0 * math.pi / longitudes)
    pc, ps = jnp.cos(coarse_angle), jnp.sin(coarse_angle)
    qc, qs = jnp.cos(fine_angle), jnp.sin(fine_angle)
    spec = spectrum.astype(jnp.float32)
    sr, si = spec[:, 0], spec[:, 1]
    vr = sr[..., None, :] * pc.T - si[..., None, :] * ps.T
    vi = sr[..., None, :] * ps.T + si[..., None, :] * pc.T
    lhs = jnp.stack([vr, vi], axis=-2)
    rhs = jnp.stack([jnp.stack([qc, qs], axis=1), jnp.stack([-qs, qc], axis=1)], axis=0)
    out = jnp.einsum("csxkam,amfb->xscfkb", lhs, rhs, precision=HI)
    out = out.reshape(out.shape[:4] + (longitudes,))
    return out * (1.0 / math.sqrt(orders))


def pair_sum(x, axis):
    if lax.axis_size(axis) != 2:
        return lax.psum(x, axis)
    return x + lax.ppermute(x, axis, [(0, 1), (1, 0)])


def pair_scatter(x, axis):
    me = lax.axis_index(axis)
    keep = jnp.where(me == 0, x[0], x[1])
    give = jnp.where(me == 0, x[1], x[0])
    got = lax.ppermute(give.astype(jnp.bfloat16), axis, [(0, 1), (1, 0)])
    return keep + got.astype(keep.dtype)


def shift_all_to_all(x, axis):
    n = lax.axis_size(axis)
    me = lax.axis_index(axis)
    rows = jnp.arange(n)
    result = jnp.zeros_like(x)
    for step in range(n):
        target = (me + step) % n
        piece = jnp.take(x, target, axis=0)
        if step:
            piece = lax.ppermute(piece, axis, [(i, (i + step) % n) for i in range(n)])
        source = (me - step) % n
        result = jnp.where((rows == source).reshape((n,) + (1,) * (x.ndim - 1)), piece[None], result)
    return result


def shift_reduce_scatter(x, axis):
    n = lax.axis_size(axis)
    me = lax.axis_index(axis)
    total = jnp.take(x, me, axis=0)
    for step in range(1, n):
        piece = jnp.take(x, (me + step) % n, axis=0).astype(jnp.bfloat16)
        piece = lax.ppermute(piece, axis, [(i, (i + step) % n) for i in range(n)])
        total = total + piece.astype(total.dtype)
    return total


def on_device(
    sphere_coef,
    live_blocks,
    cluster,
    leaf_parent,
    leaf_octant,
    box_octant,
    rotation,
    axial_one,
    axial_two,
    owner_rotation,
    owner_axial,
    owner_angle,
    turn_table,
    angular_table,
):
    partial_owner = local_boxes(
        sphere_coef,
        live_blocks[0],
        cluster,
        leaf_parent,
        leaf_octant,
        box_octant,
        rotation,
        axial_one,
        axial_two,
    )
    owner_sum = pair_sum(pair_sum(partial_owner, "sub"), "state")
    framed = owner_frame(owner_sum, owner_rotation[0], owner_axial[0])
    leaf_size = lax.axis_size("leaf")
    orders = turn_table.shape[3]
    half_orders = orders // 2
    own_orders = orders // leaf_size
    own_azimuth = owner_angle[lax.axis_index("leaf")]
    piece = turn_table[0]
    contribution = rotate_back(framed, piece, own_azimuth, half_orders)
    if leaf_size <= 4:
        root = shift_reduce_scatter(contribution.reshape((leaf_size, own_orders) + contribution.shape[1:]), "leaf")
    else:
        root = lax.psum_scatter(contribution, "leaf", scatter_dimension=0, tiled=True)
    root_coef = root.astype(jnp.bfloat16)
    field = legendre_field(root_coef, angular_table)
    channel = field.shape[1]
    group_size = lax.axis_size("state") * lax.axis_size("sub")
    lat_rows = field.shape[2] // (leaf_size * group_size)
    shaped = field.reshape(own_orders, channel, leaf_size, group_size, lat_rows)
    shaped = jnp.transpose(shaped, (3, 2, 1, 4, 0)).reshape(
        group_size, leaf_size, channel * lat_rows * own_orders
    )
    if lax.axis_size("state") == 2 and lax.axis_size("sub") == 2 and leaf_size <= 4:
        halves = shaped.reshape((2, 2) + shaped.shape[1:])
        summed = pair_scatter(pair_scatter(jnp.swapaxes(halves, 0, 1), "sub"), "state")
        moved = shift_all_to_all(summed.astype(jnp.bfloat16), "leaf")
    else:
        summed = lax.psum_scatter(shaped.astype(jnp.bfloat16), ("state", "sub"), scatter_dimension=0, tiled=True)
        moved = lax.all_to_all(summed, "leaf", split_axis=1, concat_axis=2, tiled=True)
    spectrum = moved.reshape(leaf_size, channel, lat_rows, own_orders)
    spectrum = jnp.transpose(spectrum, (1, 2, 0, 3)).reshape(2, 2, -1, lat_rows, orders)
    return synthesize(spectrum, PHI)


def solution(mesh):
    return jax.shard_map(
        on_device,
        mesh=mesh,
        in_specs=(
            P(None, None, None, None, None, ("groups", "leaf", "state", "sub")),
            P(("groups", "leaf", "state", "sub")),
            P(("groups", "leaf", "state", "sub")),
            P(("groups", "leaf", "state", "sub")),
            P(("groups", "leaf", "state", "sub")),
            P(("groups", "leaf", "state", "sub")),
            P(),
            P(),
            P(),
            P(("groups", "leaf"), None, None, None, None),
            P(("groups", "leaf"), None, None, None, ("state", "sub"), None, None),
            P("groups"),
            P(("groups", "leaf"), ("state", "sub"), None, None),
            P("leaf", ("state", "sub"), None),
        ),
        out_specs=P(("groups", "leaf", "state", "sub"), None, None, None, None),
        check_vma=False,
    )
```

```python
import math

import jax
import jax.numpy as jnp
from jax import lax
from jax.sharding import PartitionSpec as P

STATES = 4
SBLK = 4
PHI = 2048
HI = lax.Precision.HIGH
LEAF_PREC = lax.Precision.DEFAULT


def complex_join(first, second, half):
    real = first[..., :half] - second[..., half:]
    imag = first[..., half:] + second[..., :half]
    return jnp.concatenate([real, imag], axis=-1)


def turn_select(vectors, rotation, octants, backward, prec):
    degrees, orders, width = vectors.shape
    if backward:
        mats = jnp.transpose(rotation, (1, 2, 0, 4, 3))
        sign = -1.0
    else:
        mats = jnp.transpose(rotation, (1, 2, 0, 3, 4))
        sign = 1.0
    mats = mats.reshape(2, degrees, 8 * orders, orders)
    first = jnp.einsum("lQp,lpC->lQC", mats[0], vectors, precision=prec)
    second = sign * jnp.einsum("lQp,lpC->lQC", mats[1], vectors, precision=prec)
    joined = complex_join(first, second, width // 2).reshape(degrees, 8, orders, width)
    count = octants.shape[0]
    chosen = (octants[None, :] == jnp.arange(8, dtype=jnp.int32)[:, None]).astype(jnp.float32)
    column_mask = jnp.tile(chosen, (1, width // count))
    return jnp.sum(joined * column_mask[None, :, None, :], axis=1)


def axial_apply(vectors, axial, prec):
    degrees, orders, width = vectors.shape
    rest = width // 4
    moved = vectors.reshape(degrees, orders, 2, 2, rest)
    moved = jnp.transpose(moved, (1, 3, 0, 2, 4)).reshape(orders, 2 * degrees, 2 * rest)
    mats = axial.reshape(2, orders, 2 * degrees, 2 * degrees)
    first = jnp.einsum("qab,qbC->qaC", mats[0], moved, precision=prec)
    second = jnp.einsum("qab,qbC->qaC", mats[1], moved, precision=prec)
    joined = complex_join(first, second, rest).reshape(orders, 2, degrees, 2, rest)
    return jnp.transpose(joined, (2, 0, 3, 1, 4)).reshape(degrees, orders, width)


def move_expansion(vectors, octants, rotation, axial, prec):
    turned = turn_select(vectors, rotation, octants, False, prec)
    return turn_select(axial_apply(turned, axial, prec), rotation, octants, True, prec)


def local_boxes(
    sphere_block,
    live_count,
    cluster,
    leaf_parent,
    leaf_octant,
    box_octant,
    rotation,
    axial_one,
    axial_two,
):
    degrees, orders = (sphere_block.shape[0], sphere_block.shape[1])
    channel = sphere_block.shape[2] * sphere_block.shape[3] * sphere_block.shape[4]
    slots = sphere_block.shape[-1]
    per_block = slots // SBLK
    alive = jnp.arange(slots, dtype=jnp.int32) // per_block < live_count
    leaf_total = leaf_parent.shape[0]
    member = (
        (cluster[:, None] == jnp.arange(leaf_total, dtype=jnp.int32)[None, :]) & alive[:, None]
    ).astype(jnp.bfloat16)
    ident = jnp.eye(channel, dtype=jnp.bfloat16)
    spread = (ident[:, None, :, None] * member[None, :, None, :]).reshape(
        channel * slots, channel * leaf_total
    )
    leaves = jnp.dot(
        sphere_block.reshape(degrees * orders, channel * slots),
        spread,
        preferred_element_type=jnp.float32,
    ).reshape(degrees, orders, channel * leaf_total)
    moved = move_expansion(leaves, leaf_octant, rotation, axial_one, LEAF_PREC)
    box_total = box_octant.shape[0]
    parents = (leaf_parent[:, None] == jnp.arange(box_total, dtype=jnp.int32)[None, :]).astype(
        jnp.float32
    )
    wide_ident = jnp.eye(channel, dtype=jnp.float32)
    wide_parents = (wide_ident[:, None, :, None] * parents[None, :, None, :]).reshape(
        channel * leaf_total, channel * box_total
    )
    boxes = jnp.einsum("lpC,CD->lpD", moved, wide_parents, precision=HI)
    outer = move_expansion(boxes, box_octant, rotation, axial_two, LEAF_PREC)
    return outer.reshape(degrees, orders, channel, box_total).sum(-1)


def owner_frame(owner_sum, owner_turn, owner_shift):
    degrees, orders, width = owner_sum.shape
    states = width // 4
    first = jnp.einsum("lqp,lpC->lqC", owner_turn[0], owner_sum, precision=HI)
    second = jnp.einsum("lqp,lpC->lqC", owner_turn[1], owner_sum, precision=HI)
    turned = complex_join(first, second, width // 2)
    moved = turned.reshape(degrees, orders, 2, 2, states)
    moved = jnp.transpose(moved, (1, 3, 0, 2, 4)).reshape(orders, 2 * degrees, 2 * states)
    root_degrees = owner_shift.shape[3]
    mats = owner_shift.reshape(2, orders, 2 * root_degrees, 2 * degrees)
    first = jnp.einsum("qab,qbC->qaC", mats[0], moved, precision=HI)
    second = jnp.einsum("qab,qbC->qaC", mats[1], moved, precision=HI)
    joined = complex_join(first, second, states).reshape(orders, 2, root_degrees, 2, states)
    framed = jnp.transpose(joined, (2, 1, 3, 4, 0)).reshape(root_degrees, 4 * states, orders)
    return framed.astype(jnp.bfloat16)


def rotate_back(framed, functions, azimuth, half_orders):
    root_degrees, width = (framed.shape[0], framed.shape[1])
    states = width // 4
    orders_here = functions.shape[2]
    values = jnp.einsum("nCm,nmj->nCj", framed, functions, preferred_element_type=jnp.float32)
    values = values.reshape(root_degrees, 2, 2, states, orders_here)
    order_values = (jnp.arange(orders_here, dtype=jnp.int32) - half_orders).astype(jnp.float32)
    cosine = jnp.cos(order_values * azimuth)
    sine = jnp.sin(order_values * azimuth)
    real_part = cosine * values[:, :, 0] + sine * values[:, :, 1]
    imag_part = cosine * values[:, :, 1] - sine * values[:, :, 0]
    joined = jnp.stack([real_part, imag_part], axis=2)
    return jnp.transpose(joined, (4, 1, 2, 3, 0)).reshape(orders_here, 4 * states * root_degrees)


def legendre_field(root_coef, table):
    orders_here, root_degrees = (table.shape[0], table.shape[1])
    lat_total = table.shape[2] // 2
    rows = root_coef.shape[1] // root_degrees
    states = rows // 4
    half = rows // 2
    blocks = jnp.einsum(
        "jrn,jnK->jrK",
        root_coef.reshape(orders_here, rows, root_degrees),
        table,
        preferred_element_type=jnp.float32,
    )
    theta_part = blocks[:, :half, :lat_total] + blocks[:, half:, lat_total:]
    cross = blocks[:, :half, lat_total:] + blocks[:, half:, :lat_total]
    phi_part = jnp.concatenate([-cross[:, states:], cross[:, :states]], axis=1)
    return jnp.concatenate([theta_part, phi_part], axis=1)


def synthesize(spectrum, longitudes):
    orders = spectrum.shape[-1]
    fine = 128
    coarse = longitudes // fine
    order_ids = jnp.arange(orders, dtype=jnp.int32) - orders // 2
    coarse_angle = jnp.mod(order_ids[:, None] * (fine * jnp.arange(coarse, dtype=jnp.int32))[None, :], longitudes)
    coarse_angle = coarse_angle.astype(jnp.float32) * (2.0 * math.pi / longitudes)
    fine_angle = jnp.mod(order_ids[:, None] * jnp.arange(fine, dtype=jnp.int32)[None, :], longitudes)
    fine_angle = fine_angle.astype(jnp.float32) * (2.0 * math.pi / longitudes)
    pc, ps = jnp.cos(coarse_angle), jnp.sin(coarse_angle)
    qc, qs = jnp.cos(fine_angle), jnp.sin(fine_angle)
    spec = spectrum.astype(jnp.float32)
    sr, si = spec[:, 0], spec[:, 1]
    vr = sr[..., None, :] * pc.T - si[..., None, :] * ps.T
    vi = sr[..., None, :] * ps.T + si[..., None, :] * pc.T
    lhs = jnp.stack([vr, vi], axis=-2)
    rhs = jnp.stack([jnp.stack([qc, qs], axis=1), jnp.stack([-qs, qc], axis=1)], axis=0)
    out = jnp.einsum("csxkam,amfb->xscfkb", lhs, rhs, precision=HI)
    out = out.reshape(out.shape[:4] + (longitudes,))
    return out * (1.0 / math.sqrt(orders))


def pair_sum(x, axis):
    if lax.axis_size(axis) != 2:
        return lax.psum(x, axis)
    return x + lax.ppermute(x, axis, [(0, 1), (1, 0)])


def pair_scatter(x, axis):
    me = lax.axis_index(axis)
    keep = jnp.where(me == 0, x[0], x[1])
    give = jnp.where(me == 0, x[1], x[0])
    got = lax.ppermute(give.astype(jnp.bfloat16), axis, [(0, 1), (1, 0)])
    return keep + got.astype(keep.dtype)


def shift_all_to_all(x, axis):
    n = lax.axis_size(axis)
    me = lax.axis_index(axis)
    rows = jnp.arange(n)
    result = jnp.zeros_like(x)
    for step in range(n):
        target = (me + step) % n
        piece = jnp.take(x, target, axis=0)
        if step:
            piece = lax.ppermute(piece, axis, [(i, (i + step) % n) for i in range(n)])
        source = (me - step) % n
        result = jnp.where((rows == source).reshape((n,) + (1,) * (x.ndim - 1)), piece[None], result)
    return result


def shift_reduce_scatter(x, axis):
    n = lax.axis_size(axis)
    me = lax.axis_index(axis)
    total = jnp.take(x, me, axis=0)
    for step in range(1, n):
        piece = jnp.take(x, (me + step) % n, axis=0).astype(jnp.bfloat16)
        piece = lax.ppermute(piece, axis, [(i, (i + step) % n) for i in range(n)])
        total = total + piece.astype(total.dtype)
    return total


def on_device(
    sphere_coef,
    live_blocks,
    cluster,
    leaf_parent,
    leaf_octant,
    box_octant,
    rotation,
    axial_one,
    axial_two,
    owner_rotation,
    owner_axial,
    owner_angle,
    turn_table,
    angular_table,
):
    partial_owner = local_boxes(
        sphere_coef,
        live_blocks[0],
        cluster,
        leaf_parent,
        leaf_octant,
        box_octant,
        rotation,
        axial_one,
        axial_two,
    )
    owner_sum = pair_sum(pair_sum(partial_owner, "sub"), "state")
    framed = owner_frame(owner_sum, owner_rotation[0], owner_axial[0])
    leaf_size = lax.axis_size("leaf")
    orders = turn_table.shape[3]
    half_orders = orders // 2
    own_orders = orders // leaf_size
    own_azimuth = owner_angle[lax.axis_index("leaf")]
    piece = turn_table[0]
    contribution = rotate_back(framed, piece, own_azimuth, half_orders)
    if leaf_size <= 4:
        root = shift_reduce_scatter(contribution.reshape((leaf_size, own_orders) + contribution.shape[1:]), "leaf")
    else:
        root = lax.psum_scatter(contribution, "leaf", scatter_dimension=0, tiled=True)
    root_coef = root.astype(jnp.bfloat16)
    field = legendre_field(root_coef, angular_table)
    channel = field.shape[1]
    group_size = lax.axis_size("state") * lax.axis_size("sub")
    lat_rows = field.shape[2] // (leaf_size * group_size)
    shaped = field.reshape(own_orders, channel, leaf_size, group_size, lat_rows)
    shaped = jnp.transpose(shaped, (3, 2, 1, 4, 0)).reshape(
        group_size, leaf_size, channel * lat_rows * own_orders
    )
    if lax.axis_size("state") == 2 and lax.axis_size("sub") == 2 and leaf_size <= 4:
        halves = shaped.reshape((2, 2) + shaped.shape[1:])
        summed = pair_scatter(pair_scatter(jnp.swapaxes(halves, 0, 1), "sub"), "state")
        moved = shift_all_to_all(summed.astype(jnp.bfloat16), "leaf")
    else:
        summed = lax.psum_scatter(shaped.astype(jnp.bfloat16), ("state", "sub"), scatter_dimension=0, tiled=True)
        moved = lax.all_to_all(summed, "leaf", split_axis=1, concat_axis=2, tiled=True)
    spectrum = moved.reshape(leaf_size, channel, lat_rows, own_orders)
    spectrum = jnp.transpose(spectrum, (1, 2, 0, 3)).reshape(2, 2, -1, lat_rows, orders)
    return synthesize(spectrum, PHI)


def solution(mesh):
    return jax.shard_map(
        on_device,
        mesh=mesh,
        in_specs=(
            P(None, None, None, None, None, ("groups", "leaf", "state", "sub")),
            P(("groups", "leaf", "state", "sub")),
            P(("groups", "leaf", "state", "sub")),
            P(("groups", "leaf", "state", "sub")),
            P(("groups", "leaf", "state", "sub")),
            P(("groups", "leaf", "state", "sub")),
            P(),
            P(),
            P(),
            P(("groups", "leaf"), None, None, None, None),
            P(("groups", "leaf"), None, None, None, ("state", "sub"), None, None),
            P("groups"),
            P(("groups", "leaf"), ("state", "sub"), None, None),
            P("leaf", ("state", "sub"), None),
        ),
        out_specs=P(("groups", "leaf", "state", "sub"), None, None, None, None),
        check_vma=False,
    )
```

```python
import math

import jax
import jax.numpy as jnp
from jax import lax
from jax.sharding import PartitionSpec as P

STATES = 4
SBLK = 4
PHI = 2048
HI = lax.Precision.HIGH
LEAF_PREC = lax.Precision.DEFAULT


def complex_join(first, second, half):
    real = first[..., :half] - second[..., half:]
    imag = first[..., half:] + second[..., :half]
    return jnp.concatenate([real, imag], axis=-1)


def turn_select(vectors, rotation, octants, backward, prec):
    degrees, orders, width = vectors.shape
    if backward:
        mats = jnp.transpose(rotation, (1, 2, 0, 4, 3))
        sign = -1.0
    else:
        mats = jnp.transpose(rotation, (1, 2, 0, 3, 4))
        sign = 1.0
    mats = mats.reshape(2, degrees, 8 * orders, orders)
    first = jnp.einsum("lQp,lpC->lQC", mats[0], vectors, precision=prec)
    second = sign * jnp.einsum("lQp,lpC->lQC", mats[1], vectors, precision=prec)
    joined = complex_join(first, second, width // 2).reshape(degrees, 8, orders, width)
    count = octants.shape[0]
    chosen = (octants[None, :] == jnp.arange(8, dtype=jnp.int32)[:, None]).astype(jnp.float32)
    column_mask = jnp.tile(chosen, (1, width // count))
    return jnp.sum(joined * column_mask[None, :, None, :], axis=1)


def axial_apply(vectors, axial, prec):
    degrees, orders, width = vectors.shape
    rest = width // 4
    moved = vectors.reshape(degrees, orders, 2, 2, rest)
    moved = jnp.transpose(moved, (1, 3, 0, 2, 4)).reshape(orders, 2 * degrees, 2 * rest)
    mats = axial.reshape(2, orders, 2 * degrees, 2 * degrees)
    first = jnp.einsum("qab,qbC->qaC", mats[0], moved, precision=prec)
    second = jnp.einsum("qab,qbC->qaC", mats[1], moved, precision=prec)
    joined = complex_join(first, second, rest).reshape(orders, 2, degrees, 2, rest)
    return jnp.transpose(joined, (2, 0, 3, 1, 4)).reshape(degrees, orders, width)


def move_expansion(vectors, octants, rotation, axial, prec):
    turned = turn_select(vectors, rotation, octants, False, prec)
    return turn_select(axial_apply(turned, axial, prec), rotation, octants, True, prec)


def local_boxes(
    sphere_block,
    live_count,
    cluster,
    leaf_parent,
    leaf_octant,
    box_octant,
    rotation,
    axial_one,
    axial_two,
):
    degrees, orders = (sphere_block.shape[0], sphere_block.shape[1])
    channel = sphere_block.shape[2] * sphere_block.shape[3] * sphere_block.shape[4]
    slots = sphere_block.shape[-1]
    per_block = slots // SBLK
    alive = jnp.arange(slots, dtype=jnp.int32) // per_block < live_count
    leaf_total = leaf_parent.shape[0]
    member = (
        (cluster[:, None] == jnp.arange(leaf_total, dtype=jnp.int32)[None, :]) & alive[:, None]
    ).astype(jnp.bfloat16)
    leaves = jnp.dot(
        sphere_block.reshape(degrees * orders * channel, slots),
        member,
        preferred_element_type=jnp.float32,
    ).reshape(degrees, orders, channel * leaf_total)
    moved = move_expansion(leaves, leaf_octant, rotation, axial_one, LEAF_PREC)
    box_total = box_octant.shape[0]
    parents = (leaf_parent[:, None] == jnp.arange(box_total, dtype=jnp.int32)[None, :]).astype(
        jnp.float32
    )
    wide_ident = jnp.eye(channel, dtype=jnp.float32)
    wide_parents = (wide_ident[:, None, :, None] * parents[None, :, None, :]).reshape(
        channel * leaf_total, channel * box_total
    )
    boxes = jnp.einsum("lpC,CD->lpD", moved, wide_parents, precision=HI)
    outer = move_expansion(boxes, box_octant, rotation, axial_two, LEAF_PREC)
    return outer.reshape(degrees, orders, channel, box_total).sum(-1)


def owner_frame(owner_sum, owner_turn, owner_shift):
    degrees, orders, width = owner_sum.shape
    states = width // 4
    first = jnp.einsum("lqp,lpC->lqC", owner_turn[0], owner_sum, precision=HI)
    second = jnp.einsum("lqp,lpC->lqC", owner_turn[1], owner_sum, precision=HI)
    turned = complex_join(first, second, width // 2)
    moved = turned.reshape(degrees, orders, 2, 2, states)
    moved = jnp.transpose(moved, (1, 3, 0, 2, 4)).reshape(orders, 2 * degrees, 2 * states)
    root_degrees = owner_shift.shape[3]
    mats = owner_shift.reshape(2, orders, 2 * root_degrees, 2 * degrees)
    first = jnp.einsum("qab,qbC->qaC", mats[0], moved, precision=HI)
    second = jnp.einsum("qab,qbC->qaC", mats[1], moved, precision=HI)
    joined = complex_join(first, second, states).reshape(orders, 2, root_degrees, 2, states)
    framed = jnp.transpose(joined, (2, 1, 3, 4, 0)).reshape(root_degrees, 4 * states, orders)
    return framed.astype(jnp.bfloat16)


def rotate_back(framed, functions, azimuth, half_orders):
    root_degrees, width = (framed.shape[0], framed.shape[1])
    states = width // 4
    orders_here = functions.shape[2]
    values = jnp.einsum("nCm,nmj->nCj", framed, functions, preferred_element_type=jnp.float32)
    values = values.reshape(root_degrees, 2, 2, states, orders_here)
    order_values = (jnp.arange(orders_here, dtype=jnp.int32) - half_orders).astype(jnp.float32)
    cosine = jnp.cos(order_values * azimuth)
    sine = jnp.sin(order_values * azimuth)
    real_part = cosine * values[:, :, 0] + sine * values[:, :, 1]
    imag_part = cosine * values[:, :, 1] - sine * values[:, :, 0]
    joined = jnp.stack([real_part, imag_part], axis=2)
    return jnp.transpose(joined, (4, 1, 2, 3, 0)).reshape(orders_here, 4 * states * root_degrees)


def legendre_field(root_coef, table):
    orders_here, root_degrees = (table.shape[0], table.shape[1])
    lat_total = table.shape[2] // 2
    rows = root_coef.shape[1] // root_degrees
    states = rows // 4
    half = rows // 2
    blocks = jnp.einsum(
        "jrn,jnK->jrK",
        root_coef.reshape(orders_here, rows, root_degrees),
        table,
        preferred_element_type=jnp.float32,
    )
    theta_part = blocks[:, :half, :lat_total] + blocks[:, half:, lat_total:]
    cross = blocks[:, :half, lat_total:] + blocks[:, half:, :lat_total]
    phi_part = jnp.concatenate([-cross[:, states:], cross[:, :states]], axis=1)
    return jnp.concatenate([theta_part, phi_part], axis=1)


def synthesize(spectrum, longitudes):
    orders = spectrum.shape[-1]
    fine = 128
    coarse = longitudes // fine
    order_ids = jnp.arange(orders, dtype=jnp.int32) - orders // 2
    coarse_angle = jnp.mod(order_ids[:, None] * (fine * jnp.arange(coarse, dtype=jnp.int32))[None, :], longitudes)
    coarse_angle = coarse_angle.astype(jnp.float32) * (2.0 * math.pi / longitudes)
    fine_angle = jnp.mod(order_ids[:, None] * jnp.arange(fine, dtype=jnp.int32)[None, :], longitudes)
    fine_angle = fine_angle.astype(jnp.float32) * (2.0 * math.pi / longitudes)
    pc, ps = jnp.cos(coarse_angle), jnp.sin(coarse_angle)
    qc, qs = jnp.cos(fine_angle), jnp.sin(fine_angle)
    spec = spectrum.astype(jnp.float32)
    sr, si = spec[:, 0], spec[:, 1]
    vr = sr[..., None, :] * pc.T - si[..., None, :] * ps.T
    vi = sr[..., None, :] * ps.T + si[..., None, :] * pc.T
    lhs = jnp.stack([vr, vi], axis=-2)
    rhs = jnp.stack([jnp.stack([qc, qs], axis=1), jnp.stack([-qs, qc], axis=1)], axis=0)
    out = jnp.einsum("csxkam,amfb->xscfkb", lhs, rhs, precision=HI)
    out = out.reshape(out.shape[:4] + (longitudes,))
    return out * (1.0 / math.sqrt(orders))


def pair_sum(x, axis):
    if lax.axis_size(axis) != 2:
        return lax.psum(x, axis)
    return x + lax.ppermute(x, axis, [(0, 1), (1, 0)])


def pair_scatter(x, axis):
    me = lax.axis_index(axis)
    keep = jnp.where(me == 0, x[0], x[1])
    give = jnp.where(me == 0, x[1], x[0])
    got = lax.ppermute(give.astype(jnp.bfloat16), axis, [(0, 1), (1, 0)])
    return keep + got.astype(keep.dtype)


def shift_all_to_all(x, axis):
    n = lax.axis_size(axis)
    me = lax.axis_index(axis)
    rows = jnp.arange(n)
    result = jnp.zeros_like(x)
    for step in range(n):
        target = (me + step) % n
        piece = jnp.take(x, target, axis=0)
        if step:
            piece = lax.ppermute(piece, axis, [(i, (i + step) % n) for i in range(n)])
        source = (me - step) % n
        result = jnp.where((rows == source).reshape((n,) + (1,) * (x.ndim - 1)), piece[None], result)
    return result


def shift_reduce_scatter(x, axis):
    n = lax.axis_size(axis)
    me = lax.axis_index(axis)
    total = jnp.take(x, me, axis=0)
    for step in range(1, n):
        piece = jnp.take(x, (me + step) % n, axis=0).astype(jnp.bfloat16)
        piece = lax.ppermute(piece, axis, [(i, (i + step) % n) for i in range(n)])
        total = total + piece.astype(total.dtype)
    return total


def on_device(
    sphere_coef,
    live_blocks,
    cluster,
    leaf_parent,
    leaf_octant,
    box_octant,
    rotation,
    axial_one,
    axial_two,
    owner_rotation,
    owner_axial,
    owner_angle,
    turn_table,
    angular_table,
):
    partial_owner = local_boxes(
        sphere_coef,
        live_blocks[0],
        cluster,
        leaf_parent,
        leaf_octant,
        box_octant,
        rotation,
        axial_one,
        axial_two,
    )
    owner_sum = pair_sum(pair_sum(partial_owner, "sub"), "state")
    framed = owner_frame(owner_sum, owner_rotation[0], owner_axial[0])
    leaf_size = lax.axis_size("leaf")
    orders = turn_table.shape[3]
    half_orders = orders // 2
    own_orders = orders // leaf_size
    own_azimuth = owner_angle[lax.axis_index("leaf")]
    piece = turn_table[0]
    contribution = rotate_back(framed, piece, own_azimuth, half_orders)
    if leaf_size <= 4:
        root = shift_reduce_scatter(contribution.reshape((leaf_size, own_orders) + contribution.shape[1:]), "leaf")
    else:
        root = lax.psum_scatter(contribution, "leaf", scatter_dimension=0, tiled=True)
    root_coef = root.astype(jnp.bfloat16)
    field = legendre_field(root_coef, angular_table)
    channel = field.shape[1]
    group_size = lax.axis_size("state") * lax.axis_size("sub")
    lat_rows = field.shape[2] // (leaf_size * group_size)
    shaped = field.reshape(own_orders, channel, leaf_size, group_size, lat_rows)
    shaped = jnp.transpose(shaped, (3, 2, 1, 4, 0)).reshape(
        group_size, leaf_size, channel * lat_rows * own_orders
    )
    if lax.axis_size("state") == 2 and lax.axis_size("sub") == 2 and leaf_size <= 4:
        halves = shaped.reshape((2, 2) + shaped.shape[1:])
        summed = pair_scatter(pair_scatter(jnp.swapaxes(halves, 0, 1), "sub"), "state")
        moved = shift_all_to_all(summed.astype(jnp.bfloat16), "leaf")
    else:
        summed = lax.psum_scatter(shaped.astype(jnp.bfloat16), ("state", "sub"), scatter_dimension=0, tiled=True)
        moved = lax.all_to_all(summed, "leaf", split_axis=1, concat_axis=2, tiled=True)
    spectrum = moved.reshape(leaf_size, channel, lat_rows, own_orders)
    spectrum = jnp.transpose(spectrum, (1, 2, 0, 3)).reshape(2, 2, -1, lat_rows, orders)
    return synthesize(spectrum, PHI)


def solution(mesh):
    return jax.shard_map(
        on_device,
        mesh=mesh,
        in_specs=(
            P(None, None, None, None, None, ("groups", "leaf", "state", "sub")),
            P(("groups", "leaf", "state", "sub")),
            P(("groups", "leaf", "state", "sub")),
            P(("groups", "leaf", "state", "sub")),
            P(("groups", "leaf", "state", "sub")),
            P(("groups", "leaf", "state", "sub")),
            P(),
            P(),
            P(),
            P(("groups", "leaf"), None, None, None, None),
            P(("groups", "leaf"), None, None, None, ("state", "sub"), None, None),
            P("groups"),
            P(("groups", "leaf"), ("state", "sub"), None, None),
            P("leaf", ("state", "sub"), None),
        ),
        out_specs=P(("groups", "leaf", "state", "sub"), None, None, None, None),
        check_vma=False,
    )
```

```python
import math

import jax
import jax.numpy as jnp
from jax import lax
from jax.sharding import PartitionSpec as P

STATES = 4
SBLK = 4
PHI = 2048
HI = lax.Precision.HIGH
LEAF_PREC = lax.Precision.DEFAULT


def complex_join(first, second, half):
    real = first[..., :half] - second[..., half:]
    imag = first[..., half:] + second[..., :half]
    return jnp.concatenate([real, imag], axis=-1)


def turn_select(vectors, rotation, octants, backward, prec):
    degrees, orders, width = vectors.shape
    if backward:
        mats = jnp.transpose(rotation, (1, 2, 0, 4, 3))
        sign = -1.0
    else:
        mats = jnp.transpose(rotation, (1, 2, 0, 3, 4))
        sign = 1.0
    mats = mats.reshape(2, degrees, 8 * orders, orders)
    first = jnp.einsum("lQp,lpC->lQC", mats[0], vectors, precision=prec)
    second = sign * jnp.einsum("lQp,lpC->lQC", mats[1], vectors, precision=prec)
    joined = complex_join(first, second, width // 2).reshape(degrees, 8, orders, width)
    count = octants.shape[0]
    chosen = (octants[None, :] == jnp.arange(8, dtype=jnp.int32)[:, None]).astype(jnp.float32)
    column_mask = jnp.tile(chosen, (1, width // count))
    return jnp.sum(joined * column_mask[None, :, None, :], axis=1)


def axial_apply(vectors, axial, prec):
    degrees, orders, width = vectors.shape
    rest = width // 4
    moved = vectors.reshape(degrees, orders, 2, 2, rest)
    moved = jnp.transpose(moved, (1, 3, 0, 2, 4)).reshape(orders, 2 * degrees, 2 * rest)
    mats = axial.reshape(2, orders, 2 * degrees, 2 * degrees)
    first = jnp.einsum("qab,qbC->qaC", mats[0], moved, precision=prec)
    second = jnp.einsum("qab,qbC->qaC", mats[1], moved, precision=prec)
    joined = complex_join(first, second, rest).reshape(orders, 2, degrees, 2, rest)
    return jnp.transpose(joined, (2, 0, 3, 1, 4)).reshape(degrees, orders, width)


def move_expansion(vectors, octants, rotation, axial, prec):
    turned = turn_select(vectors, rotation, octants, False, prec)
    return turn_select(axial_apply(turned, axial, prec), rotation, octants, True, prec)


def local_boxes(
    sphere_block,
    live_count,
    cluster,
    leaf_parent,
    leaf_octant,
    box_octant,
    rotation,
    axial_one,
    axial_two,
):
    degrees, orders = (sphere_block.shape[0], sphere_block.shape[1])
    channel = sphere_block.shape[2] * sphere_block.shape[3] * sphere_block.shape[4]
    slots = sphere_block.shape[-1]
    per_block = slots // SBLK
    alive = jnp.arange(slots, dtype=jnp.int32) // per_block < live_count
    leaf_total = leaf_parent.shape[0]
    member = (
        (cluster[:, None] == jnp.arange(leaf_total, dtype=jnp.int32)[None, :]) & alive[:, None]
    ).astype(jnp.bfloat16)
    leaves = jnp.dot(
        sphere_block.reshape(degrees * orders * channel, slots),
        member,
        preferred_element_type=jnp.float32,
    ).reshape(degrees, orders, channel * leaf_total)
    moved = move_expansion(leaves, leaf_octant, rotation, axial_one, LEAF_PREC)
    box_total = box_octant.shape[0]
    parents = (leaf_parent[:, None] == jnp.arange(box_total, dtype=jnp.int32)[None, :]).astype(
        jnp.float32
    )
    boxes = jnp.dot(moved.reshape(-1, leaf_total), parents, precision=HI).reshape(
        degrees, orders, channel * box_total
    )
    outer = move_expansion(boxes, box_octant, rotation, axial_two, LEAF_PREC)
    return outer.reshape(degrees, orders, channel, box_total).sum(-1)


def owner_frame(owner_sum, owner_turn, owner_shift):
    degrees, orders, width = owner_sum.shape
    states = width // 4
    first = jnp.einsum("lqp,lpC->lqC", owner_turn[0], owner_sum, precision=HI)
    second = jnp.einsum("lqp,lpC->lqC", owner_turn[1], owner_sum, precision=HI)
    turned = complex_join(first, second, width // 2)
    moved = turned.reshape(degrees, orders, 2, 2, states)
    moved = jnp.transpose(moved, (1, 3, 0, 2, 4)).reshape(orders, 2 * degrees, 2 * states)
    root_degrees = owner_shift.shape[3]
    mats = owner_shift.reshape(2, orders, 2 * root_degrees, 2 * degrees)
    first = jnp.einsum("qab,qbC->qaC", mats[0], moved, precision=HI)
    second = jnp.einsum("qab,qbC->qaC", mats[1], moved, precision=HI)
    joined = complex_join(first, second, states).reshape(orders, 2, root_degrees, 2, states)
    framed = jnp.transpose(joined, (2, 1, 3, 4, 0)).reshape(root_degrees, 4 * states, orders)
    return framed.astype(jnp.bfloat16)


def rotate_back(framed, functions, azimuth, half_orders):
    root_degrees, width = (framed.shape[0], framed.shape[1])
    states = width // 4
    orders_here = functions.shape[2]
    values = jnp.einsum("nCm,nmj->nCj", framed, functions, preferred_element_type=jnp.float32)
    values = values.reshape(root_degrees, 2, 2, states, orders_here)
    order_values = (jnp.arange(orders_here, dtype=jnp.int32) - half_orders).astype(jnp.float32)
    cosine = jnp.cos(order_values * azimuth)
    sine = jnp.sin(order_values * azimuth)
    real_part = cosine * values[:, :, 0] + sine * values[:, :, 1]
    imag_part = cosine * values[:, :, 1] - sine * values[:, :, 0]
    joined = jnp.stack([real_part, imag_part], axis=2)
    return jnp.transpose(joined, (4, 1, 2, 3, 0)).reshape(orders_here, 4 * states * root_degrees)


def legendre_field(root_coef, table):
    orders_here, root_degrees = (table.shape[0], table.shape[1])
    lat_total = table.shape[2] // 2
    rows = root_coef.shape[1] // root_degrees
    states = rows // 4
    half = rows // 2
    blocks = jnp.einsum(
        "jrn,jnK->jrK",
        root_coef.reshape(orders_here, rows, root_degrees),
        table,
        preferred_element_type=jnp.float32,
    )
    theta_part = blocks[:, :half, :lat_total] + blocks[:, half:, lat_total:]
    cross = blocks[:, :half, lat_total:] + blocks[:, half:, :lat_total]
    phi_part = jnp.concatenate([-cross[:, states:], cross[:, :states]], axis=1)
    return jnp.concatenate([theta_part, phi_part], axis=1)


def synthesize(spectrum, longitudes):
    orders = spectrum.shape[-1]
    fine = 128
    coarse = longitudes // fine
    order_ids = jnp.arange(orders, dtype=jnp.int32) - orders // 2
    coarse_angle = jnp.mod(order_ids[:, None] * (fine * jnp.arange(coarse, dtype=jnp.int32))[None, :], longitudes)
    coarse_angle = coarse_angle.astype(jnp.float32) * (2.0 * math.pi / longitudes)
    fine_angle = jnp.mod(order_ids[:, None] * jnp.arange(fine, dtype=jnp.int32)[None, :], longitudes)
    fine_angle = fine_angle.astype(jnp.float32) * (2.0 * math.pi / longitudes)
    pc, ps = jnp.cos(coarse_angle), jnp.sin(coarse_angle)
    qc, qs = jnp.cos(fine_angle), jnp.sin(fine_angle)
    spec = spectrum.astype(jnp.float32)
    sr, si = spec[:, 0], spec[:, 1]
    vr = sr[..., None, :] * pc.T - si[..., None, :] * ps.T
    vi = sr[..., None, :] * ps.T + si[..., None, :] * pc.T
    lhs = jnp.stack([vr, vi], axis=-2)
    rhs = jnp.stack([jnp.stack([qc, qs], axis=1), jnp.stack([-qs, qc], axis=1)], axis=0)
    out = jnp.einsum("csxkam,amfb->xscfkb", lhs, rhs, precision=HI)
    out = out.reshape(out.shape[:4] + (longitudes,))
    return out * (1.0 / math.sqrt(orders))


def pair_sum(x, axis):
    if lax.axis_size(axis) != 2:
        return lax.psum(x, axis)
    return x + lax.ppermute(x, axis, [(0, 1), (1, 0)])


def pair_scatter(x, axis):
    me = lax.axis_index(axis)
    keep = jnp.where(me == 0, x[0], x[1])
    give = jnp.where(me == 0, x[1], x[0])
    got = lax.ppermute(give.astype(jnp.bfloat16), axis, [(0, 1), (1, 0)])
    return keep + got.astype(keep.dtype)


def shift_all_to_all(x, axis):
    n = lax.axis_size(axis)
    me = lax.axis_index(axis)
    rows = jnp.arange(n)
    result = jnp.zeros_like(x)
    for step in range(n):
        target = (me + step) % n
        piece = jnp.take(x, target, axis=0)
        if step:
            piece = lax.ppermute(piece, axis, [(i, (i + step) % n) for i in range(n)])
        source = (me - step) % n
        result = jnp.where((rows == source).reshape((n,) + (1,) * (x.ndim - 1)), piece[None], result)
    return result


def shift_reduce_scatter(x, axis):
    n = lax.axis_size(axis)
    me = lax.axis_index(axis)
    total = jnp.take(x, me, axis=0)
    for step in range(1, n):
        piece = jnp.take(x, (me + step) % n, axis=0).astype(jnp.bfloat16)
        piece = lax.ppermute(piece, axis, [(i, (i + step) % n) for i in range(n)])
        total = total + piece.astype(total.dtype)
    return total


def on_device(
    sphere_coef,
    live_blocks,
    cluster,
    leaf_parent,
    leaf_octant,
    box_octant,
    rotation,
    axial_one,
    axial_two,
    owner_rotation,
    owner_axial,
    owner_angle,
    turn_table,
    angular_table,
):
    partial_owner = local_boxes(
        sphere_coef,
        live_blocks[0],
        cluster,
        leaf_parent,
        leaf_octant,
        box_octant,
        rotation,
        axial_one,
        axial_two,
    )
    owner_sum = pair_sum(pair_sum(partial_owner, "sub"), "state")
    framed = owner_frame(owner_sum, owner_rotation[0], owner_axial[0])
    leaf_size = lax.axis_size("leaf")
    orders = turn_table.shape[3]
    half_orders = orders // 2
    own_orders = orders // leaf_size
    own_azimuth = owner_angle[lax.axis_index("leaf")]
    piece = turn_table[0]
    contribution = rotate_back(framed, piece, own_azimuth, half_orders)
    if leaf_size <= 4:
        root = shift_reduce_scatter(contribution.reshape((leaf_size, own_orders) + contribution.shape[1:]), "leaf")
    else:
        root = lax.psum_scatter(contribution, "leaf", scatter_dimension=0, tiled=True)
    root_coef = root.astype(jnp.bfloat16)
    field = legendre_field(root_coef, angular_table)
    channel = field.shape[1]
    group_size = lax.axis_size("state") * lax.axis_size("sub")
    lat_rows = field.shape[2] // (leaf_size * group_size)
    shaped = field.reshape(own_orders, channel, leaf_size, group_size, lat_rows)
    shaped = jnp.transpose(shaped, (3, 2, 1, 4, 0)).reshape(
        group_size, leaf_size, channel * lat_rows * own_orders
    )
    if lax.axis_size("state") == 2 and lax.axis_size("sub") == 2 and leaf_size <= 4:
        halves = shaped.reshape((2, 2) + shaped.shape[1:])
        summed = pair_scatter(pair_scatter(jnp.swapaxes(halves, 0, 1), "sub"), "state")
        moved = shift_all_to_all(summed.astype(jnp.bfloat16), "leaf")
    else:
        summed = lax.psum_scatter(shaped.astype(jnp.bfloat16), ("state", "sub"), scatter_dimension=0, tiled=True)
        moved = lax.all_to_all(summed, "leaf", split_axis=1, concat_axis=2, tiled=True)
    spectrum = moved.reshape(leaf_size, channel, lat_rows, own_orders)
    spectrum = jnp.transpose(spectrum, (1, 2, 0, 3)).reshape(2, 2, -1, lat_rows, orders)
    return synthesize(spectrum, PHI)


def solution(mesh):
    return jax.shard_map(
        on_device,
        mesh=mesh,
        in_specs=(
            P(None, None, None, None, None, ("groups", "leaf", "state", "sub")),
            P(("groups", "leaf", "state", "sub")),
            P(("groups", "leaf", "state", "sub")),
            P(("groups", "leaf", "state", "sub")),
            P(("groups", "leaf", "state", "sub")),
            P(("groups", "leaf", "state", "sub")),
            P(),
            P(),
            P(),
            P(("groups", "leaf"), None, None, None, None),
            P(("groups", "leaf"), None, None, None, ("state", "sub"), None, None),
            P("groups"),
            P(("groups", "leaf"), ("state", "sub"), None, None),
            P("leaf", ("state", "sub"), None),
        ),
        out_specs=P(("groups", "leaf", "state", "sub"), None, None, None, None),
        check_vma=False,
    )
```

```python
import math

import jax
import jax.numpy as jnp
from jax import lax
from jax.sharding import PartitionSpec as P

STATES = 4
SBLK = 4
PHI = 2048
HI = lax.Precision.HIGH
LEAF_PREC = lax.Precision.DEFAULT


def complex_join(first, second, half):
    real = first[..., :half] - second[..., half:]
    imag = first[..., half:] + second[..., :half]
    return jnp.concatenate([real, imag], axis=-1)


def turn_select(vectors, rotation, octants, backward, prec):
    degrees, orders, width = vectors.shape
    if backward:
        mats = jnp.transpose(rotation, (1, 2, 0, 4, 3))
        sign = -1.0
    else:
        mats = jnp.transpose(rotation, (1, 2, 0, 3, 4))
        sign = 1.0
    mats = mats.reshape(2, degrees, 8 * orders, orders)
    first = jnp.einsum("lQp,lpC->lQC", mats[0], vectors, precision=prec)
    second = sign * jnp.einsum("lQp,lpC->lQC", mats[1], vectors, precision=prec)
    joined = complex_join(first, second, width // 2).reshape(degrees, 8, orders, width)
    count = octants.shape[0]
    chosen = (octants[None, :] == jnp.arange(8, dtype=jnp.int32)[:, None]).astype(jnp.float32)
    column_mask = jnp.tile(chosen, (1, width // count))
    return jnp.sum(joined * column_mask[None, :, None, :], axis=1)


def axial_apply(vectors, axial, prec):
    degrees, orders, width = vectors.shape
    rest = width // 4
    moved = vectors.reshape(degrees, orders, 2, 2, rest)
    moved = jnp.transpose(moved, (1, 3, 0, 2, 4)).reshape(orders, 2 * degrees, 2 * rest)
    mats = axial.reshape(2, orders, 2 * degrees, 2 * degrees)
    first = jnp.einsum("qab,qbC->qaC", mats[0], moved, precision=prec)
    second = jnp.einsum("qab,qbC->qaC", mats[1], moved, precision=prec)
    joined = complex_join(first, second, rest).reshape(orders, 2, degrees, 2, rest)
    return jnp.transpose(joined, (2, 0, 3, 1, 4)).reshape(degrees, orders, width)


def move_expansion(vectors, octants, rotation, axial, prec):
    turned = turn_select(vectors, rotation, octants, False, prec)
    return turn_select(axial_apply(turned, axial, prec), rotation, octants, True, prec)


def local_boxes(
    sphere_block,
    live_count,
    cluster,
    leaf_parent,
    leaf_octant,
    box_octant,
    rotation,
    axial_one,
    axial_two,
):
    degrees, orders = (sphere_block.shape[0], sphere_block.shape[1])
    channel = sphere_block.shape[2] * sphere_block.shape[3] * sphere_block.shape[4]
    slots = sphere_block.shape[-1]
    per_block = slots // SBLK
    alive = jnp.arange(slots, dtype=jnp.int32) // per_block < live_count
    leaf_total = leaf_parent.shape[0]
    member = (
        (cluster[:, None] == jnp.arange(leaf_total, dtype=jnp.int32)[None, :]) & alive[:, None]
    ).astype(jnp.bfloat16)
    leaves = jnp.dot(
        sphere_block.reshape(degrees * orders * channel, slots),
        member,
        preferred_element_type=jnp.float32,
    ).reshape(degrees, orders, channel * leaf_total)
    moved = move_expansion(leaves, leaf_octant, rotation, axial_one, LEAF_PREC)
    box_total = box_octant.shape[0]
    parents = (leaf_parent[:, None] == jnp.arange(box_total, dtype=jnp.int32)[None, :]).astype(
        jnp.float32
    )
    wide_ident = jnp.eye(channel, dtype=jnp.float32)
    wide_parents = (wide_ident[:, None, :, None] * parents[None, :, None, :]).reshape(
        channel * leaf_total, channel * box_total
    )
    boxes = jnp.einsum("lpC,CD->lpD", moved, wide_parents, precision=HI)
    outer = move_expansion(boxes, box_octant, rotation, axial_two, HI)
    return outer.reshape(degrees, orders, channel, box_total).sum(-1)


def owner_frame(owner_sum, owner_turn, owner_shift):
    degrees, orders, width = owner_sum.shape
    states = width // 4
    first = jnp.einsum("lqp,lpC->lqC", owner_turn[0], owner_sum, precision=HI)
    second = jnp.einsum("lqp,lpC->lqC", owner_turn[1], owner_sum, precision=HI)
    turned = complex_join(first, second, width // 2)
    moved = turned.reshape(degrees, orders, 2, 2, states)
    moved = jnp.transpose(moved, (1, 3, 0, 2, 4)).reshape(orders, 2 * degrees, 2 * states)
    root_degrees = owner_shift.shape[3]
    mats = owner_shift.reshape(2, orders, 2 * root_degrees, 2 * degrees)
    first = jnp.einsum("qab,qbC->qaC", mats[0], moved, precision=HI)
    second = jnp.einsum("qab,qbC->qaC", mats[1], moved, precision=HI)
    joined = complex_join(first, second, states).reshape(orders, 2, root_degrees, 2, states)
    framed = jnp.transpose(joined, (2, 1, 3, 4, 0)).reshape(root_degrees, 4 * states, orders)
    return framed.astype(jnp.bfloat16)


def rotate_back(framed, functions, azimuth, half_orders):
    root_degrees, width = (framed.shape[0], framed.shape[1])
    states = width // 4
    orders_here = functions.shape[2]
    values = jnp.einsum("nCm,nmj->nCj", framed, functions, preferred_element_type=jnp.float32)
    values = values.reshape(root_degrees, 2, 2, states, orders_here)
    order_values = (jnp.arange(orders_here, dtype=jnp.int32) - half_orders).astype(jnp.float32)
    cosine = jnp.cos(order_values * azimuth)
    sine = jnp.sin(order_values * azimuth)
    real_part = cosine * values[:, :, 0] + sine * values[:, :, 1]
    imag_part = cosine * values[:, :, 1] - sine * values[:, :, 0]
    joined = jnp.stack([real_part, imag_part], axis=2)
    return jnp.transpose(joined, (4, 1, 2, 3, 0)).reshape(orders_here, 4 * states * root_degrees)


def legendre_field(root_coef, table):
    orders_here, root_degrees = (table.shape[0], table.shape[1])
    lat_total = table.shape[2] // 2
    rows = root_coef.shape[1] // root_degrees
    states = rows // 4
    half = rows // 2
    blocks = jnp.einsum(
        "jrn,jnK->jrK",
        root_coef.reshape(orders_here, rows, root_degrees),
        table,
        preferred_element_type=jnp.float32,
    )
    theta_part = blocks[:, :half, :lat_total] + blocks[:, half:, lat_total:]
    cross = blocks[:, :half, lat_total:] + blocks[:, half:, :lat_total]
    phi_part = jnp.concatenate([-cross[:, states:], cross[:, :states]], axis=1)
    return jnp.concatenate([theta_part, phi_part], axis=1)


def synthesize(spectrum, longitudes):
    orders = spectrum.shape[-1]
    fine = 128
    coarse = longitudes // fine
    order_ids = jnp.arange(orders, dtype=jnp.int32) - orders // 2
    coarse_angle = jnp.mod(order_ids[:, None] * (fine * jnp.arange(coarse, dtype=jnp.int32))[None, :], longitudes)
    coarse_angle = coarse_angle.astype(jnp.float32) * (2.0 * math.pi / longitudes)
    fine_angle = jnp.mod(order_ids[:, None] * jnp.arange(fine, dtype=jnp.int32)[None, :], longitudes)
    fine_angle = fine_angle.astype(jnp.float32) * (2.0 * math.pi / longitudes)
    pc, ps = jnp.cos(coarse_angle), jnp.sin(coarse_angle)
    qc, qs = jnp.cos(fine_angle), jnp.sin(fine_angle)
    spec = spectrum.astype(jnp.float32)
    sr, si = spec[:, 0], spec[:, 1]
    vr = sr[..., None, :] * pc.T - si[..., None, :] * ps.T
    vi = sr[..., None, :] * ps.T + si[..., None, :] * pc.T
    lhs = jnp.stack([vr, vi], axis=-2)
    rhs = jnp.stack([jnp.stack([qc, qs], axis=1), jnp.stack([-qs, qc], axis=1)], axis=0)
    out = jnp.einsum("csxkam,amfb->xscfkb", lhs, rhs, precision=HI)
    out = out.reshape(out.shape[:4] + (longitudes,))
    return out * (1.0 / math.sqrt(orders))


def pair_sum(x, axis):
    if lax.axis_size(axis) != 2:
        return lax.psum(x, axis)
    return x + lax.ppermute(x, axis, [(0, 1), (1, 0)])


def pair_scatter(x, axis):
    me = lax.axis_index(axis)
    keep = jnp.where(me == 0, x[0], x[1])
    give = jnp.where(me == 0, x[1], x[0])
    got = lax.ppermute(give.astype(jnp.bfloat16), axis, [(0, 1), (1, 0)])
    return keep + got.astype(keep.dtype)


def shift_all_to_all(x, axis):
    n = lax.axis_size(axis)
    me = lax.axis_index(axis)
    rows = jnp.arange(n)
    result = jnp.zeros_like(x)
    for step in range(n):
        target = (me + step) % n
        piece = jnp.take(x, target, axis=0)
        if step:
            piece = lax.ppermute(piece, axis, [(i, (i + step) % n) for i in range(n)])
        source = (me - step) % n
        result = jnp.where((rows == source).reshape((n,) + (1,) * (x.ndim - 1)), piece[None], result)
    return result


def shift_reduce_scatter(x, axis):
    n = lax.axis_size(axis)
    me = lax.axis_index(axis)
    total = jnp.take(x, me, axis=0)
    for step in range(1, n):
        piece = jnp.take(x, (me + step) % n, axis=0).astype(jnp.bfloat16)
        piece = lax.ppermute(piece, axis, [(i, (i + step) % n) for i in range(n)])
        total = total + piece.astype(total.dtype)
    return total


def on_device(
    sphere_coef,
    live_blocks,
    cluster,
    leaf_parent,
    leaf_octant,
    box_octant,
    rotation,
    axial_one,
    axial_two,
    owner_rotation,
    owner_axial,
    owner_angle,
    turn_table,
    angular_table,
):
    partial_owner = local_boxes(
        sphere_coef,
        live_blocks[0],
        cluster,
        leaf_parent,
        leaf_octant,
        box_octant,
        rotation,
        axial_one,
        axial_two,
    )
    owner_sum = pair_sum(pair_sum(partial_owner, "sub"), "state")
    framed = owner_frame(owner_sum, owner_rotation[0], owner_axial[0])
    leaf_size = lax.axis_size("leaf")
    orders = turn_table.shape[3]
    half_orders = orders // 2
    own_orders = orders // leaf_size
    own_azimuth = owner_angle[lax.axis_index("leaf")]
    piece = turn_table[0]
    contribution = rotate_back(framed, piece, own_azimuth, half_orders)
    if leaf_size <= 4:
        root = shift_reduce_scatter(contribution.reshape((leaf_size, own_orders) + contribution.shape[1:]), "leaf")
    else:
        root = lax.psum_scatter(contribution, "leaf", scatter_dimension=0, tiled=True)
    root_coef = root.astype(jnp.bfloat16)
    field = legendre_field(root_coef, angular_table)
    channel = field.shape[1]
    group_size = lax.axis_size("state") * lax.axis_size("sub")
    lat_rows = field.shape[2] // (leaf_size * group_size)
    shaped = field.reshape(own_orders, channel, leaf_size, group_size, lat_rows)
    shaped = jnp.transpose(shaped, (3, 2, 1, 4, 0)).reshape(
        group_size, leaf_size, channel * lat_rows * own_orders
    )
    if lax.axis_size("state") == 2 and lax.axis_size("sub") == 2 and leaf_size <= 4:
        halves = shaped.reshape((2, 2) + shaped.shape[1:])
        summed = pair_scatter(pair_scatter(jnp.swapaxes(halves, 0, 1), "sub"), "state")
        moved = shift_all_to_all(summed.astype(jnp.bfloat16), "leaf")
    else:
        summed = lax.psum_scatter(shaped.astype(jnp.bfloat16), ("state", "sub"), scatter_dimension=0, tiled=True)
        moved = lax.all_to_all(summed, "leaf", split_axis=1, concat_axis=2, tiled=True)
    spectrum = moved.reshape(leaf_size, channel, lat_rows, own_orders)
    spectrum = jnp.transpose(spectrum, (1, 2, 0, 3)).reshape(2, 2, -1, lat_rows, orders)
    return synthesize(spectrum, PHI)


def solution(mesh):
    return jax.shard_map(
        on_device,
        mesh=mesh,
        in_specs=(
            P(None, None, None, None, None, ("groups", "leaf", "state", "sub")),
            P(("groups", "leaf", "state", "sub")),
            P(("groups", "leaf", "state", "sub")),
            P(("groups", "leaf", "state", "sub")),
            P(("groups", "leaf", "state", "sub")),
            P(("groups", "leaf", "state", "sub")),
            P(),
            P(),
            P(),
            P(("groups", "leaf"), None, None, None, None),
            P(("groups", "leaf"), None, None, None, ("state", "sub"), None, None),
            P("groups"),
            P(("groups", "leaf"), ("state", "sub"), None, None),
            P("leaf", ("state", "sub"), None),
        ),
        out_specs=P(("groups", "leaf", "state", "sub"), None, None, None, None),
        check_vma=False,
    )
```

```python
import math

import jax
import jax.numpy as jnp
from jax import lax
from jax.sharding import PartitionSpec as P

STATES = 4
SBLK = 4
PHI = 2048
HI = lax.Precision.HIGH
LEAF_PREC = lax.Precision.DEFAULT


def complex_join(first, second, half):
    real = first[..., :half] - second[..., half:]
    imag = first[..., half:] + second[..., :half]
    return jnp.concatenate([real, imag], axis=-1)


def turn_select(vectors, rotation, octants, backward, prec):
    degrees, orders, width = vectors.shape
    if backward:
        mats = jnp.transpose(rotation, (2, 1, 0, 4, 3))
        sign = -1.0
    else:
        mats = jnp.transpose(rotation, (2, 1, 0, 3, 4))
        sign = 1.0
    mats = mats.reshape(degrees, 2 * 8 * orders, orders)
    both = jnp.einsum("lQp,lpC->lQC", mats, vectors, precision=prec)
    first = both[:, : 8 * orders]
    second = sign * both[:, 8 * orders :]
    joined = complex_join(first, second, width // 2).reshape(degrees, 8, orders, width)
    count = octants.shape[0]
    chosen = (octants[None, :] == jnp.arange(8, dtype=jnp.int32)[:, None]).astype(jnp.float32)
    column_mask = jnp.tile(chosen, (1, width // count))
    return jnp.sum(joined * column_mask[None, :, None, :], axis=1)


def axial_apply(vectors, axial, prec):
    degrees, orders, width = vectors.shape
    rest = width // 4
    moved = vectors.reshape(degrees, orders, 2, 2, rest)
    moved = jnp.transpose(moved, (1, 3, 0, 2, 4)).reshape(orders, 2 * degrees, 2 * rest)
    mats = jnp.swapaxes(axial.reshape(2, orders, 2 * degrees, 2 * degrees), 0, 1).reshape(orders, 4 * degrees, 2 * degrees)
    both = jnp.einsum("qab,qbC->qaC", mats, moved, precision=prec)
    first = both[:, : 2 * degrees]
    second = both[:, 2 * degrees :]
    joined = complex_join(first, second, rest).reshape(orders, 2, degrees, 2, rest)
    return jnp.transpose(joined, (2, 0, 3, 1, 4)).reshape(degrees, orders, width)


def move_expansion(vectors, octants, rotation, axial, prec):
    turned = turn_select(vectors, rotation, octants, False, prec)
    return turn_select(axial_apply(turned, axial, prec), rotation, octants, True, prec)


def local_boxes(
    sphere_block,
    live_count,
    cluster,
    leaf_parent,
    leaf_octant,
    box_octant,
    rotation,
    axial_one,
    axial_two,
):
    degrees, orders = (sphere_block.shape[0], sphere_block.shape[1])
    channel = sphere_block.shape[2] * sphere_block.shape[3] * sphere_block.shape[4]
    slots = sphere_block.shape[-1]
    per_block = slots // SBLK
    alive = jnp.arange(slots, dtype=jnp.int32) // per_block < live_count
    leaf_total = leaf_parent.shape[0]
    member = (
        (cluster[:, None] == jnp.arange(leaf_total, dtype=jnp.int32)[None, :]) & alive[:, None]
    ).astype(jnp.bfloat16)
    leaves = jnp.dot(
        sphere_block.reshape(degrees * orders * channel, slots),
        member,
        preferred_element_type=jnp.float32,
    ).reshape(degrees, orders, channel * leaf_total)
    moved = move_expansion(leaves, leaf_octant, rotation, axial_one, LEAF_PREC)
    box_total = box_octant.shape[0]
    parents = (leaf_parent[:, None] == jnp.arange(box_total, dtype=jnp.int32)[None, :]).astype(
        jnp.float32
    )
    wide_ident = jnp.eye(channel, dtype=jnp.float32)
    wide_parents = (wide_ident[:, None, :, None] * parents[None, :, None, :]).reshape(
        channel * leaf_total, channel * box_total
    )
    boxes = jnp.einsum("lpC,CD->lpD", moved, wide_parents, precision=HI)
    outer = move_expansion(boxes, box_octant, rotation, axial_two, LEAF_PREC)
    return outer.reshape(degrees, orders, channel, box_total).sum(-1)


def owner_frame(owner_sum, owner_turn, owner_shift):
    degrees, orders, width = owner_sum.shape
    states = width // 4
    first = jnp.einsum("lqp,lpC->lqC", owner_turn[0], owner_sum, precision=HI)
    second = jnp.einsum("lqp,lpC->lqC", owner_turn[1], owner_sum, precision=HI)
    turned = complex_join(first, second, width // 2)
    moved = turned.reshape(degrees, orders, 2, 2, states)
    moved = jnp.transpose(moved, (1, 3, 0, 2, 4)).reshape(orders, 2 * degrees, 2 * states)
    root_degrees = owner_shift.shape[3]
    mats = owner_shift.reshape(2, orders, 2 * root_degrees, 2 * degrees)
    first = jnp.einsum("qab,qbC->qaC", mats[0], moved, precision=HI)
    second = jnp.einsum("qab,qbC->qaC", mats[1], moved, precision=HI)
    joined = complex_join(first, second, states).reshape(orders, 2, root_degrees, 2, states)
    framed = jnp.transpose(joined, (2, 1, 3, 4, 0)).reshape(root_degrees, 4 * states, orders)
    return framed.astype(jnp.bfloat16)


def rotate_back(framed, functions, azimuth, half_orders):
    root_degrees, width = (framed.shape[0], framed.shape[1])
    states = width // 4
    orders_here = functions.shape[2]
    values = jnp.einsum("nCm,nmj->nCj", framed, functions, preferred_element_type=jnp.float32)
    values = values.reshape(root_degrees, 2, 2, states, orders_here)
    order_values = (jnp.arange(orders_here, dtype=jnp.int32) - half_orders).astype(jnp.float32)
    cosine = jnp.cos(order_values * azimuth)
    sine = jnp.sin(order_values * azimuth)
    real_part = cosine * values[:, :, 0] + sine * values[:, :, 1]
    imag_part = cosine * values[:, :, 1] - sine * values[:, :, 0]
    joined = jnp.stack([real_part, imag_part], axis=2)
    return jnp.transpose(joined, (4, 1, 2, 3, 0)).reshape(orders_here, 4 * states * root_degrees)


def legendre_field(root_coef, table):
    orders_here, root_degrees = (table.shape[0], table.shape[1])
    lat_total = table.shape[2] // 2
    rows = root_coef.shape[1] // root_degrees
    states = rows // 4
    half = rows // 2
    blocks = jnp.einsum(
        "jrn,jnK->jrK",
        root_coef.reshape(orders_here, rows, root_degrees),
        table,
        preferred_element_type=jnp.float32,
    )
    theta_part = blocks[:, :half, :lat_total] + blocks[:, half:, lat_total:]
    cross = blocks[:, :half, lat_total:] + blocks[:, half:, :lat_total]
    phi_part = jnp.concatenate([-cross[:, states:], cross[:, :states]], axis=1)
    return jnp.concatenate([theta_part, phi_part], axis=1)


def synthesize(spectrum, longitudes):
    orders = spectrum.shape[-1]
    fine = 128
    coarse = longitudes // fine
    order_ids = jnp.arange(orders, dtype=jnp.int32) - orders // 2
    coarse_angle = jnp.mod(order_ids[:, None] * (fine * jnp.arange(coarse, dtype=jnp.int32))[None, :], longitudes)
    coarse_angle = coarse_angle.astype(jnp.float32) * (2.0 * math.pi / longitudes)
    fine_angle = jnp.mod(order_ids[:, None] * jnp.arange(fine, dtype=jnp.int32)[None, :], longitudes)
    fine_angle = fine_angle.astype(jnp.float32) * (2.0 * math.pi / longitudes)
    pc, ps = jnp.cos(coarse_angle), jnp.sin(coarse_angle)
    qc, qs = jnp.cos(fine_angle), jnp.sin(fine_angle)
    spec = spectrum.astype(jnp.float32)
    sr, si = spec[:, 0], spec[:, 1]
    vr = sr[..., None, :] * pc.T - si[..., None, :] * ps.T
    vi = sr[..., None, :] * ps.T + si[..., None, :] * pc.T
    lhs = jnp.stack([vr, vi], axis=-2)
    rhs = jnp.stack([jnp.stack([qc, qs], axis=1), jnp.stack([-qs, qc], axis=1)], axis=0)
    out = jnp.einsum("csxkam,amfb->xscfkb", lhs, rhs, precision=HI)
    out = out.reshape(out.shape[:4] + (longitudes,))
    return out * (1.0 / math.sqrt(orders))


def pair_sum(x, axis):
    if lax.axis_size(axis) != 2:
        return lax.psum(x, axis)
    return x + lax.ppermute(x, axis, [(0, 1), (1, 0)])


def pair_scatter(x, axis):
    me = lax.axis_index(axis)
    keep = jnp.where(me == 0, x[0], x[1])
    give = jnp.where(me == 0, x[1], x[0])
    got = lax.ppermute(give.astype(jnp.bfloat16), axis, [(0, 1), (1, 0)])
    return keep + got.astype(keep.dtype)


def shift_all_to_all(x, axis):
    n = lax.axis_size(axis)
    me = lax.axis_index(axis)
    rows = jnp.arange(n)
    result = jnp.zeros_like(x)
    for step in range(n):
        target = (me + step) % n
        piece = jnp.take(x, target, axis=0)
        if step:
            piece = lax.ppermute(piece, axis, [(i, (i + step) % n) for i in range(n)])
        source = (me - step) % n
        result = jnp.where((rows == source).reshape((n,) + (1,) * (x.ndim - 1)), piece[None], result)
    return result


def shift_reduce_scatter(x, axis):
    n = lax.axis_size(axis)
    me = lax.axis_index(axis)
    total = jnp.take(x, me, axis=0)
    for step in range(1, n):
        piece = jnp.take(x, (me + step) % n, axis=0).astype(jnp.bfloat16)
        piece = lax.ppermute(piece, axis, [(i, (i + step) % n) for i in range(n)])
        total = total + piece.astype(total.dtype)
    return total


def on_device(
    sphere_coef,
    live_blocks,
    cluster,
    leaf_parent,
    leaf_octant,
    box_octant,
    rotation,
    axial_one,
    axial_two,
    owner_rotation,
    owner_axial,
    owner_angle,
    turn_table,
    angular_table,
):
    partial_owner = local_boxes(
        sphere_coef,
        live_blocks[0],
        cluster,
        leaf_parent,
        leaf_octant,
        box_octant,
        rotation,
        axial_one,
        axial_two,
    )
    owner_sum = pair_sum(pair_sum(partial_owner, "sub"), "state")
    framed = owner_frame(owner_sum, owner_rotation[0], owner_axial[0])
    leaf_size = lax.axis_size("leaf")
    orders = turn_table.shape[3]
    half_orders = orders // 2
    own_orders = orders // leaf_size
    own_azimuth = owner_angle[lax.axis_index("leaf")]
    piece = turn_table[0]
    contribution = rotate_back(framed, piece, own_azimuth, half_orders)
    if leaf_size <= 4:
        root = shift_reduce_scatter(contribution.reshape((leaf_size, own_orders) + contribution.shape[1:]), "leaf")
    else:
        root = lax.psum_scatter(contribution, "leaf", scatter_dimension=0, tiled=True)
    root_coef = root.astype(jnp.bfloat16)
    field = legendre_field(root_coef, angular_table)
    channel = field.shape[1]
    group_size = lax.axis_size("state") * lax.axis_size("sub")
    lat_rows = field.shape[2] // (leaf_size * group_size)
    shaped = field.reshape(own_orders, channel, leaf_size, group_size, lat_rows)
    shaped = jnp.transpose(shaped, (3, 2, 1, 4, 0)).reshape(
        group_size, leaf_size, channel * lat_rows * own_orders
    )
    if lax.axis_size("state") == 2 and lax.axis_size("sub") == 2 and leaf_size <= 4:
        halves = shaped.reshape((2, 2) + shaped.shape[1:])
        summed = pair_scatter(pair_scatter(jnp.swapaxes(halves, 0, 1), "sub"), "state")
        moved = shift_all_to_all(summed.astype(jnp.bfloat16), "leaf")
    else:
        summed = lax.psum_scatter(shaped.astype(jnp.bfloat16), ("state", "sub"), scatter_dimension=0, tiled=True)
        moved = lax.all_to_all(summed, "leaf", split_axis=1, concat_axis=2, tiled=True)
    spectrum = moved.reshape(leaf_size, channel, lat_rows, own_orders)
    spectrum = jnp.transpose(spectrum, (1, 2, 0, 3)).reshape(2, 2, -1, lat_rows, orders)
    return synthesize(spectrum, PHI)


def solution(mesh):
    return jax.shard_map(
        on_device,
        mesh=mesh,
        in_specs=(
            P(None, None, None, None, None, ("groups", "leaf", "state", "sub")),
            P(("groups", "leaf", "state", "sub")),
            P(("groups", "leaf", "state", "sub")),
            P(("groups", "leaf", "state", "sub")),
            P(("groups", "leaf", "state", "sub")),
            P(("groups", "leaf", "state", "sub")),
            P(),
            P(),
            P(),
            P(("groups", "leaf"), None, None, None, None),
            P(("groups", "leaf"), None, None, None, ("state", "sub"), None, None),
            P("groups"),
            P(("groups", "leaf"), ("state", "sub"), None, None),
            P("leaf", ("state", "sub"), None),
        ),
        out_specs=P(("groups", "leaf", "state", "sub"), None, None, None, None),
        check_vma=False,
    )
```

```python
import math

import jax
import jax.numpy as jnp
from jax import lax
from jax.sharding import PartitionSpec as P

STATES = 4
SBLK = 4
PHI = 2048
HI = lax.Precision.HIGH
LEAF_PREC = lax.Precision.DEFAULT


def complex_join(first, second, half):
    real = first[..., :half] - second[..., half:]
    imag = first[..., half:] + second[..., :half]
    return jnp.concatenate([real, imag], axis=-1)


def turn_select(vectors, rotation, octants, backward, prec):
    degrees, orders, width = vectors.shape
    if backward:
        mats = jnp.transpose(rotation, (2, 1, 0, 4, 3))
        sign = -1.0
    else:
        mats = jnp.transpose(rotation, (2, 1, 0, 3, 4))
        sign = 1.0
    mats = mats.reshape(degrees, 2 * 8 * orders, orders)
    both = jnp.einsum("lQp,lpC->lQC", mats, vectors, precision=prec)
    first = both[:, : 8 * orders]
    second = sign * both[:, 8 * orders :]
    joined = complex_join(first, second, width // 2).reshape(degrees, 8, orders, width)
    count = octants.shape[0]
    chosen = (octants[None, :] == jnp.arange(8, dtype=jnp.int32)[:, None]).astype(jnp.float32)
    column_mask = jnp.tile(chosen, (1, width // count))
    return jnp.sum(joined * column_mask[None, :, None, :], axis=1)


def axial_apply(vectors, axial, prec):
    degrees, orders, width = vectors.shape
    rest = width // 4
    moved = vectors.reshape(degrees, orders, 2, 2, rest)
    moved = jnp.transpose(moved, (1, 3, 0, 2, 4)).reshape(orders, 2 * degrees, 2 * rest)
    mats = jnp.swapaxes(axial.reshape(2, orders, 2 * degrees, 2 * degrees), 0, 1).reshape(orders, 4 * degrees, 2 * degrees)
    both = jnp.einsum("qab,qbC->qaC", mats, moved, precision=prec)
    first = both[:, : 2 * degrees]
    second = both[:, 2 * degrees :]
    joined = complex_join(first, second, rest).reshape(orders, 2, degrees, 2, rest)
    return jnp.transpose(joined, (2, 0, 3, 1, 4)).reshape(degrees, orders, width)


def move_expansion(vectors, octants, rotation, axial, prec):
    turned = turn_select(vectors, rotation, octants, False, prec)
    return turn_select(axial_apply(turned, axial, prec), rotation, octants, True, prec)


def local_boxes(
    sphere_block,
    live_count,
    cluster,
    leaf_parent,
    leaf_octant,
    box_octant,
    rotation,
    axial_one,
    axial_two,
):
    degrees, orders = (sphere_block.shape[0], sphere_block.shape[1])
    channel = sphere_block.shape[2] * sphere_block.shape[3] * sphere_block.shape[4]
    slots = sphere_block.shape[-1]
    per_block = slots // SBLK
    alive = jnp.arange(slots, dtype=jnp.int32) // per_block < live_count
    leaf_total = leaf_parent.shape[0]
    member = (
        (cluster[:, None] == jnp.arange(leaf_total, dtype=jnp.int32)[None, :]) & alive[:, None]
    ).astype(jnp.bfloat16)
    leaves = jnp.dot(
        sphere_block.reshape(degrees * orders * channel, slots),
        member,
        preferred_element_type=jnp.float32,
    ).reshape(degrees, orders, channel * leaf_total)
    moved = move_expansion(leaves, leaf_octant, rotation, axial_one, LEAF_PREC)
    box_total = box_octant.shape[0]
    parents = (leaf_parent[:, None] == jnp.arange(box_total, dtype=jnp.int32)[None, :]).astype(
        jnp.float32
    )
    wide_ident = jnp.eye(channel, dtype=jnp.float32)
    wide_parents = (wide_ident[:, None, :, None] * parents[None, :, None, :]).reshape(
        channel * leaf_total, channel * box_total
    )
    boxes = jnp.einsum("lpC,CD->lpD", moved, wide_parents, precision=HI)
    outer = move_expansion(boxes, box_octant, rotation, axial_two, LEAF_PREC)
    return outer.reshape(degrees, orders, channel, box_total).sum(-1)


def owner_frame(owner_sum, owner_turn, owner_shift):
    degrees, orders, width = owner_sum.shape
    states = width // 4
    turns = jnp.swapaxes(owner_turn, 0, 1).reshape(degrees, 2 * orders, orders)
    both = jnp.einsum("lqp,lpC->lqC", turns, owner_sum, precision=HI)
    first = both[:, :orders]
    second = both[:, orders:]
    turned = complex_join(first, second, width // 2)
    moved = turned.reshape(degrees, orders, 2, 2, states)
    moved = jnp.transpose(moved, (1, 3, 0, 2, 4)).reshape(orders, 2 * degrees, 2 * states)
    root_degrees = owner_shift.shape[3]
    mats = owner_shift.reshape(2, orders, 2 * root_degrees, 2 * degrees)
    mats = jnp.swapaxes(mats, 0, 1).reshape(orders, 4 * root_degrees, 2 * degrees)
    both = jnp.einsum("qab,qbC->qaC", mats, moved, precision=HI)
    first = both[:, : 2 * root_degrees]
    second = both[:, 2 * root_degrees :]
    joined = complex_join(first, second, states).reshape(orders, 2, root_degrees, 2, states)
    framed = jnp.transpose(joined, (2, 1, 3, 4, 0)).reshape(root_degrees, 4 * states, orders)
    return framed.astype(jnp.bfloat16)


def rotate_back(framed, functions, azimuth, half_orders):
    root_degrees, width = (framed.shape[0], framed.shape[1])
    states = width // 4
    orders_here = functions.shape[2]
    values = jnp.einsum("nCm,nmj->nCj", framed, functions, preferred_element_type=jnp.float32)
    values = values.reshape(root_degrees, 2, 2, states, orders_here)
    order_values = (jnp.arange(orders_here, dtype=jnp.int32) - half_orders).astype(jnp.float32)
    cosine = jnp.cos(order_values * azimuth)
    sine = jnp.sin(order_values * azimuth)
    real_part = cosine * values[:, :, 0] + sine * values[:, :, 1]
    imag_part = cosine * values[:, :, 1] - sine * values[:, :, 0]
    joined = jnp.stack([real_part, imag_part], axis=2)
    return jnp.transpose(joined, (4, 1, 2, 3, 0)).reshape(orders_here, 4 * states * root_degrees)


def legendre_field(root_coef, table):
    orders_here, root_degrees = (table.shape[0], table.shape[1])
    lat_total = table.shape[2] // 2
    rows = root_coef.shape[1] // root_degrees
    states = rows // 4
    half = rows // 2
    blocks = jnp.einsum(
        "jrn,jnK->jrK",
        root_coef.reshape(orders_here, rows, root_degrees),
        table,
        preferred_element_type=jnp.float32,
    )
    theta_part = blocks[:, :half, :lat_total] + blocks[:, half:, lat_total:]
    cross = blocks[:, :half, lat_total:] + blocks[:, half:, :lat_total]
    phi_part = jnp.concatenate([-cross[:, states:], cross[:, :states]], axis=1)
    return jnp.concatenate([theta_part, phi_part], axis=1)


def synthesize(spectrum, longitudes):
    orders = spectrum.shape[-1]
    fine = 128
    coarse = longitudes // fine
    order_ids = jnp.arange(orders, dtype=jnp.int32) - orders // 2
    coarse_angle = jnp.mod(order_ids[:, None] * (fine * jnp.arange(coarse, dtype=jnp.int32))[None, :], longitudes)
    coarse_angle = coarse_angle.astype(jnp.float32) * (2.0 * math.pi / longitudes)
    fine_angle = jnp.mod(order_ids[:, None] * jnp.arange(fine, dtype=jnp.int32)[None, :], longitudes)
    fine_angle = fine_angle.astype(jnp.float32) * (2.0 * math.pi / longitudes)
    pc, ps = jnp.cos(coarse_angle), jnp.sin(coarse_angle)
    qc, qs = jnp.cos(fine_angle), jnp.sin(fine_angle)
    spec = spectrum.astype(jnp.float32)
    sr, si = spec[:, 0], spec[:, 1]
    vr = sr[..., None, :] * pc.T - si[..., None, :] * ps.T
    vi = sr[..., None, :] * ps.T + si[..., None, :] * pc.T
    lhs = jnp.stack([vr, vi], axis=-2)
    rhs = jnp.stack([jnp.stack([qc, qs], axis=1), jnp.stack([-qs, qc], axis=1)], axis=0)
    out = jnp.einsum("csxkam,amfb->xscfkb", lhs, rhs, precision=HI)
    out = out.reshape(out.shape[:4] + (longitudes,))
    return out * (1.0 / math.sqrt(orders))


def pair_sum(x, axis):
    if lax.axis_size(axis) != 2:
        return lax.psum(x, axis)
    return x + lax.ppermute(x, axis, [(0, 1), (1, 0)])


def pair_scatter(x, axis):
    me = lax.axis_index(axis)
    keep = jnp.where(me == 0, x[0], x[1])
    give = jnp.where(me == 0, x[1], x[0])
    got = lax.ppermute(give.astype(jnp.bfloat16), axis, [(0, 1), (1, 0)])
    return keep + got.astype(keep.dtype)


def shift_all_to_all(x, axis):
    n = lax.axis_size(axis)
    me = lax.axis_index(axis)
    rows = jnp.arange(n)
    result = jnp.zeros_like(x)
    for step in range(n):
        target = (me + step) % n
        piece = jnp.take(x, target, axis=0)
        if step:
            piece = lax.ppermute(piece, axis, [(i, (i + step) % n) for i in range(n)])
        source = (me - step) % n
        result = jnp.where((rows == source).reshape((n,) + (1,) * (x.ndim - 1)), piece[None], result)
    return result


def shift_reduce_scatter(x, axis):
    n = lax.axis_size(axis)
    me = lax.axis_index(axis)
    total = jnp.take(x, me, axis=0)
    for step in range(1, n):
        piece = jnp.take(x, (me + step) % n, axis=0).astype(jnp.bfloat16)
        piece = lax.ppermute(piece, axis, [(i, (i + step) % n) for i in range(n)])
        total = total + piece.astype(total.dtype)
    return total


def on_device(
    sphere_coef,
    live_blocks,
    cluster,
    leaf_parent,
    leaf_octant,
    box_octant,
    rotation,
    axial_one,
    axial_two,
    owner_rotation,
    owner_axial,
    owner_angle,
    turn_table,
    angular_table,
):
    partial_owner = local_boxes(
        sphere_coef,
        live_blocks[0],
        cluster,
        leaf_parent,
        leaf_octant,
        box_octant,
        rotation,
        axial_one,
        axial_two,
    )
    owner_sum = pair_sum(pair_sum(partial_owner, "sub"), "state")
    framed = owner_frame(owner_sum, owner_rotation[0], owner_axial[0])
    leaf_size = lax.axis_size("leaf")
    orders = turn_table.shape[3]
    half_orders = orders // 2
    own_orders = orders // leaf_size
    own_azimuth = owner_angle[lax.axis_index("leaf")]
    piece = turn_table[0]
    contribution = rotate_back(framed, piece, own_azimuth, half_orders)
    if leaf_size <= 4:
        root = shift_reduce_scatter(contribution.reshape((leaf_size, own_orders) + contribution.shape[1:]), "leaf")
    else:
        root = lax.psum_scatter(contribution, "leaf", scatter_dimension=0, tiled=True)
    root_coef = root.astype(jnp.bfloat16)
    field = legendre_field(root_coef, angular_table)
    channel = field.shape[1]
    group_size = lax.axis_size("state") * lax.axis_size("sub")
    lat_rows = field.shape[2] // (leaf_size * group_size)
    shaped = field.reshape(own_orders, channel, leaf_size, group_size, lat_rows)
    shaped = jnp.transpose(shaped, (3, 2, 1, 4, 0)).reshape(
        group_size, leaf_size, channel * lat_rows * own_orders
    )
    if lax.axis_size("state") == 2 and lax.axis_size("sub") == 2 and leaf_size <= 4:
        halves = shaped.reshape((2, 2) + shaped.shape[1:])
        summed = pair_scatter(pair_scatter(jnp.swapaxes(halves, 0, 1), "sub"), "state")
        moved = shift_all_to_all(summed.astype(jnp.bfloat16), "leaf")
    else:
        summed = lax.psum_scatter(shaped.astype(jnp.bfloat16), ("state", "sub"), scatter_dimension=0, tiled=True)
        moved = lax.all_to_all(summed, "leaf", split_axis=1, concat_axis=2, tiled=True)
    spectrum = moved.reshape(leaf_size, channel, lat_rows, own_orders)
    spectrum = jnp.transpose(spectrum, (1, 2, 0, 3)).reshape(2, 2, -1, lat_rows, orders)
    return synthesize(spectrum, PHI)


def solution(mesh):
    return jax.shard_map(
        on_device,
        mesh=mesh,
        in_specs=(
            P(None, None, None, None, None, ("groups", "leaf", "state", "sub")),
            P(("groups", "leaf", "state", "sub")),
            P(("groups", "leaf", "state", "sub")),
            P(("groups", "leaf", "state", "sub")),
            P(("groups", "leaf", "state", "sub")),
            P(("groups", "leaf", "state", "sub")),
            P(),
            P(),
            P(),
            P(("groups", "leaf"), None, None, None, None),
            P(("groups", "leaf"), None, None, None, ("state", "sub"), None, None),
            P("groups"),
            P(("groups", "leaf"), ("state", "sub"), None, None),
            P("leaf", ("state", "sub"), None),
        ),
        out_specs=P(("groups", "leaf", "state", "sub"), None, None, None, None),
        check_vma=False,
    )
```

```python
import math

import jax
import jax.numpy as jnp
from jax import lax
from jax.sharding import PartitionSpec as P

STATES = 4
SBLK = 4
PHI = 2048
HI = lax.Precision.HIGH
LEAF_PREC = lax.Precision.DEFAULT


def complex_join(first, second, half):
    real = first[..., :half] - second[..., half:]
    imag = first[..., half:] + second[..., :half]
    return jnp.concatenate([real, imag], axis=-1)


def turn_select(vectors, rotation, octants, backward, prec):
    degrees, orders, width = vectors.shape
    if backward:
        mats = jnp.transpose(rotation, (2, 1, 0, 4, 3))
        sign = -1.0
    else:
        mats = jnp.transpose(rotation, (2, 1, 0, 3, 4))
        sign = 1.0
    mats = mats.reshape(degrees, 2 * 8 * orders, orders)
    both = jnp.einsum("lQp,lpC->lQC", mats, vectors, precision=prec)
    first = both[:, : 8 * orders]
    second = sign * both[:, 8 * orders :]
    joined = complex_join(first, second, width // 2).reshape(degrees, 8, orders, width)
    count = octants.shape[0]
    chosen = (octants[None, :] == jnp.arange(8, dtype=jnp.int32)[:, None]).astype(jnp.float32)
    column_mask = jnp.tile(chosen, (1, width // count))
    return jnp.sum(joined * column_mask[None, :, None, :], axis=1)


def axial_apply(vectors, axial, prec):
    degrees, orders, width = vectors.shape
    rest = width // 4
    moved = vectors.reshape(degrees, orders, 2, 2, rest)
    moved = jnp.transpose(moved, (1, 3, 0, 2, 4)).reshape(orders, 2 * degrees, 2 * rest)
    mats = jnp.swapaxes(axial.reshape(2, orders, 2 * degrees, 2 * degrees), 0, 1).reshape(orders, 4 * degrees, 2 * degrees)
    both = jnp.einsum("qab,qbC->qaC", mats, moved, precision=prec)
    first = both[:, : 2 * degrees]
    second = both[:, 2 * degrees :]
    joined = complex_join(first, second, rest).reshape(orders, 2, degrees, 2, rest)
    return jnp.transpose(joined, (2, 0, 3, 1, 4)).reshape(degrees, orders, width)


def move_expansion(vectors, octants, rotation, axial, prec):
    turned = turn_select(vectors, rotation, octants, False, prec)
    return turn_select(axial_apply(turned, axial, prec), rotation, octants, True, prec)


def local_boxes(
    sphere_block,
    live_count,
    cluster,
    leaf_parent,
    leaf_octant,
    box_octant,
    rotation,
    axial_one,
    axial_two,
):
    degrees, orders = (sphere_block.shape[0], sphere_block.shape[1])
    channel = sphere_block.shape[2] * sphere_block.shape[3] * sphere_block.shape[4]
    slots = sphere_block.shape[-1]
    per_block = slots // SBLK
    alive = jnp.arange(slots, dtype=jnp.int32) // per_block < live_count
    leaf_total = leaf_parent.shape[0]
    member = (
        (cluster[:, None] == jnp.arange(leaf_total, dtype=jnp.int32)[None, :]) & alive[:, None]
    ).astype(jnp.bfloat16)
    leaves = jnp.dot(
        sphere_block.reshape(degrees * orders * channel, slots),
        member,
        preferred_element_type=jnp.float32,
    ).reshape(degrees, orders, channel * leaf_total)
    moved = move_expansion(leaves, leaf_octant, rotation, axial_one, LEAF_PREC)
    box_total = box_octant.shape[0]
    parents = (leaf_parent[:, None] == jnp.arange(box_total, dtype=jnp.int32)[None, :]).astype(
        jnp.float32
    )
    wide_ident = jnp.eye(channel, dtype=jnp.float32)
    wide_parents = (wide_ident[:, None, :, None] * parents[None, :, None, :]).reshape(
        channel * leaf_total, channel * box_total
    )
    boxes = jnp.einsum("lpC,CD->lpD", moved, wide_parents, precision=HI)
    outer = move_expansion(boxes, box_octant, rotation, axial_two, LEAF_PREC)
    return outer.reshape(degrees, orders, channel, box_total).sum(-1)


def owner_frame(owner_sum, owner_turn, owner_shift):
    degrees, orders, width = owner_sum.shape
    states = width // 4
    turns = jnp.swapaxes(owner_turn, 0, 1).reshape(degrees, 2 * orders, orders)
    both = jnp.einsum("lqp,lpC->lqC", turns, owner_sum, precision=HI)
    first = both[:, :orders]
    second = both[:, orders:]
    turned = complex_join(first, second, width // 2)
    moved = turned.reshape(degrees, orders, 2, 2, states)
    moved = jnp.transpose(moved, (1, 3, 0, 2, 4)).reshape(orders, 2 * degrees, 2 * states)
    root_degrees = owner_shift.shape[3]
    mats = owner_shift.reshape(2, orders, 2 * root_degrees, 2 * degrees)
    mats = jnp.swapaxes(mats, 0, 1).reshape(orders, 4 * root_degrees, 2 * degrees)
    both = jnp.einsum("qab,qbC->qaC", mats, moved, precision=HI)
    first = both[:, : 2 * root_degrees]
    second = both[:, 2 * root_degrees :]
    joined = complex_join(first, second, states).reshape(orders, 2, root_degrees, 2, states)
    framed = jnp.transpose(joined, (2, 1, 3, 4, 0)).reshape(root_degrees, 4 * states, orders)
    return framed.astype(jnp.bfloat16)


def rotate_back(framed, functions, azimuth, half_orders):
    root_degrees, width = (framed.shape[0], framed.shape[1])
    states = width // 4
    orders_here = functions.shape[2]
    values = jnp.einsum("nCm,nmj->nCj", framed, functions, preferred_element_type=jnp.float32)
    values = values.reshape(root_degrees, 2, 2, states, orders_here)
    order_values = (jnp.arange(orders_here, dtype=jnp.int32) - half_orders).astype(jnp.float32)
    cosine = jnp.cos(order_values * azimuth)
    sine = jnp.sin(order_values * azimuth)
    real_part = cosine * values[:, :, 0] + sine * values[:, :, 1]
    imag_part = cosine * values[:, :, 1] - sine * values[:, :, 0]
    joined = jnp.stack([real_part, imag_part], axis=2)
    return jnp.transpose(joined, (4, 1, 2, 3, 0)).reshape(orders_here, 4 * states * root_degrees)


def legendre_field(root_coef, table):
    orders_here, root_degrees = (table.shape[0], table.shape[1])
    lat_total = table.shape[2] // 2
    rows = root_coef.shape[1] // root_degrees
    states = rows // 4
    half = rows // 2
    blocks = jnp.einsum(
        "jrn,jnK->jrK",
        root_coef.reshape(orders_here, rows, root_degrees),
        table,
        preferred_element_type=jnp.float32,
    )
    theta_part = blocks[:, :half, :lat_total] + blocks[:, half:, lat_total:]
    cross = blocks[:, :half, lat_total:] + blocks[:, half:, :lat_total]
    phi_part = jnp.concatenate([-cross[:, states:], cross[:, :states]], axis=1)
    return jnp.concatenate([theta_part, phi_part], axis=1)


def synthesize(spectrum, longitudes):
    orders = spectrum.shape[-1]
    fine = 128
    coarse = longitudes // fine
    order_ids = jnp.arange(orders, dtype=jnp.int32) - orders // 2
    coarse_angle = jnp.mod(order_ids[:, None] * (fine * jnp.arange(coarse, dtype=jnp.int32))[None, :], longitudes)
    coarse_angle = coarse_angle.astype(jnp.float32) * (2.0 * math.pi / longitudes)
    fine_angle = jnp.mod(order_ids[:, None] * jnp.arange(fine, dtype=jnp.int32)[None, :], longitudes)
    fine_angle = fine_angle.astype(jnp.float32) * (2.0 * math.pi / longitudes)
    pc, ps = jnp.cos(coarse_angle), jnp.sin(coarse_angle)
    qc, qs = jnp.cos(fine_angle), jnp.sin(fine_angle)
    spec = spectrum.astype(jnp.float32)
    sr, si = spec[:, 0], spec[:, 1]
    vr = sr[..., None, :] * pc.T - si[..., None, :] * ps.T
    vi = sr[..., None, :] * ps.T + si[..., None, :] * pc.T
    lhs = jnp.stack([vr, vi], axis=-2)
    rhs = jnp.stack([jnp.stack([qc, qs], axis=1), jnp.stack([-qs, qc], axis=1)], axis=0)
    out = jnp.einsum("csxkam,amfb->xscfkb", lhs, rhs, precision=HI)
    out = out.reshape(out.shape[:4] + (longitudes,))
    return out * (1.0 / math.sqrt(orders))


def pair_sum(x, axis):
    if lax.axis_size(axis) != 2:
        return lax.psum(x, axis)
    return x + lax.ppermute(x, axis, [(0, 1), (1, 0)])


def pair_scatter(x, axis):
    me = lax.axis_index(axis)
    keep = jnp.where(me == 0, x[0], x[1])
    give = jnp.where(me == 0, x[1], x[0])
    got = lax.ppermute(give.astype(jnp.bfloat16), axis, [(0, 1), (1, 0)])
    return keep + got.astype(keep.dtype)


def rolled_blocks(x, start):
    n = x.shape[0]
    return lax.dynamic_slice_in_dim(jnp.concatenate([x, x], axis=0), start % n, n, axis=0)


def shift_all_to_all(x, axis):
    n = lax.axis_size(axis)
    me = lax.axis_index(axis)
    sends = rolled_blocks(x, me)
    got = [sends[0]]
    for step in range(1, n):
        got.append(lax.ppermute(sends[step], axis, [(i, (i + step) % n) for i in range(n)]))
    ahead = jnp.stack([got[(n - k) % n] for k in range(n)], axis=0)
    return rolled_blocks(ahead, n - me)


def shift_reduce_scatter(x, axis):
    n = lax.axis_size(axis)
    me = lax.axis_index(axis)
    sends = rolled_blocks(x, me)
    total = sends[0]
    for step in range(1, n):
        piece = lax.ppermute(sends[step].astype(jnp.bfloat16), axis, [(i, (i + step) % n) for i in range(n)])
        total = total + piece.astype(total.dtype)
    return total


def on_device(
    sphere_coef,
    live_blocks,
    cluster,
    leaf_parent,
    leaf_octant,
    box_octant,
    rotation,
    axial_one,
    axial_two,
    owner_rotation,
    owner_axial,
    owner_angle,
    turn_table,
    angular_table,
):
    partial_owner = local_boxes(
        sphere_coef,
        live_blocks[0],
        cluster,
        leaf_parent,
        leaf_octant,
        box_octant,
        rotation,
        axial_one,
        axial_two,
    )
    owner_sum = pair_sum(pair_sum(partial_owner, "sub"), "state")
    framed = owner_frame(owner_sum, owner_rotation[0], owner_axial[0])
    leaf_size = lax.axis_size("leaf")
    orders = turn_table.shape[3]
    half_orders = orders // 2
    own_orders = orders // leaf_size
    own_azimuth = owner_angle[lax.axis_index("leaf")]
    piece = turn_table[0]
    contribution = rotate_back(framed, piece, own_azimuth, half_orders)
    if leaf_size <= 4:
        root = shift_reduce_scatter(contribution.reshape((leaf_size, own_orders) + contribution.shape[1:]), "leaf")
    else:
        root = lax.psum_scatter(contribution, "leaf", scatter_dimension=0, tiled=True)
    root_coef = root.astype(jnp.bfloat16)
    field = legendre_field(root_coef, angular_table)
    channel = field.shape[1]
    group_size = lax.axis_size("state") * lax.axis_size("sub")
    lat_rows = field.shape[2] // (leaf_size * group_size)
    shaped = field.reshape(own_orders, channel, leaf_size, group_size, lat_rows)
    shaped = jnp.transpose(shaped, (3, 2, 1, 4, 0)).reshape(
        group_size, leaf_size, channel * lat_rows * own_orders
    )
    if lax.axis_size("state") == 2 and lax.axis_size("sub") == 2 and leaf_size <= 4:
        halves = shaped.reshape((2, 2) + shaped.shape[1:])
        summed = pair_scatter(pair_scatter(jnp.swapaxes(halves, 0, 1), "sub"), "state")
        moved = shift_all_to_all(summed.astype(jnp.bfloat16), "leaf")
    else:
        summed = lax.psum_scatter(shaped.astype(jnp.bfloat16), ("state", "sub"), scatter_dimension=0, tiled=True)
        moved = lax.all_to_all(summed, "leaf", split_axis=1, concat_axis=2, tiled=True)
    spectrum = moved.reshape(leaf_size, channel, lat_rows, own_orders)
    spectrum = jnp.transpose(spectrum, (1, 2, 0, 3)).reshape(2, 2, -1, lat_rows, orders)
    return synthesize(spectrum, PHI)


def solution(mesh):
    return jax.shard_map(
        on_device,
        mesh=mesh,
        in_specs=(
            P(None, None, None, None, None, ("groups", "leaf", "state", "sub")),
            P(("groups", "leaf", "state", "sub")),
            P(("groups", "leaf", "state", "sub")),
            P(("groups", "leaf", "state", "sub")),
            P(("groups", "leaf", "state", "sub")),
            P(("groups", "leaf", "state", "sub")),
            P(),
            P(),
            P(),
            P(("groups", "leaf"), None, None, None, None),
            P(("groups", "leaf"), None, None, None, ("state", "sub"), None, None),
            P("groups"),
            P(("groups", "leaf"), ("state", "sub"), None, None),
            P("leaf", ("state", "sub"), None),
        ),
        out_specs=P(("groups", "leaf", "state", "sub"), None, None, None, None),
        check_vma=False,
    )
```
